32 devices in a mesh: lat: 8 (over z, y), grp: 4 (over x, core).
Axes of the slice: x: 2, y: 2, z: 4, core: 2. Of those that a mesh axis runs over, the one named last changes fastest.
Arguments:
- fine_source: float32 [8, 24, 4, 4, 512], P('lat', None, None, None, 'grp'), may hold values from -6 to 6
- links: bfloat16 [8, 4, 18, 4, 4, 512], P('lat', None, None, None, None, 'grp'), may hold values from -2.5 to 2.5
- test_vectors: bfloat16 [8, 24, 24, 4, 4, 512], P('lat', None, None, None, None, 'grp'), may hold values from -0.15625 to 0.15625
- aggregate_map: int32 [8, 4, 4, 8, 64], P('lat', None, None, 'grp'), may hold values from 0 to 15, never falling along the last dimension, each value on 1 to 8 neighbouring positions
- colouring: int32 [8, 4, 16], P('lat', 'grp'), may hold values 0 or 1
- coarse_operator: bfloat16 [8, 4, 9, 2, 48, 768], P('lat', 'grp'), may hold values from -1 to 3
- block_inverse: bfloat16 [8, 4, 2, 48, 768], P('lat', 'grp'), may hold values from -1 to 1
Outputs:
- solution: float32 [8, 24, 4, 4, 512], P('lat', None, None, None, 'grp')
- coarse_correction: float32 [8, 4, 2, 48, 16], P('lat', 'grp')
The draws below stay inside these ranges and needn't reach their ends.
Inputs may be any that keep to these rules, and one draw needn't show every extreme that they name: `aggregate_map`: along each line of 64 sites in x the numbers never fall, and each of 0 to 15 covers 1 to 8 consecutive sites.
All inputs are finite; a program needn't handle non-finite values. No bound on the sum of `colouring` on one device may be relied on, other than what follows from the above.
Results may differ from the reference program's by a relative error of at most 0.0029.
Values may be sent and summed in bfloat16 or wider, within the bound.
No kernel may reach another device: no remote copies, remote signals or barrier semaphores. Data moves between devices by JAX's collectives and lax.ppermute only.
A program may use at most 128 MiB of HBM per device.

```python
import math
import jax
import jax.numpy as jnp
import numpy as np
from jax import lax

CT = 4
CZ = 4
CY = 2
CX = 64
PZ = 8
NVEC = 24
AGG = 16
AGG_MOST = 8
MR_STEPS = 2
DOMAINS = 8
GROUPS = 4
NY = 8
SITES = 2048
CDOF = 48


def coarse_draw(key, leading, diagonal, spread):
    full_shape = leading + (2, CDOF, CDOF * AGG)
    noise_part = jax.random.truncated_normal(key, -3.0, 3.0, full_shape, jnp.float32)
    identity = (jnp.arange(CDOF)[:, None] == jnp.arange(CDOF * AGG)[None, :] // AGG).astype(jnp.float32)
    real_only = (jnp.arange(2) == 0).astype(jnp.float32)[:, None, None]
    return (noise_part * (spread / math.sqrt(CDOF)), identity[None] * real_only * diagonal)


def draw_coarse_operator(key, part):
    noise_part, centre = coarse_draw(jax.random.fold_in(key, 11), (DOMAINS, GROUPS, 9), 2.0, 0.35)
    self_term = (jnp.arange(9) == 0).astype(jnp.float32)[:, None, None, None]
    return (noise_part + centre[None] * self_term).astype(jnp.bfloat16)


def draw_block_inverse(key, part):
    noise_part, centre = coarse_draw(jax.random.fold_in(key, 23), (DOMAINS, GROUPS), 0.5, 0.12)
    return (noise_part + centre).astype(jnp.bfloat16)


def with_ends(array, own_key, least, high):
    extent = array.shape
    spot = [jax.random.randint(jax.random.fold_in(own_key, axis), (), 0, extent[axis]) for axis in range(len(extent))]
    array = array.at[tuple(spot)].set(least)
    longest = extent.index(max(extent))
    spot[longest] = (spot[longest] + 1) % extent[longest]
    return array.at[tuple(spot)].set(high)


def steps_of(rng, shape, split, low, high):
    def one(position, shards_of):
        steps = jax.random.uniform(jax.random.fold_in(jax.random.fold_in(rng, 6), position), (shards_of,), jnp.float32, low / len(split), high / len(split))
        return jnp.repeat(jnp.exp(steps), shape[position] // shards_of).reshape((-1,) + (1,) * (len(shape) - position - 1))

    factor_of = one(*split[0])
    for cut in split[1:]:
        factor_of = factor_of * one(*cut)
    return factor_of


def profile(count, total, reach, skew):
    loads = [(1 << 20) // math.isqrt(standing ** skew) + 1 for standing in range(2, count + 1)]
    rest, counts = total - reach - (count - 1), [1] * (count - 1)
    while rest > 0:
        free = [i for i in range(count - 1) if counts[i] < reach]
        pool, budget = sum([loads[i] for i in free]), rest
        for i in free:
            addition = min(reach - counts[i], max(1, budget * loads[i] // pool), rest)
            counts[i] = counts[i] + addition
            rest = rest - addition
    return np.array([reach] + counts)


def ragged_sizes(stream_key, amount, total, bound, lean):
    if amount == 2:
        one = jax.random.randint(stream_key, (), max(1, total - bound), min(bound, total - 1) + 1)
        return jnp.stack([one, total - one])
    sizes = jnp.asarray(profile(amount, total, bound, lean), jnp.int32)
    pairs = (amount - 1) // 2
    giver, receiver = sizes[1:1 + 2 * pairs:2], sizes[2:2 + 2 * pairs:2]
    margin = jnp.minimum(giver - 1, bound - receiver)
    passed = jax.random.randint(jax.random.fold_in(stream_key, 1), (pairs,), 0, 1 << 20) % (margin + 1)
    sizes = sizes.at[1:1 + 2 * pairs:2].set(giver - passed).at[2:2 + 2 * pairs:2].set(receiver + passed)
    return sizes[jax.random.permutation(jax.random.fold_in(stream_key, 2), amount)]


def gaussian(own_key, dims, deviation, reach, split=(), kind=jnp.bfloat16):
    factor_of = steps_of(own_key, dims, split, -0.22, 0.18) if split else 1.0
    result = jax.random.normal(own_key, dims, jnp.float32) * deviation * factor_of
    return jnp.minimum(jnp.maximum(result, -reach), reach).astype(kind)


def setup_inputs(seed: int = 0) -> dict:
    key_of = jax.random.split(jax.random.key(seed), 8)
    return {
        "fine_source": gaussian(key_of[0], (DOMAINS, 24, CT, CZ, NY * CX), 1.0, 6.0, ((0, 8), (4, 4)), jnp.float32),
        "links": gaussian(key_of[1], (DOMAINS, 4, 18, CT, CZ, NY * CX), 0.4, 2.5, ((0, 8), (5, 4))),
        "test_vectors": gaussian(key_of[2], (DOMAINS, NVEC, 24, CT, CZ, NY * CX), (12 * SITES // AGG) ** -0.5, 0.15625, ((0, 8), (5, 4))),
        "aggregate_map": jax.vmap(lambda own: jnp.searchsorted(jnp.cumsum(ragged_sizes(own, AGG, CX, AGG_MOST, 1)), jnp.arange(CX), side="right"))(jax.random.split(key_of[3], DOMAINS * CT * CZ * NY)).reshape((DOMAINS, CT, CZ, NY, CX)).astype(jnp.int32),
        "colouring": with_ends((jax.random.randint(key_of[4], (DOMAINS, GROUPS, AGG), 0, 2) < 1).astype(jnp.int32), jax.random.fold_in(key_of[4], 1), 0, 1),
        "coarse_operator": draw_coarse_operator(jax.random.fold_in(key_of[7], 71), 0),
        "block_inverse": draw_block_inverse(jax.random.fold_in(key_of[7], 71), 0),
    }


def times_minus_i(values):
    return jnp.stack([values[1], -values[0]])


def times_plus_i(values):
    return jnp.stack([-values[1], values[0]])


def spin_factor(direction, spin_pair):
    if direction == 0:
        return jnp.stack([times_minus_i(spin_pair[:, 1]), times_minus_i(spin_pair[:, 0])], axis=1)
    if direction == 1:
        return jnp.stack([-spin_pair[:, 1], spin_pair[:, 0]], axis=1)
    if direction == 2:
        return jnp.stack([times_minus_i(spin_pair[:, 0]), times_plus_i(spin_pair[:, 1])], axis=1)
    return spin_pair


def project_minus(direction, spinor):
    return spinor[:, :2] - spin_factor(direction, spinor[:, 2:])


def project_plus(direction, spinor):
    return spinor[:, :2] + spin_factor(direction, spinor[:, 2:])


def rebuild_minus(direction, half_spinor):
    lower_part = spin_factor(direction, half_spinor) if direction < 3 else -half_spinor
    return jnp.concatenate([half_spinor, lower_part], axis=1)


def rebuild_plus(direction, half_spinor):
    lower_part = -spin_factor(direction, half_spinor) if direction < 3 else half_spinor
    return jnp.concatenate([half_spinor, lower_part], axis=1)


def colour_product(gauge_link, half_spinor, adjoint):
    link_real = gauge_link[0]
    link_imag = gauge_link[1]
    if adjoint:
        link_real = jnp.swapaxes(link_real, 0, 1)
        link_imag = -jnp.swapaxes(link_imag, 0, 1)
    spin_real = half_spinor[0][:, None]
    spin_imag = half_spinor[1][:, None]
    real_part = jnp.sum(link_real[None] * spin_real - link_imag[None] * spin_imag, axis=2)
    imag_part = jnp.sum(link_real[None] * spin_imag + link_imag[None] * spin_real, axis=2)
    return jnp.stack([real_part, imag_part])


def complex_scale(factor_real, factor_imag, lattice):
    return jnp.stack([factor_real * lattice[0] - factor_imag * lattice[1],
                      factor_real * lattice[1] + factor_imag * lattice[0]])


def apply_blocks(blocks, nearby):
    matrices = blocks.reshape(blocks.shape[0], 2, CDOF, CDOF, AGG)
    vector_real = nearby[:, 0][:, None]
    vector_imag = nearby[:, 1][:, None]
    real_part = jnp.sum(matrices[:, 0] * vector_real - matrices[:, 1] * vector_imag, axis=(0, 2))
    imag_part = jnp.sum(matrices[:, 0] * vector_imag + matrices[:, 1] * vector_real, axis=(0, 2))
    return jnp.stack([real_part, imag_part])


def domain_valid():
    index_list = jnp.arange(DOMAINS)
    plane_position = (index_list + 2) % PZ
    return plane_position < PZ - 1, plane_position > 0, index_list < DOMAINS - PZ, index_list >= PZ


def shift_lattice(lattice, direction, forward):
    if direction == 0:
        column_position = jnp.arange(lattice.shape[6]) % CX
        if forward:
            return jnp.where(column_position == CX - 1, jnp.roll(lattice, CX - 1, axis=6), jnp.roll(lattice, -1, axis=6))
        return jnp.where(column_position == 0, jnp.roll(lattice, 1 - CX, axis=6), jnp.roll(lattice, 1, axis=6))
    if direction == 1:
        return jnp.roll(lattice, -CX if forward else CX, axis=6)
    axis_pos = 5 if direction == 2 else 4
    stride = 1 if direction == 2 else PZ
    valid_list = domain_valid()
    length = lattice.shape[axis_pos]
    if forward:
        allowed = valid_list[0] if direction == 2 else valid_list[2]
        ghost_face = jnp.roll(lax.slice_in_dim(lattice, 0, 1, axis=axis_pos), -stride, axis=3)
        ghost_face = jnp.where(allowed.reshape(1, 1, 1, -1, 1, 1, 1), ghost_face, jnp.zeros_like(ghost_face))
        return jnp.concatenate([lax.slice_in_dim(lattice, 1, length, axis=axis_pos), ghost_face], axis=axis_pos)
    allowed = valid_list[1] if direction == 2 else valid_list[3]
    ghost_face = jnp.roll(lax.slice_in_dim(lattice, length - 1, length, axis=axis_pos), stride, axis=3)
    ghost_face = jnp.where(allowed.reshape(1, 1, 1, -1, 1, 1, 1), ghost_face, jnp.zeros_like(ghost_face))
    return jnp.concatenate([ghost_face, lax.slice_in_dim(lattice, 0, length - 1, axis=axis_pos)], axis=axis_pos)


def wilson(spinor, gauge_links, block_masks):
    hop_total = jnp.zeros_like(spinor)
    for direction in range(4):
        gauge_link = gauge_links[direction]
        ahead_part = shift_lattice(project_minus(direction, spinor), direction, True)
        behind_part = shift_lattice(colour_product(gauge_link, project_plus(direction, spinor), True), direction, False)
        if block_masks is not None:
            ahead_part = ahead_part * block_masks[0][direction]
            behind_part = behind_part * block_masks[1][direction]
        hop_total = hop_total + rebuild_minus(direction, colour_product(gauge_link, ahead_part, False))
        hop_total = hop_total + rebuild_plus(direction, behind_part)
    return 4.5 * spinor - 0.5 * hop_total


def reference(fine_source, links, test_vectors, aggregate_map, colouring, coarse_operator, block_inverse):
    line_sites = NY * CX
    source_field = jnp.transpose(fine_source.reshape(DOMAINS, 2, 4, 3, CT, CZ, line_sites), (1, 2, 3, 0, 4, 5, 6))
    gauge_field = jnp.transpose(links.reshape(DOMAINS, 4, 2, 3, 3, CT, CZ, line_sites), (1, 2, 3, 4, 0, 5, 6, 7))
    gauge_links = [gauge_field[direction] for direction in range(4)]
    local_map = aggregate_map.reshape(DOMAINS, CT, CZ, line_sites)
    group_index = (jnp.arange(line_sites) // (CY * CX)).astype(jnp.int32)
    local_block = group_index * AGG + local_map
    block_index = jnp.arange(DOMAINS, dtype=jnp.int32)[:, None, None, None] * (GROUPS * AGG) + local_block
    labels = (block_index + 1).astype(jnp.float32)[None, None, None]
    ahead_masks = [(shift_lattice(labels, direction, True) == labels).astype(jnp.float32) for direction in range(4)]
    behind_masks = [(shift_lattice(labels, direction, False) == labels).astype(jnp.float32) for direction in range(4)]
    site_block = block_index.reshape(-1)
    segment_total = DOMAINS * GROUPS * AGG
    colour_site = colouring.reshape(-1)[site_block].reshape(DOMAINS, CT, CZ, line_sites)
    colour_masks = [(colour_site == colour_pass).astype(jnp.float32) for colour_pass in range(2)]

    def block_solve(residue):
        update = jnp.zeros_like(residue)
        remainder = residue
        for repeat in range(MR_STEPS):
            image_field = wilson(remainder, gauge_links, (ahead_masks, behind_masks))
            image_flat = image_field.reshape(2, 12, -1)
            rest_flat = remainder.reshape(2, 12, -1)
            site_terms = jnp.stack([
                jnp.sum(image_flat[0] * rest_flat[0] + image_flat[1] * rest_flat[1], axis=0),
                jnp.sum(image_flat[0] * rest_flat[1] - image_flat[1] * rest_flat[0], axis=0),
                jnp.sum(image_flat[0] * image_flat[0] + image_flat[1] * image_flat[1], axis=0)], axis=1)
            block_sums = jax.ops.segment_sum(site_terms, site_block, num_segments=segment_total)
            factor_real = (block_sums[:, 0] / (block_sums[:, 2] + 1e-6))[site_block].reshape(DOMAINS, CT, CZ, line_sites)
            factor_imag = (block_sums[:, 1] / (block_sums[:, 2] + 1e-6))[site_block].reshape(DOMAINS, CT, CZ, line_sites)
            update = update + complex_scale(factor_real, factor_imag, remainder)
            remainder = remainder - complex_scale(factor_real, factor_imag, image_field)
        return update

    def sweep(start, from_zero):
        current = start
        for colour_pass in range(2):
            if from_zero and colour_pass == 0:
                residue = source_field
            else:
                residue = source_field - wilson(current, gauge_links, None)
            current = current + colour_masks[colour_pass] * block_solve(residue)
        return current

    smoothed = sweep(jnp.zeros_like(source_field), True)
    residual = (source_field - wilson(smoothed, gauge_links, None)).astype(jnp.bfloat16)
    per_domain = CT * CZ * line_sites
    residual_domains = jnp.moveaxis(residual, 3, 0).reshape(DOMAINS, 2, 2, 6, per_domain)
    vector_domains = test_vectors.reshape(DOMAINS, NVEC, 2, 2, 6, per_domain)
    block_domains = local_block.reshape(DOMAINS, per_domain)

    def restrict_one(domain_items):
        wide_vectors = domain_items[0].astype(jnp.float32)
        wide_residual = domain_items[1].astype(jnp.float32)
        real_part = jnp.sum(wide_vectors[:, 0] * wide_residual[0] + wide_vectors[:, 1] * wide_residual[1], axis=2)
        imag_part = jnp.sum(wide_vectors[:, 0] * wide_residual[1] - wide_vectors[:, 1] * wide_residual[0], axis=2)
        stacked = jnp.stack([real_part, imag_part]).reshape(2 * NVEC * 2, -1).T
        block_sums = jax.ops.segment_sum(stacked, domain_items[2], num_segments=GROUPS * AGG)
        block_sums = block_sums.reshape(GROUPS, AGG, 2, NVEC, 2)
        return jnp.transpose(block_sums, (0, 2, 4, 3, 1)).reshape(GROUPS, 2, CDOF, AGG)

    coarse_source = lax.map(restrict_one, (vector_domains, residual_domains, block_domains))

    def neighbours(vector):
        valid_list = domain_valid()

        def keep_if(allowed, values):
            return jnp.where(allowed.reshape(-1, 1, 1, 1, 1), values, jnp.zeros_like(values))

        return jnp.stack([vector, jnp.roll(vector, -1, axis=4), jnp.roll(vector, 1, axis=4),
                          jnp.roll(vector, -1, axis=1), jnp.roll(vector, 1, axis=1),
                          keep_if(valid_list[0], jnp.roll(vector, -1, axis=0)),
                          keep_if(valid_list[1], jnp.roll(vector, 1, axis=0)),
                          keep_if(valid_list[2], jnp.roll(vector, -PZ, axis=0)),
                          keep_if(valid_list[3], jnp.roll(vector, PZ, axis=0))], axis=2)

    def coarse(vector):
        nearby = neighbours(vector)

        def one_domain(domain_items):
            return jax.vmap(apply_blocks)(domain_items[0].astype(jnp.float32), domain_items[1])

        return lax.map(one_domain, (coarse_operator, nearby))

    def precondition(vector):
        return jax.vmap(jax.vmap(apply_blocks))(block_inverse.astype(jnp.float32)[:, :, None], vector[:, :, None])

    correction = precondition(coarse_source)
    for repeat in range(2):
        correction = correction + precondition(coarse_source - coarse(correction))

    def prolong_one(domain_items):
        coarse_table = jnp.transpose(domain_items[1].reshape(GROUPS, 2, 2, NVEC, AGG), (0, 4, 1, 2, 3))
        coarse_table = coarse_table.reshape(GROUPS * AGG, 2, 2, NVEC)
        at_sites = coarse_table[domain_items[2]]
        spread_real = jnp.transpose(at_sites[:, 0], (2, 1, 0))[:, :, None]
        spread_imag = jnp.transpose(at_sites[:, 1], (2, 1, 0))[:, :, None]
        wide_vectors = domain_items[0].astype(jnp.float32)
        real_part = jnp.sum(wide_vectors[:, 0] * spread_real - wide_vectors[:, 1] * spread_imag, axis=0)
        imag_part = jnp.sum(wide_vectors[:, 0] * spread_imag + wide_vectors[:, 1] * spread_real, axis=0)
        return jnp.stack([real_part, imag_part])

    added = lax.map(prolong_one, (vector_domains, correction, block_domains))
    corrected = smoothed + jnp.moveaxis(added.reshape(DOMAINS, 2, 4, 3, CT, CZ, line_sites), 0, 3)
    solution = sweep(corrected, False)
    solution_out = jnp.transpose(solution, (3, 0, 1, 2, 4, 5, 6)).reshape(DOMAINS, 24, CT, CZ, line_sites)
    return solution_out, correction
```

```python
import functools

import jax
import jax.numpy as jnp
from jax import lax
from jax.experimental import pallas as pl
from jax.experimental.pallas import tpu as pltpu
from jax.sharding import PartitionSpec as P

CX = 64
PZ = 8
NVEC = 24
AGG = 16
MR_STEPS = 2
CDOF = 48


def passed_along(shard, axis, by):
    size = lax.axis_size(axis)
    return lax.ppermute(shard, axis, [(i, (i + by) % size) for i in range(size)])


def padded_2(shard, sides, width):
    for axis, dim in sides:
        size, length = (lax.axis_size(axis), shard.shape[dim])
        up = [(i, (i + 1) % size) for i in range(size)]
        down = [(j, i) for i, j in up]
        last = lax.slice_in_dim(shard, length - width, length, axis=dim)
        first = lax.slice_in_dim(shard, 0, width, axis=dim)
        before = lax.ppermute(last, axis, up)
        after = lax.ppermute(first, axis, down)
        shard = jnp.concatenate([before, shard, after], axis=dim)
    return shard


def times_minus_i(values):
    return jnp.stack([values[1], -values[0]])


def times_plus_i(values):
    return jnp.stack([-values[1], values[0]])


def spin_factor(direction, spin_pair):
    if direction == 0:
        return jnp.stack([times_minus_i(spin_pair[:, 1]), times_minus_i(spin_pair[:, 0])], axis=1)
    if direction == 1:
        return jnp.stack([-spin_pair[:, 1], spin_pair[:, 0]], axis=1)
    if direction == 2:
        return jnp.stack([times_minus_i(spin_pair[:, 0]), times_plus_i(spin_pair[:, 1])], axis=1)
    return spin_pair


def project_minus(direction, spinor):
    return spinor[:, :2] - spin_factor(direction, spinor[:, 2:])


def project_plus(direction, spinor):
    return spinor[:, :2] + spin_factor(direction, spinor[:, 2:])


def rebuild_minus(direction, half_spinor):
    lower_part = spin_factor(direction, half_spinor) if direction < 3 else -half_spinor
    return jnp.concatenate([half_spinor, lower_part], axis=1)


def rebuild_plus(direction, half_spinor):
    lower_part = -spin_factor(direction, half_spinor) if direction < 3 else half_spinor
    return jnp.concatenate([half_spinor, lower_part], axis=1)


def colour_product(gauge_link, half_spinor, adjoint):
    link_real = gauge_link[0]
    link_imag = gauge_link[1]
    if adjoint:
        link_real = jnp.swapaxes(link_real, 0, 1)
        link_imag = -jnp.swapaxes(link_imag, 0, 1)
    spin_real = half_spinor[0][:, None]
    spin_imag = half_spinor[1][:, None]
    real_part = jnp.sum(link_real[None] * spin_real - link_imag[None] * spin_imag, axis=2)
    imag_part = jnp.sum(link_real[None] * spin_imag + link_imag[None] * spin_real, axis=2)
    return jnp.stack([real_part, imag_part])


def complex_scale(factor_real, factor_imag, lattice):
    return jnp.stack(
        [
            factor_real * lattice[0] - factor_imag * lattice[1],
            factor_real * lattice[1] + factor_imag * lattice[0],
        ]
    )


def apply_blocks(blocks, nearby):
    matrices = blocks.reshape(blocks.shape[0], 2, CDOF, CDOF, AGG)
    vector_real = nearby[:, 0][:, None]
    vector_imag = nearby[:, 1][:, None]
    real_part = jnp.sum(matrices[:, 0] * vector_real - matrices[:, 1] * vector_imag, axis=(0, 2))
    imag_part = jnp.sum(matrices[:, 0] * vector_imag + matrices[:, 1] * vector_real, axis=(0, 2))
    return jnp.stack([real_part, imag_part])


def keep_if(allowed, values):
    return jnp.where(allowed, values, jnp.zeros_like(values))


def permute_from(value, axis, offset, allowed):
    size = lax.axis_size(axis)
    pairs = [((i + offset) % size, i) for i in range(size) if allowed(i)]
    if not pairs:
        return None
    return lax.ppermute(value, axis, pairs)


class Shifts:
    def __init__(self, rows, lanes):
        self.rows = rows
        self.lanes = lanes
        self.lane = lax.broadcasted_iota(jnp.int32, (rows, lanes), 1)
        self.row = lax.broadcasted_iota(jnp.int32, (rows, lanes), 0)
        self.xpos = self.lane % CX
        self.zpos = self.row % 4

    def roll(self, a, shift, axis):
        n = a.shape[axis]
        return pltpu.roll(a, shift % n, a.ndim + axis)

    def ahead(self, direction, a, nbr):
        if direction == 0:
            return jnp.where(self.xpos == CX - 1, self.roll(a, CX - 1, -1), self.roll(a, -1, -1))
        if direction == 1:
            half = self.lanes // 2
            filled = jnp.where(self.lane < half, 0.0 if nbr is None else nbr, a)
            return self.roll(filled, half, -1)
        if direction == 2:
            inner = self.roll(a, -1, -2)
            outer = 0.0 if nbr is None else self.roll(nbr, 3, -2)
            return jnp.where(self.zpos == 3, outer, inner)
        filled = jnp.where(self.row < 4, 0.0 if nbr is None else nbr, a)
        return self.roll(filled, -4, -2)

    def behind(self, direction, a, nbr):
        if direction == 0:
            return jnp.where(self.xpos == 0, self.roll(a, 1 - CX, -1), self.roll(a, 1, -1))
        if direction == 1:
            half = self.lanes // 2
            filled = jnp.where(self.lane >= half, 0.0 if nbr is None else nbr, a)
            return self.roll(filled, half, -1)
        if direction == 2:
            inner = self.roll(a, 1, -2)
            outer = 0.0 if nbr is None else self.roll(nbr, -3, -2)
            return jnp.where(self.zpos == 0, outer, inner)
        filled = jnp.where(self.row >= self.rows - 4, 0.0 if nbr is None else nbr, a)
        return self.roll(filled, 4, -2)


def hopping(spinor, links, back_links, ahead_list, behind_list):
    hop_total = None
    for direction in range(4):
        ahead_half = colour_product(links[direction], project_minus(direction, ahead_list[direction]), False)
        behind_half = colour_product(back_links[direction], project_plus(direction, behind_list[direction]), True)
        term = rebuild_minus(direction, ahead_half) + rebuild_plus(direction, behind_half)
        hop_total = term if hop_total is None else hop_total + term
    return 4.5 * spinor - 0.5 * hop_total


def pass_kernel(*refs, first, residual_only, present):
    refs = list(refs)
    out_ref = refs.pop()

    def take():
        return refs.pop(0)

    src_ref = take()
    links_ref = take()
    ghost_refs = [None, None, None, None]
    for direction in (1, 2, 3):
        if present["ghost"][direction]:
            ghost_refs[direction] = take()
    labels_ref = take()
    member_ref = take()
    cmask_ref = None if residual_only else take()
    spinor_ref = None
    halo_refs = {}
    if not first:
        spinor_ref = take()
        for direction in (1, 2, 3):
            for side in ("ahead", "behind"):
                if present[side][direction]:
                    halo_refs[(side, direction)] = take()

    rows, lanes = src_ref.shape[-2], src_ref.shape[-1]
    sh = Shifts(rows, lanes)
    shape = (2, 4, 3, rows, lanes)
    source = src_ref[...].reshape(shape)
    link_all = links_ref[...].astype(jnp.float32)
    links = [link_all[d].reshape(2, 3, 3, rows, lanes) for d in range(4)]
    back_links = []
    for direction in range(4):
        ghost = None
        if ghost_refs[direction] is not None:
            ghost = ghost_refs[direction][...].astype(jnp.float32).reshape(2, 3, 3, rows, lanes)
        back_links.append(sh.behind(direction, links[direction], ghost))

    def load_halo(side, direction):
        ref = halo_refs.get((side, direction))
        return None if ref is None else ref[...].reshape(shape)

    def wilson_global(spinor):
        ahead_list = [sh.ahead(d, spinor, load_halo("ahead", d)) for d in range(4)]
        behind_list = [sh.behind(d, spinor, load_halo("behind", d)) for d in range(4)]
        return hopping(spinor, links, back_links, ahead_list, behind_list)

    if first:
        residue = source
        current = None
    else:
        current = spinor_ref[...].reshape(shape)
        residue = source - wilson_global(current)
    if residual_only:
        out_ref[...] = residue.reshape(out_ref.shape)
        return

    labels = labels_ref[...]
    ahead_masks = [(sh.ahead(d, labels, None) == labels).astype(jnp.float32) for d in range(4)]
    behind_masks = [(sh.behind(d, labels, None) == labels).astype(jnp.float32) for d in range(4)]
    member = member_ref[...]

    def wilson_block(spinor):
        ahead_list = [sh.ahead(d, spinor, None) * ahead_masks[d] for d in range(4)]
        behind_list = [sh.behind(d, spinor, None) * behind_masks[d] for d in range(4)]
        return hopping(spinor, links, back_links, ahead_list, behind_list)

    def block_total(values):
        return jnp.sum(jnp.sum(member * values[None], axis=2, keepdims=True), axis=1, keepdims=True)

    update = None
    remainder = residue
    for repeat in range(MR_STEPS):
        image = wilson_block(remainder)
        image_flat = image.reshape(2, 12, rows, lanes)
        rest_flat = remainder.reshape(2, 12, rows, lanes)
        dot_real = jnp.sum(image_flat[0] * rest_flat[0] + image_flat[1] * rest_flat[1], axis=0)
        dot_imag = jnp.sum(image_flat[0] * rest_flat[1] - image_flat[1] * rest_flat[0], axis=0)
        norm = jnp.sum(image_flat[0] * image_flat[0] + image_flat[1] * image_flat[1], axis=0)
        denominator = block_total(norm) + 1e-06
        factor_real = jnp.sum(member * (block_total(dot_real) / denominator), axis=0)
        factor_imag = jnp.sum(member * (block_total(dot_imag) / denominator), axis=0)
        step = complex_scale(factor_real, factor_imag, remainder)
        update = step if update is None else update + step
        remainder = remainder - complex_scale(factor_real, factor_imag, image)
    update = update * cmask_ref[...]
    result = update if current is None else current + update
    out_ref[...] = result.reshape(out_ref.shape)


def run_pass(source, links, ghosts, labels, member, cmask, spinor, halos, residual_only=False):
    first = spinor is None
    present = {
        "ghost": [g is not None for g in ghosts],
        "ahead": [h is not None for h in halos["ahead"]] if not first else [False] * 4,
        "behind": [h is not None for h in halos["behind"]] if not first else [False] * 4,
    }
    operands = [source, links] + [g for g in ghosts[1:] if g is not None] + [labels, member]
    if not residual_only:
        operands.append(cmask)
    if not first:
        operands.append(spinor)
        for direction in (1, 2, 3):
            for side in ("ahead", "behind"):
                if present[side][direction]:
                    operands.append(halos[side][direction])
    kernel = functools.partial(pass_kernel, first=first, residual_only=residual_only, present=present)
    return pl.pallas_call(kernel, out_shape=jax.ShapeDtypeStruct(source.shape, jnp.float32))(*operands)


def body(
    fine_source, links, test_vectors, aggregate_map, colouring, coarse_operator, block_inverse
):
    time_extent = fine_source.shape[2]
    plane_extent = fine_source.shape[3]
    line_extent = fine_source.shape[4]
    rows = time_extent * plane_extent
    site_count = rows * line_extent
    domain_index = lax.axis_index("lat")
    domain_count = lax.axis_size("lat")
    plane_position = (domain_index + 2) % PZ
    upper_valid = plane_position < PZ - 1
    lower_valid = plane_position > 0
    later_valid = domain_index < domain_count - PZ
    earlier_valid = domain_index >= PZ

    source = fine_source.reshape(24, rows, line_extent)
    link_rows = links.reshape(4, 18, rows, line_extent)
    label_rows = aggregate_map.reshape(rows, line_extent)
    member = (label_rows[None] == jnp.arange(AGG, dtype=jnp.int32)[:, None, None]).astype(jnp.float32)
    colour_list = colouring.reshape(AGG)
    colour_masks = [
        jnp.sum(member * (colour_list == k).astype(jnp.float32)[:, None, None], axis=0) for k in range(2)
    ]
    labels = (label_rows + 1).astype(jnp.float32)

    def z_up_ok(i):
        return (i + 2) % PZ != PZ - 1

    def z_down_ok(i):
        return (i + 2) % PZ != 0

    def t_up_ok(i):
        return i + PZ < domain_count

    def t_down_ok(i):
        return i - PZ >= 0

    ghosts = [
        None,
        permute_from(link_rows[1], "grp", -1, lambda i: True),
        permute_from(link_rows[2], "lat", -1, z_down_ok),
        permute_from(link_rows[3], "lat", -PZ, t_down_ok),
    ]

    def halos_of(spinor):
        return {
            "ahead": [
                None,
                permute_from(spinor, "grp", 1, lambda i: True),
                permute_from(spinor, "lat", 1, z_up_ok),
                permute_from(spinor, "lat", PZ, t_up_ok),
            ],
            "behind": [
                None,
                permute_from(spinor, "grp", -1, lambda i: True),
                permute_from(spinor, "lat", -1, z_down_ok),
                permute_from(spinor, "lat", -PZ, t_down_ok),
            ],
        }

    def smoother_pass(spinor, colour_pass):
        halos = None if spinor is None else halos_of(spinor)
        return run_pass(source, link_rows, ghosts, labels, member, colour_masks[colour_pass], spinor, halos)

    def sweep(start):
        current = smoother_pass(start, 0)
        return smoother_pass(current, 1)

    smoothed = sweep(None)
    residue = run_pass(
        source, link_rows, ghosts, labels, member, None, smoothed, halos_of(smoothed), residual_only=True
    )
    residual = residue.astype(jnp.bfloat16)
    membership = member.reshape(AGG, site_count).T
    member_weights = membership.astype(jnp.bfloat16)
    weighted = residual.reshape(2, 2, 6, site_count)[..., None] * member_weights
    vectors = test_vectors.reshape(NVEC, 2, 2, 6, site_count)

    def contract(left, right):
        return jnp.einsum("kxqn,xqnj->xkj", left, right, preferred_element_type=jnp.float32)

    real_part = contract(vectors[:, 0], weighted[0]) + contract(vectors[:, 1], weighted[1])
    imag_part = contract(vectors[:, 0], weighted[1]) - contract(vectors[:, 1], weighted[0])
    coarse_source = jnp.stack([real_part, imag_part]).reshape(2, CDOF, AGG)
    operator_blocks = coarse_operator.reshape(9, 2, CDOF, CDOF * AGG)
    inverse_blocks = block_inverse.reshape(1, 2, CDOF, CDOF * AGG)

    def precondition(vector):
        return apply_blocks(inverse_blocks, vector[None])

    correction = precondition(coarse_source)
    for repeat in range(2):
        loop_values = padded_2(correction[None], (("grp", 0),), 1)
        nearby_arrived = []
        for nearby_offset in (-1, 1, -PZ, PZ):
            nearby_arrived.append(passed_along(correction, "lat", nearby_offset))
        correction = correction + precondition(
            coarse_source
            - apply_blocks(
                operator_blocks,
                jnp.stack(
                    [
                        correction,
                        jnp.roll(correction, -1, axis=2),
                        jnp.roll(correction, 1, axis=2),
                        loop_values[2],
                        loop_values[0],
                        keep_if(upper_valid, nearby_arrived[0]),
                        keep_if(lower_valid, nearby_arrived[1]),
                        keep_if(later_valid, nearby_arrived[2]),
                        keep_if(earlier_valid, nearby_arrived[3]),
                    ]
                ),
            )
        )
    expanded = jnp.dot(
        correction.reshape(2 * CDOF, AGG), membership.T, precision=lax.Precision.HIGHEST
    ).reshape(2, 2, NVEC, site_count)
    spread_real = jnp.swapaxes(expanded[0], 0, 1)[:, :, None]
    spread_imag = jnp.swapaxes(expanded[1], 0, 1)[:, :, None]
    real_part = jnp.sum(vectors[:, 0] * spread_real - vectors[:, 1] * spread_imag, axis=0)
    imag_part = jnp.sum(vectors[:, 0] * spread_imag + vectors[:, 1] * spread_real, axis=0)
    corrected = smoothed + jnp.stack([real_part, imag_part]).reshape(24, rows, line_extent)
    solution = sweep(corrected)
    return (
        solution.reshape(1, 24, time_extent, plane_extent, line_extent),
        correction.reshape(1, 1, 2, CDOF, AGG),
    )


def solution(mesh):
    return jax.shard_map(
        body,
        mesh=mesh,
        in_specs=(
            P("lat", None, None, None, "grp"),
            P("lat", None, None, None, None, "grp"),
            P("lat", None, None, None, None, "grp"),
            P("lat", None, None, "grp", None),
            P("lat", "grp", None),
            P("lat", "grp", None, None, None, None),
            P("lat", "grp", None, None, None),
        ),
        out_specs=(P("lat", None, None, None, "grp"), P("lat", "grp", None, None, None)),
        check_vma=False,
    )
```

```python
import functools

import jax
import jax.numpy as jnp
from jax import lax
from jax.experimental import pallas as pl
from jax.experimental.pallas import tpu as pltpu
from jax.sharding import PartitionSpec as P

CX = 64
PZ = 8
NVEC = 24
AGG = 16
MR_STEPS = 2
CDOF = 48


def passed_along(shard, axis, by):
    size = lax.axis_size(axis)
    return lax.ppermute(shard, axis, [(i, (i + by) % size) for i in range(size)])


def padded_2(shard, sides, width):
    for axis, dim in sides:
        size, length = (lax.axis_size(axis), shard.shape[dim])
        up = [(i, (i + 1) % size) for i in range(size)]
        down = [(j, i) for i, j in up]
        last = lax.slice_in_dim(shard, length - width, length, axis=dim)
        first = lax.slice_in_dim(shard, 0, width, axis=dim)
        before = lax.ppermute(last, axis, up)
        after = lax.ppermute(first, axis, down)
        shard = jnp.concatenate([before, shard, after], axis=dim)
    return shard


def times_minus_i(values):
    return jnp.stack([values[1], -values[0]])


def times_plus_i(values):
    return jnp.stack([-values[1], values[0]])


def spin_factor(direction, spin_pair):
    if direction == 0:
        return jnp.stack([times_minus_i(spin_pair[:, 1]), times_minus_i(spin_pair[:, 0])], axis=1)
    if direction == 1:
        return jnp.stack([-spin_pair[:, 1], spin_pair[:, 0]], axis=1)
    if direction == 2:
        return jnp.stack([times_minus_i(spin_pair[:, 0]), times_plus_i(spin_pair[:, 1])], axis=1)
    return spin_pair


def project_minus(direction, spinor):
    return spinor[:, :2] - spin_factor(direction, spinor[:, 2:])


def project_plus(direction, spinor):
    return spinor[:, :2] + spin_factor(direction, spinor[:, 2:])


def rebuild_minus(direction, half_spinor):
    lower_part = spin_factor(direction, half_spinor) if direction < 3 else -half_spinor
    return jnp.concatenate([half_spinor, lower_part], axis=1)


def rebuild_plus(direction, half_spinor):
    lower_part = -spin_factor(direction, half_spinor) if direction < 3 else half_spinor
    return jnp.concatenate([half_spinor, lower_part], axis=1)


def colour_product(gauge_link, half_spinor, adjoint):
    link_real = gauge_link[0]
    link_imag = gauge_link[1]
    if adjoint:
        link_real = jnp.swapaxes(link_real, 0, 1)
        link_imag = -jnp.swapaxes(link_imag, 0, 1)
    spin_real = half_spinor[0][:, None]
    spin_imag = half_spinor[1][:, None]
    real_part = jnp.sum(link_real[None] * spin_real - link_imag[None] * spin_imag, axis=2)
    imag_part = jnp.sum(link_real[None] * spin_imag + link_imag[None] * spin_real, axis=2)
    return jnp.stack([real_part, imag_part])


def complex_scale(factor_real, factor_imag, lattice):
    return jnp.stack(
        [
            factor_real * lattice[0] - factor_imag * lattice[1],
            factor_real * lattice[1] + factor_imag * lattice[0],
        ]
    )


def apply_blocks(blocks, nearby):
    matrices = blocks.reshape(blocks.shape[0], 2, CDOF, CDOF, AGG)
    vector_real = nearby[:, 0][:, None]
    vector_imag = nearby[:, 1][:, None]
    real_part = jnp.sum(matrices[:, 0] * vector_real - matrices[:, 1] * vector_imag, axis=(0, 2))
    imag_part = jnp.sum(matrices[:, 0] * vector_imag + matrices[:, 1] * vector_real, axis=(0, 2))
    return jnp.stack([real_part, imag_part])


def keep_if(allowed, values):
    return jnp.where(allowed, values, jnp.zeros_like(values))


def permute_from(value, axis, offset, allowed):
    size = lax.axis_size(axis)
    pairs = [((i + offset) % size, i) for i in range(size) if allowed(i)]
    if not pairs:
        return None
    return lax.ppermute(value, axis, pairs)


class Shifts:
    def __init__(self, rows, lanes):
        self.rows = rows
        self.lanes = lanes
        self.lane = lax.broadcasted_iota(jnp.int32, (rows, lanes), 1)
        self.row = lax.broadcasted_iota(jnp.int32, (rows, lanes), 0)
        self.xpos = self.lane % CX
        self.zpos = self.row % 4

    def roll(self, a, shift, axis):
        n = a.shape[axis]
        return pltpu.roll(a, shift % n, a.ndim + axis)

    def ahead(self, direction, a, nbr):
        if direction == 0:
            return jnp.where(self.xpos == CX - 1, self.roll(a, CX - 1, -1), self.roll(a, -1, -1))
        if direction == 1:
            half = self.lanes // 2
            filled = jnp.where(self.lane < half, 0.0 if nbr is None else nbr, a)
            return self.roll(filled, half, -1)
        if direction == 2:
            inner = self.roll(a, -1, -2)
            outer = 0.0 if nbr is None else self.roll(nbr, 3, -2)
            return jnp.where(self.zpos == 3, outer, inner)
        filled = jnp.where(self.row < 4, 0.0 if nbr is None else nbr, a)
        return self.roll(filled, -4, -2)

    def behind(self, direction, a, nbr):
        if direction == 0:
            return jnp.where(self.xpos == 0, self.roll(a, 1 - CX, -1), self.roll(a, 1, -1))
        if direction == 1:
            half = self.lanes // 2
            filled = jnp.where(self.lane >= half, 0.0 if nbr is None else nbr, a)
            return self.roll(filled, half, -1)
        if direction == 2:
            inner = self.roll(a, 1, -2)
            outer = 0.0 if nbr is None else self.roll(nbr, -3, -2)
            return jnp.where(self.zpos == 0, outer, inner)
        filled = jnp.where(self.row >= self.rows - 4, 0.0 if nbr is None else nbr, a)
        return self.roll(filled, 4, -2)


def hopping(spinor, links, back_links, ahead_list, behind_list):
    hop_total = None
    for direction in range(4):
        ahead_half = colour_product(links[direction], project_minus(direction, ahead_list[direction]), False)
        behind_half = colour_product(back_links[direction], project_plus(direction, behind_list[direction]), True)
        term = rebuild_minus(direction, ahead_half) + rebuild_plus(direction, behind_half)
        hop_total = term if hop_total is None else hop_total + term
    return 4.5 * spinor - 0.5 * hop_total


def pass_kernel(*refs, first, residual_only, present):
    refs = list(refs)
    out_ref = refs.pop()

    def take():
        return refs.pop(0)

    src_ref = take()
    links_ref = take()
    ghost_refs = [None, None, None, None]
    for direction in (1, 2, 3):
        if present["ghost"][direction]:
            ghost_refs[direction] = take()
    labels_ref = take()
    member_ref = take()
    cmask_ref = None if residual_only else take()
    spinor_ref = None
    halo_refs = {}
    if not first:
        spinor_ref = take()
        for direction in (1, 2, 3):
            for side in ("ahead", "behind"):
                if present[side][direction]:
                    halo_refs[(side, direction)] = take()

    rows, lanes = src_ref.shape[-2], src_ref.shape[-1]
    sh = Shifts(rows, lanes)
    shape = (2, 4, 3, rows, lanes)
    source = src_ref[...].reshape(shape)
    link_all = links_ref[...].astype(jnp.float32)
    links = [link_all[d].reshape(2, 3, 3, rows, lanes) for d in range(4)]
    back_links = []
    for direction in range(4):
        ghost = None
        if ghost_refs[direction] is not None:
            ghost = ghost_refs[direction][...].astype(jnp.float32).reshape(2, 3, 3, rows, lanes)
        back_links.append(sh.behind(direction, links[direction], ghost))

    def load_halo(side, direction):
        ref = halo_refs.get((side, direction))
        return None if ref is None else ref[...].reshape(shape)

    def wilson_global(spinor):
        ahead_list = [sh.ahead(d, spinor, load_halo("ahead", d)) for d in range(4)]
        behind_list = [sh.behind(d, spinor, load_halo("behind", d)) for d in range(4)]
        return hopping(spinor, links, back_links, ahead_list, behind_list)

    if first:
        residue = source
        current = None
    else:
        current = spinor_ref[...].reshape(shape)
        residue = source - wilson_global(current)
    if residual_only:
        out_ref[...] = residue.reshape(out_ref.shape)
        return

    labels = labels_ref[...]
    ahead_masks = [(sh.ahead(d, labels, None) == labels).astype(jnp.float32) for d in range(4)]
    behind_masks = [(sh.behind(d, labels, None) == labels).astype(jnp.float32) for d in range(4)]
    member = member_ref[...]

    def wilson_block(spinor):
        ahead_list = [sh.ahead(d, spinor, None) * ahead_masks[d] for d in range(4)]
        behind_list = [sh.behind(d, spinor, None) * behind_masks[d] for d in range(4)]
        return hopping(spinor, links, back_links, ahead_list, behind_list)

    def block_total(values):
        return jnp.sum(jnp.sum(member * values[None], axis=2, keepdims=True), axis=1, keepdims=True)

    update = None
    remainder = residue
    for repeat in range(MR_STEPS):
        image = wilson_block(remainder)
        image_flat = image.reshape(2, 12, rows, lanes)
        rest_flat = remainder.reshape(2, 12, rows, lanes)
        dot_real = jnp.sum(image_flat[0] * rest_flat[0] + image_flat[1] * rest_flat[1], axis=0)
        dot_imag = jnp.sum(image_flat[0] * rest_flat[1] - image_flat[1] * rest_flat[0], axis=0)
        norm = jnp.sum(image_flat[0] * image_flat[0] + image_flat[1] * image_flat[1], axis=0)
        denominator = block_total(norm) + 1e-06
        factor_real = jnp.sum(member * (block_total(dot_real) / denominator), axis=0)
        factor_imag = jnp.sum(member * (block_total(dot_imag) / denominator), axis=0)
        step = complex_scale(factor_real, factor_imag, remainder)
        update = step if update is None else update + step
        remainder = remainder - complex_scale(factor_real, factor_imag, image)
    update = update * cmask_ref[...]
    result = update if current is None else current + update
    out_ref[...] = result.reshape(out_ref.shape)


def run_pass(source, links, ghosts, labels, member, cmask, spinor, halos, residual_only=False):
    first = spinor is None
    present = {
        "ghost": [g is not None for g in ghosts],
        "ahead": [h is not None for h in halos["ahead"]] if not first else [False] * 4,
        "behind": [h is not None for h in halos["behind"]] if not first else [False] * 4,
    }
    operands = [source, links] + [g for g in ghosts[1:] if g is not None] + [labels, member]
    if not residual_only:
        operands.append(cmask)
    if not first:
        operands.append(spinor)
        for direction in (1, 2, 3):
            for side in ("ahead", "behind"):
                if present[side][direction]:
                    operands.append(halos[side][direction])
    kernel = functools.partial(pass_kernel, first=first, residual_only=residual_only, present=present)
    return pl.pallas_call(kernel, out_shape=jax.ShapeDtypeStruct(source.shape, jnp.float32))(*operands)


def body(
    fine_source, links, test_vectors, aggregate_map, colouring, coarse_operator, block_inverse
):
    time_extent = fine_source.shape[2]
    plane_extent = fine_source.shape[3]
    line_extent = fine_source.shape[4]
    rows = time_extent * plane_extent
    site_count = rows * line_extent
    domain_index = lax.axis_index("lat")
    domain_count = lax.axis_size("lat")
    plane_position = (domain_index + 2) % PZ
    upper_valid = plane_position < PZ - 1
    lower_valid = plane_position > 0
    later_valid = domain_index < domain_count - PZ
    earlier_valid = domain_index >= PZ

    source = fine_source.reshape(24, rows, line_extent)
    link_rows = links.reshape(4, 18, rows, line_extent)
    label_rows = aggregate_map.reshape(rows, line_extent)
    member = (label_rows[None] == jnp.arange(AGG, dtype=jnp.int32)[:, None, None]).astype(jnp.float32)
    colour_list = colouring.reshape(AGG)
    colour_masks = [
        jnp.sum(member * (colour_list == k).astype(jnp.float32)[:, None, None], axis=0) for k in range(2)
    ]
    labels = (label_rows + 1).astype(jnp.float32)

    def z_up_ok(i):
        return (i + 2) % PZ != PZ - 1

    def z_down_ok(i):
        return (i + 2) % PZ != 0

    def t_up_ok(i):
        return i + PZ < domain_count

    def t_down_ok(i):
        return i - PZ >= 0

    ghosts = [
        None,
        permute_from(link_rows[1], "grp", -1, lambda i: True),
        permute_from(link_rows[2], "lat", -1, z_down_ok),
        permute_from(link_rows[3], "lat", -PZ, t_down_ok),
    ]

    def halos_of(spinor):
        return {
            "ahead": [
                None,
                permute_from(spinor, "grp", 1, lambda i: True),
                permute_from(spinor, "lat", 1, z_up_ok),
                permute_from(spinor, "lat", PZ, t_up_ok),
            ],
            "behind": [
                None,
                permute_from(spinor, "grp", -1, lambda i: True),
                permute_from(spinor, "lat", -1, z_down_ok),
                permute_from(spinor, "lat", -PZ, t_down_ok),
            ],
        }

    def smoother_pass(spinor, colour_pass):
        halos = None if spinor is None else halos_of(spinor)
        return run_pass(source, link_rows, ghosts, labels, member, colour_masks[colour_pass], spinor, halos)

    def sweep(start):
        current = smoother_pass(start, 0)
        return smoother_pass(current, 1)

    smoothed = sweep(None)
    residue = run_pass(
        source, link_rows, ghosts, labels, member, None, smoothed, halos_of(smoothed), residual_only=True
    )
    residual = residue.astype(jnp.bfloat16)
    membership = member.reshape(AGG, site_count).T
    member_weights = membership.astype(jnp.bfloat16)
    weighted = residual.reshape(2, 2, 6, site_count)[..., None] * member_weights
    vectors = test_vectors.reshape(NVEC, 2, 2, 6, site_count)

    def contract(left, right):
        return jnp.einsum("kxqn,xqnj->xkj", left, right, preferred_element_type=jnp.float32)

    real_part = contract(vectors[:, 0], weighted[0]) + contract(vectors[:, 1], weighted[1])
    imag_part = contract(vectors[:, 0], weighted[1]) - contract(vectors[:, 1], weighted[0])
    coarse_source = jnp.stack([real_part, imag_part]).reshape(2, CDOF, AGG)
    operator_blocks = coarse_operator.reshape(9, 2 * CDOF, CDOF * AGG)
    inverse_blocks = block_inverse.reshape(2 * CDOF, CDOF * AGG)
    eye = jnp.eye(AGG, dtype=jnp.float32)

    def block_product(blocks, vector):
        expanded_vector = jnp.transpose(vector, (1, 2, 0))[:, :, :, None] * eye[None, :, None, :]
        product = jnp.dot(
            blocks,
            expanded_vector.reshape(CDOF * AGG, 2 * AGG),
            precision=lax.Precision.HIGHEST,
            preferred_element_type=jnp.float32,
        )
        return product.reshape(2, CDOF, 2, AGG)

    def combine(product):
        return jnp.stack(
            [product[0, :, 0] - product[1, :, 1], product[0, :, 1] + product[1, :, 0]]
        )

    def precondition(vector):
        return combine(block_product(inverse_blocks, vector))

    correction = precondition(coarse_source)
    for repeat in range(2):
        nearby = [
            correction,
            jnp.roll(correction, -1, axis=2),
            jnp.roll(correction, 1, axis=2),
            permute_from(correction, "grp", 1, lambda i: True),
            permute_from(correction, "grp", -1, lambda i: True),
            permute_from(correction, "lat", 1, z_up_ok),
            permute_from(correction, "lat", -1, z_down_ok),
            permute_from(correction, "lat", PZ, t_up_ok),
            permute_from(correction, "lat", -PZ, t_down_ok),
        ]
        total = None
        for direction, vector in enumerate(nearby):
            if vector is None:
                continue
            product = block_product(operator_blocks[direction], vector)
            total = product if total is None else total + product
        correction = correction + precondition(coarse_source - combine(total))
    expanded = jnp.dot(
        correction.reshape(2 * CDOF, AGG), membership.T, precision=lax.Precision.HIGHEST
    ).reshape(2, 2, NVEC, site_count)
    spread_real = jnp.swapaxes(expanded[0], 0, 1)[:, :, None]
    spread_imag = jnp.swapaxes(expanded[1], 0, 1)[:, :, None]
    real_part = jnp.sum(vectors[:, 0] * spread_real - vectors[:, 1] * spread_imag, axis=0)
    imag_part = jnp.sum(vectors[:, 0] * spread_imag + vectors[:, 1] * spread_real, axis=0)
    corrected = smoothed + jnp.stack([real_part, imag_part]).reshape(24, rows, line_extent)
    solution = sweep(corrected)
    return (
        solution.reshape(1, 24, time_extent, plane_extent, line_extent),
        correction.reshape(1, 1, 2, CDOF, AGG),
    )


def solution(mesh):
    return jax.shard_map(
        body,
        mesh=mesh,
        in_specs=(
            P("lat", None, None, None, "grp"),
            P("lat", None, None, None, None, "grp"),
            P("lat", None, None, None, None, "grp"),
            P("lat", None, None, "grp", None),
            P("lat", "grp", None),
            P("lat", "grp", None, None, None, None),
            P("lat", "grp", None, None, None),
        ),
        out_specs=(P("lat", None, None, None, "grp"), P("lat", "grp", None, None, None)),
        check_vma=False,
    )
```

```python
import functools

import jax
import jax.numpy as jnp
from jax import lax
from jax.experimental import pallas as pl
from jax.experimental.pallas import tpu as pltpu
from jax.sharding import PartitionSpec as P

CX = 64
PZ = 8
NVEC = 24
AGG = 16
MR_STEPS = 2
CDOF = 48


def passed_along(shard, axis, by):
    size = lax.axis_size(axis)
    return lax.ppermute(shard, axis, [(i, (i + by) % size) for i in range(size)])


def padded_2(shard, sides, width):
    for axis, dim in sides:
        size, length = (lax.axis_size(axis), shard.shape[dim])
        up = [(i, (i + 1) % size) for i in range(size)]
        down = [(j, i) for i, j in up]
        last = lax.slice_in_dim(shard, length - width, length, axis=dim)
        first = lax.slice_in_dim(shard, 0, width, axis=dim)
        before = lax.ppermute(last, axis, up)
        after = lax.ppermute(first, axis, down)
        shard = jnp.concatenate([before, shard, after], axis=dim)
    return shard


def times_minus_i(values):
    return jnp.stack([values[1], -values[0]])


def times_plus_i(values):
    return jnp.stack([-values[1], values[0]])


def spin_factor(direction, spin_pair):
    if direction == 0:
        return jnp.stack([times_minus_i(spin_pair[:, 1]), times_minus_i(spin_pair[:, 0])], axis=1)
    if direction == 1:
        return jnp.stack([-spin_pair[:, 1], spin_pair[:, 0]], axis=1)
    if direction == 2:
        return jnp.stack([times_minus_i(spin_pair[:, 0]), times_plus_i(spin_pair[:, 1])], axis=1)
    return spin_pair


def project_minus(direction, spinor):
    return spinor[:, :2] - spin_factor(direction, spinor[:, 2:])


def project_plus(direction, spinor):
    return spinor[:, :2] + spin_factor(direction, spinor[:, 2:])


def rebuild_minus(direction, half_spinor):
    lower_part = spin_factor(direction, half_spinor) if direction < 3 else -half_spinor
    return jnp.concatenate([half_spinor, lower_part], axis=1)


def rebuild_plus(direction, half_spinor):
    lower_part = -spin_factor(direction, half_spinor) if direction < 3 else half_spinor
    return jnp.concatenate([half_spinor, lower_part], axis=1)


def colour_product(gauge_link, half_spinor, adjoint):
    link_real = gauge_link[0]
    link_imag = gauge_link[1]
    if adjoint:
        link_real = jnp.swapaxes(link_real, 0, 1)
        link_imag = -jnp.swapaxes(link_imag, 0, 1)
    spin_real = half_spinor[0][:, None]
    spin_imag = half_spinor[1][:, None]
    real_part = jnp.sum(link_real[None] * spin_real - link_imag[None] * spin_imag, axis=2)
    imag_part = jnp.sum(link_real[None] * spin_imag + link_imag[None] * spin_real, axis=2)
    return jnp.stack([real_part, imag_part])


def complex_scale(factor_real, factor_imag, lattice):
    return jnp.stack(
        [
            factor_real * lattice[0] - factor_imag * lattice[1],
            factor_real * lattice[1] + factor_imag * lattice[0],
        ]
    )


def apply_blocks(blocks, nearby):
    matrices = blocks.reshape(blocks.shape[0], 2, CDOF, CDOF, AGG)
    vector_real = nearby[:, 0][:, None]
    vector_imag = nearby[:, 1][:, None]
    real_part = jnp.sum(matrices[:, 0] * vector_real - matrices[:, 1] * vector_imag, axis=(0, 2))
    imag_part = jnp.sum(matrices[:, 0] * vector_imag + matrices[:, 1] * vector_real, axis=(0, 2))
    return jnp.stack([real_part, imag_part])


def keep_if(allowed, values):
    return jnp.where(allowed, values, jnp.zeros_like(values))


def permute_from(value, axis, offset, allowed):
    size = lax.axis_size(axis)
    pairs = [((i + offset) % size, i) for i in range(size) if allowed(i)]
    if not pairs:
        return None
    return lax.ppermute(value, axis, pairs)


class Shifts:
    def __init__(self, rows, lanes):
        self.rows = rows
        self.lanes = lanes
        self.lane = lax.broadcasted_iota(jnp.int32, (rows, lanes), 1)
        self.row = lax.broadcasted_iota(jnp.int32, (rows, lanes), 0)
        self.xpos = self.lane % CX
        self.zpos = self.row % 4

    def roll(self, a, shift, axis):
        n = a.shape[axis]
        return pltpu.roll(a, shift % n, a.ndim + axis)

    def ahead(self, direction, a, nbr):
        if direction == 0:
            return jnp.where(self.xpos == CX - 1, self.roll(a, CX - 1, -1), self.roll(a, -1, -1))
        if direction == 1:
            half = self.lanes // 2
            filled = jnp.where(self.lane < half, 0.0 if nbr is None else nbr, a)
            return self.roll(filled, half, -1)
        if direction == 2:
            inner = self.roll(a, -1, -2)
            outer = 0.0 if nbr is None else self.roll(nbr, 3, -2)
            return jnp.where(self.zpos == 3, outer, inner)
        filled = jnp.where(self.row < 4, 0.0 if nbr is None else nbr, a)
        return self.roll(filled, -4, -2)

    def behind(self, direction, a, nbr):
        if direction == 0:
            return jnp.where(self.xpos == 0, self.roll(a, 1 - CX, -1), self.roll(a, 1, -1))
        if direction == 1:
            half = self.lanes // 2
            filled = jnp.where(self.lane >= half, 0.0 if nbr is None else nbr, a)
            return self.roll(filled, half, -1)
        if direction == 2:
            inner = self.roll(a, 1, -2)
            outer = 0.0 if nbr is None else self.roll(nbr, -3, -2)
            return jnp.where(self.zpos == 0, outer, inner)
        filled = jnp.where(self.row >= self.rows - 4, 0.0 if nbr is None else nbr, a)
        return self.roll(filled, 4, -2)


def hopping(spinor, links, back_links, ahead_list, behind_list):
    hop_total = None
    for direction in range(4):
        ahead_half = colour_product(links[direction], project_minus(direction, ahead_list[direction]), False)
        behind_half = colour_product(back_links[direction], project_plus(direction, behind_list[direction]), True)
        term = rebuild_minus(direction, ahead_half) + rebuild_plus(direction, behind_half)
        hop_total = term if hop_total is None else hop_total + term
    return 4.5 * spinor - 0.5 * hop_total


def pass_kernel(*refs, first, residual_only, present):
    refs = list(refs)
    out_ref = refs.pop()

    def take():
        return refs.pop(0)

    src_ref = take()
    links_ref = take()
    ghost_refs = [None, None, None, None]
    for direction in (1, 2, 3):
        if present["ghost"][direction]:
            ghost_refs[direction] = take()
    labels_ref = take()
    member_ref = take()
    cmask_ref = None if residual_only else take()
    spinor_ref = None
    halo_refs = {}
    if not first:
        spinor_ref = take()
        for direction in (1, 2, 3):
            for side in ("ahead", "behind"):
                if present[side][direction]:
                    halo_refs[(side, direction)] = take()

    rows, lanes = src_ref.shape[-2], src_ref.shape[-1]
    sh = Shifts(rows, lanes)
    shape = (2, 4, 3, rows, lanes)
    source = src_ref[...].reshape(shape)
    link_all = links_ref[...].astype(jnp.float32)
    links = [link_all[d].reshape(2, 3, 3, rows, lanes) for d in range(4)]
    back_links = []
    for direction in range(4):
        ghost = None
        if ghost_refs[direction] is not None:
            ghost = ghost_refs[direction][...].astype(jnp.float32).reshape(2, 3, 3, rows, lanes)
        back_links.append(sh.behind(direction, links[direction], ghost))

    def load_halo(side, direction):
        ref = halo_refs.get((side, direction))
        return None if ref is None else ref[...].reshape(shape)

    def wilson_global(spinor):
        ahead_list = [sh.ahead(d, spinor, load_halo("ahead", d)) for d in range(4)]
        behind_list = [sh.behind(d, spinor, load_halo("behind", d)) for d in range(4)]
        return hopping(spinor, links, back_links, ahead_list, behind_list)

    if first:
        residue = source
        current = None
    else:
        current = spinor_ref[...].reshape(shape)
        residue = source - wilson_global(current)
    if residual_only:
        out_ref[...] = residue.reshape(out_ref.shape)
        return

    labels = labels_ref[...]
    ahead_masks = [(sh.ahead(d, labels, None) == labels).astype(jnp.float32) for d in range(4)]
    behind_masks = [(sh.behind(d, labels, None) == labels).astype(jnp.float32) for d in range(4)]
    member = member_ref[...]

    def wilson_block(spinor):
        ahead_list = [sh.ahead(d, spinor, None) * ahead_masks[d] for d in range(4)]
        behind_list = [sh.behind(d, spinor, None) * behind_masks[d] for d in range(4)]
        return hopping(spinor, links, back_links, ahead_list, behind_list)

    def block_total(values):
        return jnp.sum(jnp.sum(member * values[None], axis=2, keepdims=True), axis=1, keepdims=True)

    update = None
    remainder = residue
    for repeat in range(MR_STEPS):
        image = wilson_block(remainder)
        image_flat = image.reshape(2, 12, rows, lanes)
        rest_flat = remainder.reshape(2, 12, rows, lanes)
        dot_real = jnp.sum(image_flat[0] * rest_flat[0] + image_flat[1] * rest_flat[1], axis=0)
        dot_imag = jnp.sum(image_flat[0] * rest_flat[1] - image_flat[1] * rest_flat[0], axis=0)
        norm = jnp.sum(image_flat[0] * image_flat[0] + image_flat[1] * image_flat[1], axis=0)
        denominator = block_total(norm) + 1e-06
        factor_real = jnp.sum(member * (block_total(dot_real) / denominator), axis=0)
        factor_imag = jnp.sum(member * (block_total(dot_imag) / denominator), axis=0)
        step = complex_scale(factor_real, factor_imag, remainder)
        update = step if update is None else update + step
        remainder = remainder - complex_scale(factor_real, factor_imag, image)
    update = update * cmask_ref[...]
    result = update if current is None else current + update
    out_ref[...] = result.reshape(out_ref.shape)


def run_pass(source, links, ghosts, labels, member, cmask, spinor, halos, residual_only=False):
    first = spinor is None
    present = {
        "ghost": [g is not None for g in ghosts],
        "ahead": [h is not None for h in halos["ahead"]] if not first else [False] * 4,
        "behind": [h is not None for h in halos["behind"]] if not first else [False] * 4,
    }
    operands = [source, links] + [g for g in ghosts[1:] if g is not None] + [labels, member]
    if not residual_only:
        operands.append(cmask)
    if not first:
        operands.append(spinor)
        for direction in (1, 2, 3):
            for side in ("ahead", "behind"):
                if present[side][direction]:
                    operands.append(halos[side][direction])
    kernel = functools.partial(pass_kernel, first=first, residual_only=residual_only, present=present)
    return pl.pallas_call(kernel, out_shape=jax.ShapeDtypeStruct(source.shape, jnp.float32))(*operands)


def coarse_kernel(*refs, present):
    refs = list(refs)
    out_ref = refs.pop()
    source_ref, inverse_ref = refs[0], refs[1]
    first = len(refs) == 2
    width = source_ref.shape[-1]
    chunks = width // 128
    lane = lax.broadcasted_iota(jnp.int32, (1, width), 1)
    position = lane % AGG
    selector = (
        lax.broadcasted_iota(jnp.int32, (8, 128), 1) // AGG == lax.broadcasted_iota(jnp.int32, (8, 128), 0)
    ).astype(jnp.float32)

    def reduce_flat(product):
        partial = product[:, 0:128]
        for q in range(1, chunks):
            partial = partial + product[:, q * 128:(q + 1) * 128]
        for shift in (64, 32, 16):
            partial = partial + pltpu.roll(partial, shift, 1)
        pieces = [
            jnp.sum(partial[8 * q:8 * q + 8] * selector, axis=0, keepdims=True) for q in range(chunks)
        ]
        return jnp.concatenate(pieces, axis=1)

    def roll_within(vector, shift):
        pieces = [pltpu.roll(vector[:, q * 128:(q + 1) * 128], shift % 128, 1) for q in range(chunks)]
        return jnp.concatenate(pieces, axis=1)

    def accumulate(acc, blocks_ref, index, vector):
        block_real = blocks_ref[index + (0,)].astype(jnp.float32)
        block_imag = blocks_ref[index + (1,)].astype(jnp.float32)
        real_part = block_real * vector[0] - block_imag * vector[1]
        imag_part = block_real * vector[1] + block_imag * vector[0]
        if acc is None:
            return [real_part, imag_part]
        return [acc[0] + real_part, acc[1] + imag_part]

    def precondition(vector):
        acc = accumulate(None, inverse_ref, (), vector)
        return [reduce_flat(acc[0]), reduce_flat(acc[1])]

    source = [source_ref[0], source_ref[1]]
    if first:
        result = precondition(source)
    else:
        operator_ref, current_ref = refs[2], refs[3]
        nearby_refs = refs[4:]
        current = [current_ref[0], current_ref[1]]
        ahead = [
            jnp.where(position == AGG - 1, roll_within(c, AGG - 1), roll_within(c, -1)) for c in current
        ]
        behind = [jnp.where(position == 0, roll_within(c, 1 - AGG), roll_within(c, 1)) for c in current]
        vectors = [current, ahead, behind]
        taken = 0
        for flag in present:
            if flag:
                vectors.append([nearby_refs[taken][0], nearby_refs[taken][1]])
                taken += 1
            else:
                vectors.append(None)
        acc = None
        for direction, vector in enumerate(vectors):
            if vector is not None:
                acc = accumulate(acc, operator_ref, (direction,), vector)
        residue = [source[0] - reduce_flat(acc[0]), source[1] - reduce_flat(acc[1])]
        step = precondition(residue)
        result = [current[0] + step[0], current[1] + step[1]]
    out_ref[0] = result[0]
    out_ref[1] = result[1]


def run_coarse(source, inverse_blocks, operator_blocks, current, nearby):
    operands = [source, inverse_blocks]
    present = ()
    if current is not None:
        present = tuple(v is not None for v in nearby)
        operands += [operator_blocks, current] + [v for v in nearby if v is not None]
    kernel = functools.partial(coarse_kernel, present=present)
    return pl.pallas_call(kernel, out_shape=jax.ShapeDtypeStruct(source.shape, jnp.float32))(*operands)


def body(
    fine_source, links, test_vectors, aggregate_map, colouring, coarse_operator, block_inverse
):
    time_extent = fine_source.shape[2]
    plane_extent = fine_source.shape[3]
    line_extent = fine_source.shape[4]
    rows = time_extent * plane_extent
    site_count = rows * line_extent
    domain_index = lax.axis_index("lat")
    domain_count = lax.axis_size("lat")
    plane_position = (domain_index + 2) % PZ
    upper_valid = plane_position < PZ - 1
    lower_valid = plane_position > 0
    later_valid = domain_index < domain_count - PZ
    earlier_valid = domain_index >= PZ

    source = fine_source.reshape(24, rows, line_extent)
    link_rows = links.reshape(4, 18, rows, line_extent)
    label_rows = aggregate_map.reshape(rows, line_extent)
    member = (label_rows[None] == jnp.arange(AGG, dtype=jnp.int32)[:, None, None]).astype(jnp.float32)
    colour_list = colouring.reshape(AGG)
    colour_masks = [
        jnp.sum(member * (colour_list == k).astype(jnp.float32)[:, None, None], axis=0) for k in range(2)
    ]
    labels = (label_rows + 1).astype(jnp.float32)

    def z_up_ok(i):
        return (i + 2) % PZ != PZ - 1

    def z_down_ok(i):
        return (i + 2) % PZ != 0

    def t_up_ok(i):
        return i + PZ < domain_count

    def t_down_ok(i):
        return i - PZ >= 0

    ghosts = [
        None,
        permute_from(link_rows[1], "grp", -1, lambda i: True),
        permute_from(link_rows[2], "lat", -1, z_down_ok),
        permute_from(link_rows[3], "lat", -PZ, t_down_ok),
    ]

    def halos_of(spinor):
        return {
            "ahead": [
                None,
                permute_from(spinor, "grp", 1, lambda i: True),
                permute_from(spinor, "lat", 1, z_up_ok),
                permute_from(spinor, "lat", PZ, t_up_ok),
            ],
            "behind": [
                None,
                permute_from(spinor, "grp", -1, lambda i: True),
                permute_from(spinor, "lat", -1, z_down_ok),
                permute_from(spinor, "lat", -PZ, t_down_ok),
            ],
        }

    def smoother_pass(spinor, colour_pass):
        halos = None if spinor is None else halos_of(spinor)
        return run_pass(source, link_rows, ghosts, labels, member, colour_masks[colour_pass], spinor, halos)

    def sweep(start):
        current = smoother_pass(start, 0)
        return smoother_pass(current, 1)

    smoothed = sweep(None)
    residue = run_pass(
        source, link_rows, ghosts, labels, member, None, smoothed, halos_of(smoothed), residual_only=True
    )
    residual = residue.astype(jnp.bfloat16)
    membership = member.reshape(AGG, site_count).T
    member_weights = membership.astype(jnp.bfloat16)
    weighted = residual.reshape(2, 2, 6, site_count)[..., None] * member_weights
    vectors = test_vectors.reshape(NVEC, 2, 2, 6, site_count)

    def contract(left, right):
        return jnp.einsum("kxqn,xqnj->xkj", left, right, preferred_element_type=jnp.float32)

    real_part = contract(vectors[:, 0], weighted[0]) + contract(vectors[:, 1], weighted[1])
    imag_part = contract(vectors[:, 0], weighted[1]) - contract(vectors[:, 1], weighted[0])
    coarse_source = jnp.stack([real_part, imag_part]).reshape(2, CDOF, AGG)
    flat_source = coarse_source.reshape(2, 1, CDOF * AGG)
    operator_blocks = coarse_operator.reshape(9, 2, CDOF, CDOF * AGG)
    inverse_blocks = block_inverse.reshape(2, CDOF, CDOF * AGG)
    correction = run_coarse(flat_source, inverse_blocks, operator_blocks, None, None)
    for repeat in range(2):
        nearby = [
            permute_from(correction, "grp", 1, lambda i: True),
            permute_from(correction, "grp", -1, lambda i: True),
            permute_from(correction, "lat", 1, z_up_ok),
            permute_from(correction, "lat", -1, z_down_ok),
            permute_from(correction, "lat", PZ, t_up_ok),
            permute_from(correction, "lat", -PZ, t_down_ok),
        ]
        correction = run_coarse(flat_source, inverse_blocks, operator_blocks, correction, nearby)
    correction = correction.reshape(2, CDOF, AGG)
    expanded = jnp.dot(
        correction.reshape(2 * CDOF, AGG), membership.T, precision=lax.Precision.HIGHEST
    ).reshape(2, 2, NVEC, site_count)
    spread_real = jnp.swapaxes(expanded[0], 0, 1)[:, :, None]
    spread_imag = jnp.swapaxes(expanded[1], 0, 1)[:, :, None]
    real_part = jnp.sum(vectors[:, 0] * spread_real - vectors[:, 1] * spread_imag, axis=0)
    imag_part = jnp.sum(vectors[:, 0] * spread_imag + vectors[:, 1] * spread_real, axis=0)
    corrected = smoothed + jnp.stack([real_part, imag_part]).reshape(24, rows, line_extent)
    solution = sweep(corrected)
    return (
        solution.reshape(1, 24, time_extent, plane_extent, line_extent),
        correction.reshape(1, 1, 2, CDOF, AGG),
    )


def solution(mesh):
    return jax.shard_map(
        body,
        mesh=mesh,
        in_specs=(
            P("lat", None, None, None, "grp"),
            P("lat", None, None, None, None, "grp"),
            P("lat", None, None, None, None, "grp"),
            P("lat", None, None, "grp", None),
            P("lat", "grp", None),
            P("lat", "grp", None, None, None, None),
            P("lat", "grp", None, None, None),
        ),
        out_specs=(P("lat", None, None, None, "grp"), P("lat", "grp", None, None, None)),
        check_vma=False,
    )
```

```python
import functools

import jax
import jax.numpy as jnp
from jax import lax
from jax.experimental import pallas as pl
from jax.experimental.pallas import tpu as pltpu
from jax.sharding import PartitionSpec as P

CX = 64
PZ = 8
NVEC = 24
AGG = 16
MR_STEPS = 2
CDOF = 48


def passed_along(shard, axis, by):
    size = lax.axis_size(axis)
    return lax.ppermute(shard, axis, [(i, (i + by) % size) for i in range(size)])


def padded_2(shard, sides, width):
    for axis, dim in sides:
        size, length = (lax.axis_size(axis), shard.shape[dim])
        up = [(i, (i + 1) % size) for i in range(size)]
        down = [(j, i) for i, j in up]
        last = lax.slice_in_dim(shard, length - width, length, axis=dim)
        first = lax.slice_in_dim(shard, 0, width, axis=dim)
        before = lax.ppermute(last, axis, up)
        after = lax.ppermute(first, axis, down)
        shard = jnp.concatenate([before, shard, after], axis=dim)
    return shard


def times_minus_i(values):
    return jnp.stack([values[1], -values[0]])


def times_plus_i(values):
    return jnp.stack([-values[1], values[0]])


def spin_factor(direction, spin_pair):
    if direction == 0:
        return jnp.stack([times_minus_i(spin_pair[:, 1]), times_minus_i(spin_pair[:, 0])], axis=1)
    if direction == 1:
        return jnp.stack([-spin_pair[:, 1], spin_pair[:, 0]], axis=1)
    if direction == 2:
        return jnp.stack([times_minus_i(spin_pair[:, 0]), times_plus_i(spin_pair[:, 1])], axis=1)
    return spin_pair


def project_minus(direction, spinor):
    return spinor[:, :2] - spin_factor(direction, spinor[:, 2:])


def project_plus(direction, spinor):
    return spinor[:, :2] + spin_factor(direction, spinor[:, 2:])


def rebuild_minus(direction, half_spinor):
    lower_part = spin_factor(direction, half_spinor) if direction < 3 else -half_spinor
    return jnp.concatenate([half_spinor, lower_part], axis=1)


def rebuild_plus(direction, half_spinor):
    lower_part = -spin_factor(direction, half_spinor) if direction < 3 else half_spinor
    return jnp.concatenate([half_spinor, lower_part], axis=1)


def colour_product(gauge_link, half_spinor, adjoint):
    link_real = gauge_link[0]
    link_imag = gauge_link[1]
    if adjoint:
        link_real = jnp.swapaxes(link_real, 0, 1)
        link_imag = -jnp.swapaxes(link_imag, 0, 1)
    spin_real = half_spinor[0][:, None]
    spin_imag = half_spinor[1][:, None]
    real_part = jnp.sum(link_real[None] * spin_real - link_imag[None] * spin_imag, axis=2)
    imag_part = jnp.sum(link_real[None] * spin_imag + link_imag[None] * spin_real, axis=2)
    return jnp.stack([real_part, imag_part])


def complex_scale(factor_real, factor_imag, lattice):
    return jnp.stack(
        [
            factor_real * lattice[0] - factor_imag * lattice[1],
            factor_real * lattice[1] + factor_imag * lattice[0],
        ]
    )


def apply_blocks(blocks, nearby):
    matrices = blocks.reshape(blocks.shape[0], 2, CDOF, CDOF, AGG)
    vector_real = nearby[:, 0][:, None]
    vector_imag = nearby[:, 1][:, None]
    real_part = jnp.sum(matrices[:, 0] * vector_real - matrices[:, 1] * vector_imag, axis=(0, 2))
    imag_part = jnp.sum(matrices[:, 0] * vector_imag + matrices[:, 1] * vector_real, axis=(0, 2))
    return jnp.stack([real_part, imag_part])


def keep_if(allowed, values):
    return jnp.where(allowed, values, jnp.zeros_like(values))


def permute_from(value, axis, offset, allowed):
    size = lax.axis_size(axis)
    pairs = [((i + offset) % size, i) for i in range(size) if allowed(i)]
    if not pairs:
        return None
    return lax.ppermute(value, axis, pairs)


class Shifts:
    def __init__(self, rows, lanes):
        self.rows = rows
        self.lanes = lanes
        self.lane = lax.broadcasted_iota(jnp.int32, (rows, lanes), 1)
        self.row = lax.broadcasted_iota(jnp.int32, (rows, lanes), 0)
        self.xpos = self.lane % CX
        self.zpos = self.row % 4

    def roll(self, a, shift, axis):
        n = a.shape[axis]
        return pltpu.roll(a, shift % n, a.ndim + axis)

    def ahead(self, direction, a, nbr, placed=False):
        if direction == 0:
            return jnp.where(self.xpos == CX - 1, self.roll(a, CX - 1, -1), self.roll(a, -1, -1))
        if direction == 1:
            half = self.lanes // 2
            filled = jnp.where(self.lane < half, 0.0 if nbr is None else nbr, a)
            return self.roll(filled, half, -1)
        if direction == 2:
            inner = self.roll(a, -1, -2)
            outer = 0.0 if nbr is None else (nbr if placed else self.roll(nbr, 3, -2))
            return jnp.where(self.zpos == 3, outer, inner)
        filled = jnp.where(self.row < 4, 0.0 if nbr is None else nbr, a)
        return self.roll(filled, -4, -2)

    def behind(self, direction, a, nbr, placed=False):
        if direction == 0:
            return jnp.where(self.xpos == 0, self.roll(a, 1 - CX, -1), self.roll(a, 1, -1))
        if direction == 1:
            half = self.lanes // 2
            filled = jnp.where(self.lane >= half, 0.0 if nbr is None else nbr, a)
            return self.roll(filled, half, -1)
        if direction == 2:
            inner = self.roll(a, 1, -2)
            outer = 0.0 if nbr is None else (nbr if placed else self.roll(nbr, -3, -2))
            return jnp.where(self.zpos == 0, outer, inner)
        filled = jnp.where(self.row >= self.rows - 4, 0.0 if nbr is None else nbr, a)
        return self.roll(filled, 4, -2)


def hopping(spinor, links, back_links, ahead_list, behind_list):
    hop_total = None
    for direction in range(4):
        ahead_half = colour_product(links[direction], project_minus(direction, ahead_list[direction]), False)
        behind_half = colour_product(back_links[direction], project_plus(direction, behind_list[direction]), True)
        term = rebuild_minus(direction, ahead_half) + rebuild_plus(direction, behind_half)
        hop_total = term if hop_total is None else hop_total + term
    return 4.5 * spinor - 0.5 * hop_total


FACES = ("z_low", "z_high", "t_low", "t_high")


def face_rows(name):
    return {"z_low": (0, 4), "z_high": (3, 4), "t_low": (0, 1), "t_high": (12, 1)}[name]


def pass_kernel(*refs, first, residual_only, present, faces):
    refs = list(refs)
    scratch_refs = {}
    for key in reversed([k for k in (("ahead", 2), ("behind", 2), ("ahead", 3), ("behind", 3)) if present[k[0]][k[1]]]):
        scratch_refs[key] = refs.pop()
    face_refs = {}
    for name in reversed(faces):
        face_refs[name] = refs.pop()
    out_ref = refs.pop()

    def take():
        return refs.pop(0)

    src_ref = take()
    links_ref = take()
    ghost_refs = [None, None, None, None]
    for direction in (1, 2, 3):
        if present["ghost"][direction]:
            ghost_refs[direction] = take()
    labels_ref = take()
    member_ref = take()
    cmask_ref = None if residual_only else take()
    spinor_ref = None
    halo_refs = {}
    if not first:
        spinor_ref = take()
        for direction in (1, 2, 3):
            for side in ("ahead", "behind"):
                if present[side][direction]:
                    halo_refs[(side, direction)] = take()

    rows, lanes = src_ref.shape[-2], src_ref.shape[-1]
    sh = Shifts(rows, lanes)
    shape = (2, 4, 3, rows, lanes)
    source = src_ref[...].reshape(shape)
    link_all = links_ref[...].astype(jnp.float32)
    links = [link_all[d].reshape(2, 3, 3, rows, lanes) for d in range(4)]
    back_links = []
    for direction in range(4):
        ghost = None
        if ghost_refs[direction] is not None:
            ghost = ghost_refs[direction][...].astype(jnp.float32).reshape(2, 3, 3, rows, lanes)
        back_links.append(sh.behind(direction, links[direction], ghost))

    placement = {("ahead", 2): (3, 4), ("behind", 2): (0, 4), ("ahead", 3): (0, 1), ("behind", 3): (12, 1)}
    for key, scratch in scratch_refs.items():
        start, stride = placement[key]
        scratch[:, pl.ds(start, 4, stride=stride), :] = halo_refs[key][...]

    def load_halo(side, direction):
        ref = scratch_refs.get((side, direction), halo_refs.get((side, direction)))
        return None if ref is None else ref[...].reshape(shape)

    def wilson_global(spinor):
        ahead_list = [sh.ahead(d, spinor, load_halo("ahead", d), True) for d in range(4)]
        behind_list = [sh.behind(d, spinor, load_halo("behind", d), True) for d in range(4)]
        return hopping(spinor, links, back_links, ahead_list, behind_list)

    if first:
        residue = source
        current = None
    else:
        current = spinor_ref[...].reshape(shape)
        residue = source - wilson_global(current)
    if residual_only:
        out_ref[...] = residue.reshape(out_ref.shape)
        return

    labels = labels_ref[...]
    ahead_masks = [(sh.ahead(d, labels, None) == labels).astype(jnp.float32) for d in range(4)]
    behind_masks = [(sh.behind(d, labels, None) == labels).astype(jnp.float32) for d in range(4)]
    member = member_ref[...]

    def wilson_block(spinor):
        ahead_list = [sh.ahead(d, spinor, None) * ahead_masks[d] for d in range(4)]
        behind_list = [sh.behind(d, spinor, None) * behind_masks[d] for d in range(4)]
        return hopping(spinor, links, back_links, ahead_list, behind_list)

    def block_total(values):
        return jnp.sum(jnp.sum(member * values[None], axis=2, keepdims=True), axis=1, keepdims=True)

    update = None
    remainder = residue
    for repeat in range(MR_STEPS):
        image = wilson_block(remainder)
        image_flat = image.reshape(2, 12, rows, lanes)
        rest_flat = remainder.reshape(2, 12, rows, lanes)
        dot_real = jnp.sum(image_flat[0] * rest_flat[0] + image_flat[1] * rest_flat[1], axis=0)
        dot_imag = jnp.sum(image_flat[0] * rest_flat[1] - image_flat[1] * rest_flat[0], axis=0)
        norm = jnp.sum(image_flat[0] * image_flat[0] + image_flat[1] * image_flat[1], axis=0)
        denominator = block_total(norm) + 1e-06
        factor_real = jnp.sum(member * (block_total(dot_real) / denominator), axis=0)
        factor_imag = jnp.sum(member * (block_total(dot_imag) / denominator), axis=0)
        step = complex_scale(factor_real, factor_imag, remainder)
        update = step if update is None else update + step
        remainder = remainder - complex_scale(factor_real, factor_imag, image)
    update = update * cmask_ref[...]
    result = update if current is None else current + update
    out_ref[...] = result.reshape(out_ref.shape)
    for name, face_ref in face_refs.items():
        start, stride = face_rows(name)
        face_ref[...] = out_ref[:, pl.ds(start, 4, stride=stride), :]


def run_pass(source, links, ghosts, labels, member, cmask, spinor, halos, residual_only=False, faces=()):
    first = spinor is None
    if first:
        ghosts = [None, None, None, None]
    present = {
        "ghost": [g is not None for g in ghosts],
        "ahead": [h is not None for h in halos["ahead"]] if not first else [False] * 4,
        "behind": [h is not None for h in halos["behind"]] if not first else [False] * 4,
    }
    operands = [source, links] + [g for g in ghosts[1:] if g is not None] + [labels, member]
    if not residual_only:
        operands.append(cmask)
    if not first:
        operands.append(spinor)
        for direction in (1, 2, 3):
            for side in ("ahead", "behind"):
                if present[side][direction]:
                    operands.append(halos[side][direction])
    kernel = functools.partial(
        pass_kernel, first=first, residual_only=residual_only, present=present, faces=faces
    )
    face_shape = (source.shape[0], 4, source.shape[2])
    out_shape = [jax.ShapeDtypeStruct(source.shape, jnp.float32)]
    out_shape += [jax.ShapeDtypeStruct(face_shape, jnp.float32) for name in faces]
    scratch = [
        pltpu.VMEM(source.shape, jnp.float32)
        for k in (("ahead", 2), ("behind", 2), ("ahead", 3), ("behind", 3))
        if present[k[0]][k[1]]
    ]
    results = pl.pallas_call(kernel, out_shape=out_shape, scratch_shapes=scratch)(*operands)
    return results[0], dict(zip(faces, results[1:]))


def coarse_kernel(*refs, present):
    refs = list(refs)
    out_ref = refs.pop()
    source_ref, inverse_ref = refs[0], refs[1]
    first = len(refs) == 2
    width = source_ref.shape[-1]
    chunks = width // 128
    lane = lax.broadcasted_iota(jnp.int32, (1, width), 1)
    position = lane % AGG
    selector = (
        lax.broadcasted_iota(jnp.int32, (8, 128), 1) // AGG == lax.broadcasted_iota(jnp.int32, (8, 128), 0)
    ).astype(jnp.float32)

    def reduce_flat(product):
        partial = product[:, 0:128]
        for q in range(1, chunks):
            partial = partial + product[:, q * 128:(q + 1) * 128]
        for shift in (64, 32, 16):
            partial = partial + pltpu.roll(partial, shift, 1)
        pieces = [
            jnp.sum(partial[8 * q:8 * q + 8] * selector, axis=0, keepdims=True) for q in range(chunks)
        ]
        return jnp.concatenate(pieces, axis=1)

    def roll_within(vector, shift):
        pieces = [pltpu.roll(vector[:, q * 128:(q + 1) * 128], shift % 128, 1) for q in range(chunks)]
        return jnp.concatenate(pieces, axis=1)

    def accumulate(acc, blocks_ref, index, vector):
        block_real = blocks_ref[index + (0,)].astype(jnp.float32)
        block_imag = blocks_ref[index + (1,)].astype(jnp.float32)
        real_part = block_real * vector[0] - block_imag * vector[1]
        imag_part = block_real * vector[1] + block_imag * vector[0]
        if acc is None:
            return [real_part, imag_part]
        return [acc[0] + real_part, acc[1] + imag_part]

    def precondition(vector):
        acc = accumulate(None, inverse_ref, (), vector)
        return [reduce_flat(acc[0]), reduce_flat(acc[1])]

    source = [source_ref[0], source_ref[1]]
    if first:
        result = precondition(source)
    else:
        operator_ref, current_ref = refs[2], refs[3]
        nearby_refs = refs[4:]
        current = [current_ref[0], current_ref[1]]
        ahead = [
            jnp.where(position == AGG - 1, roll_within(c, AGG - 1), roll_within(c, -1)) for c in current
        ]
        behind = [jnp.where(position == 0, roll_within(c, 1 - AGG), roll_within(c, 1)) for c in current]
        vectors = [current, ahead, behind]
        taken = 0
        for flag in present:
            if flag:
                vectors.append([nearby_refs[taken][0], nearby_refs[taken][1]])
                taken += 1
            else:
                vectors.append(None)
        acc = None
        for direction, vector in enumerate(vectors):
            if vector is not None:
                acc = accumulate(acc, operator_ref, (direction,), vector)
        residue = [source[0] - reduce_flat(acc[0]), source[1] - reduce_flat(acc[1])]
        step = precondition(residue)
        result = [current[0] + step[0], current[1] + step[1]]
    out_ref[0] = result[0]
    out_ref[1] = result[1]


def run_coarse(source, inverse_blocks, operator_blocks, current, nearby):
    operands = [source, inverse_blocks]
    present = ()
    if current is not None:
        present = tuple(v is not None for v in nearby)
        operands += [operator_blocks, current] + [v for v in nearby if v is not None]
    kernel = functools.partial(coarse_kernel, present=present)
    return pl.pallas_call(kernel, out_shape=jax.ShapeDtypeStruct(source.shape, jnp.float32))(*operands)


def body(
    fine_source, links, test_vectors, aggregate_map, colouring, coarse_operator, block_inverse
):
    time_extent = fine_source.shape[2]
    plane_extent = fine_source.shape[3]
    line_extent = fine_source.shape[4]
    rows = time_extent * plane_extent
    site_count = rows * line_extent
    domain_index = lax.axis_index("lat")
    domain_count = lax.axis_size("lat")
    plane_position = (domain_index + 2) % PZ
    upper_valid = plane_position < PZ - 1
    lower_valid = plane_position > 0
    later_valid = domain_index < domain_count - PZ
    earlier_valid = domain_index >= PZ

    source = fine_source.reshape(24, rows, line_extent)
    link_rows = links.reshape(4, 18, rows, line_extent)
    label_rows = aggregate_map.reshape(rows, line_extent)
    member = (label_rows[None] == jnp.arange(AGG, dtype=jnp.int32)[:, None, None]).astype(jnp.float32)
    colour_list = colouring.reshape(AGG)
    colour_masks = [
        jnp.sum(member * (colour_list == k).astype(jnp.float32)[:, None, None], axis=0) for k in range(2)
    ]
    labels = (label_rows + 1).astype(jnp.float32)

    def z_up_ok(i):
        return (i + 2) % PZ != PZ - 1

    def z_down_ok(i):
        return (i + 2) % PZ != 0

    def t_up_ok(i):
        return i + PZ < domain_count

    def t_down_ok(i):
        return i - PZ >= 0

    ghosts = [
        None,
        permute_from(link_rows[1], "grp", -1, lambda i: True),
        permute_from(link_rows[2], "lat", -1, z_down_ok),
        permute_from(link_rows[3], "lat", -PZ, t_down_ok),
    ]

    needed = [name for name, ok in zip(FACES, (z_up_ok, z_down_ok, t_up_ok, t_down_ok))
              if any(ok(i) for i in range(domain_count))]

    def faces_of(spinor):
        result = {}
        for name in needed:
            start, stride = face_rows(name)
            result[name] = lax.slice_in_dim(spinor, start, start + 3 * stride + 1, stride, axis=1)
        return result

    def halos_of(spinor, faces):
        def face(name):
            return faces[name] if name in faces else None

        return {
            "ahead": [
                None,
                permute_from(spinor, "grp", 1, lambda i: True),
                permute_from(face("z_low"), "lat", 1, z_up_ok) if face("z_low") is not None else None,
                permute_from(face("t_low"), "lat", PZ, t_up_ok) if face("t_low") is not None else None,
            ],
            "behind": [
                None,
                permute_from(spinor, "grp", -1, lambda i: True),
                permute_from(face("z_high"), "lat", -1, z_down_ok) if face("z_high") is not None else None,
                permute_from(face("t_high"), "lat", -PZ, t_down_ok) if face("t_high") is not None else None,
            ],
        }

    def smoother_pass(spinor, faces, colour_pass, out_faces):
        halos = None if spinor is None else halos_of(spinor, faces)
        return run_pass(
            source, link_rows, ghosts, labels, member, colour_masks[colour_pass], spinor, halos,
            faces=out_faces,
        )

    def sweep(start, faces, last_faces):
        current, current_faces = smoother_pass(start, faces, 0, tuple(needed))
        return smoother_pass(current, current_faces, 1, last_faces)

    smoothed, smoothed_faces = sweep(None, None, tuple(needed))
    residue, _ = run_pass(
        source, link_rows, ghosts, labels, member, None, smoothed, halos_of(smoothed, smoothed_faces),
        residual_only=True,
    )
    residual = residue.astype(jnp.bfloat16)
    membership = member.reshape(AGG, site_count).T
    member_weights = membership.astype(jnp.bfloat16)
    weighted = residual.reshape(2, 2, 6, site_count)[..., None] * member_weights
    vectors = test_vectors.reshape(NVEC, 2, 2, 6, site_count)

    def contract(left, right):
        return jnp.einsum("kxqn,xqnj->xkj", left, right, preferred_element_type=jnp.float32)

    real_part = contract(vectors[:, 0], weighted[0]) + contract(vectors[:, 1], weighted[1])
    imag_part = contract(vectors[:, 0], weighted[1]) - contract(vectors[:, 1], weighted[0])
    coarse_source = jnp.stack([real_part, imag_part]).reshape(2, CDOF, AGG)
    flat_source = coarse_source.reshape(2, 1, CDOF * AGG)
    operator_blocks = coarse_operator.reshape(9, 2, CDOF, CDOF * AGG)
    inverse_blocks = block_inverse.reshape(2, CDOF, CDOF * AGG)
    correction = run_coarse(flat_source, inverse_blocks, operator_blocks, None, None)
    for repeat in range(2):
        nearby = [
            permute_from(correction, "grp", 1, lambda i: True),
            permute_from(correction, "grp", -1, lambda i: True),
            permute_from(correction, "lat", 1, z_up_ok),
            permute_from(correction, "lat", -1, z_down_ok),
            permute_from(correction, "lat", PZ, t_up_ok),
            permute_from(correction, "lat", -PZ, t_down_ok),
        ]
        correction = run_coarse(flat_source, inverse_blocks, operator_blocks, correction, nearby)
    correction = correction.reshape(2, CDOF, AGG)
    expanded = jnp.dot(
        correction.reshape(2 * CDOF, AGG), membership.T, precision=lax.Precision.HIGHEST
    ).reshape(2, 2, NVEC, site_count)
    spread_real = jnp.swapaxes(expanded[0], 0, 1)[:, :, None]
    spread_imag = jnp.swapaxes(expanded[1], 0, 1)[:, :, None]
    real_part = jnp.sum(vectors[:, 0] * spread_real - vectors[:, 1] * spread_imag, axis=0)
    imag_part = jnp.sum(vectors[:, 0] * spread_imag + vectors[:, 1] * spread_real, axis=0)
    corrected = smoothed + jnp.stack([real_part, imag_part]).reshape(24, rows, line_extent)
    solution, _ = sweep(corrected, faces_of(corrected), ())
    return (
        solution.reshape(1, 24, time_extent, plane_extent, line_extent),
        correction.reshape(1, 1, 2, CDOF, AGG),
    )


def solution(mesh):
    return jax.shard_map(
        body,
        mesh=mesh,
        in_specs=(
            P("lat", None, None, None, "grp"),
            P("lat", None, None, None, None, "grp"),
            P("lat", None, None, None, None, "grp"),
            P("lat", None, None, "grp", None),
            P("lat", "grp", None),
            P("lat", "grp", None, None, None, None),
            P("lat", "grp", None, None, None),
        ),
        out_specs=(P("lat", None, None, None, "grp"), P("lat", "grp", None, None, None)),
        check_vma=False,
    )
```

```python
import functools

import jax
import jax.numpy as jnp
from jax import lax
from jax.experimental import pallas as pl
from jax.experimental.pallas import tpu as pltpu
from jax.sharding import PartitionSpec as P

CX = 64
PZ = 8
NVEC = 24
AGG = 16
MR_STEPS = 2
CDOF = 48


def passed_along(shard, axis, by):
    size = lax.axis_size(axis)
    return lax.ppermute(shard, axis, [(i, (i + by) % size) for i in range(size)])


def padded_2(shard, sides, width):
    for axis, dim in sides:
        size, length = (lax.axis_size(axis), shard.shape[dim])
        up = [(i, (i + 1) % size) for i in range(size)]
        down = [(j, i) for i, j in up]
        last = lax.slice_in_dim(shard, length - width, length, axis=dim)
        first = lax.slice_in_dim(shard, 0, width, axis=dim)
        before = lax.ppermute(last, axis, up)
        after = lax.ppermute(first, axis, down)
        shard = jnp.concatenate([before, shard, after], axis=dim)
    return shard


def times_minus_i(values):
    return jnp.stack([values[1], -values[0]])


def times_plus_i(values):
    return jnp.stack([-values[1], values[0]])


def spin_factor(direction, spin_pair):
    if direction == 0:
        return jnp.stack([times_minus_i(spin_pair[:, 1]), times_minus_i(spin_pair[:, 0])], axis=1)
    if direction == 1:
        return jnp.stack([-spin_pair[:, 1], spin_pair[:, 0]], axis=1)
    if direction == 2:
        return jnp.stack([times_minus_i(spin_pair[:, 0]), times_plus_i(spin_pair[:, 1])], axis=1)
    return spin_pair


def project_minus(direction, spinor):
    return spinor[:, :2] - spin_factor(direction, spinor[:, 2:])


def project_plus(direction, spinor):
    return spinor[:, :2] + spin_factor(direction, spinor[:, 2:])


def rebuild_minus(direction, half_spinor):
    lower_part = spin_factor(direction, half_spinor) if direction < 3 else -half_spinor
    return jnp.concatenate([half_spinor, lower_part], axis=1)


def rebuild_plus(direction, half_spinor):
    lower_part = -spin_factor(direction, half_spinor) if direction < 3 else half_spinor
    return jnp.concatenate([half_spinor, lower_part], axis=1)


def colour_product(gauge_link, half_spinor, adjoint):
    link_real = gauge_link[0]
    link_imag = gauge_link[1]
    if adjoint:
        link_real = jnp.swapaxes(link_real, 0, 1)
        link_imag = -jnp.swapaxes(link_imag, 0, 1)
    spin_real = half_spinor[0][:, None]
    spin_imag = half_spinor[1][:, None]
    real_part = jnp.sum(link_real[None] * spin_real - link_imag[None] * spin_imag, axis=2)
    imag_part = jnp.sum(link_real[None] * spin_imag + link_imag[None] * spin_real, axis=2)
    return jnp.stack([real_part, imag_part])


def complex_scale(factor_real, factor_imag, lattice):
    return jnp.stack(
        [
            factor_real * lattice[0] - factor_imag * lattice[1],
            factor_real * lattice[1] + factor_imag * lattice[0],
        ]
    )


def apply_blocks(blocks, nearby):
    matrices = blocks.reshape(blocks.shape[0], 2, CDOF, CDOF, AGG)
    vector_real = nearby[:, 0][:, None]
    vector_imag = nearby[:, 1][:, None]
    real_part = jnp.sum(matrices[:, 0] * vector_real - matrices[:, 1] * vector_imag, axis=(0, 2))
    imag_part = jnp.sum(matrices[:, 0] * vector_imag + matrices[:, 1] * vector_real, axis=(0, 2))
    return jnp.stack([real_part, imag_part])


def keep_if(allowed, values):
    return jnp.where(allowed, values, jnp.zeros_like(values))


def permute_from(value, axis, offset, allowed):
    size = lax.axis_size(axis)
    pairs = [((i + offset) % size, i) for i in range(size) if allowed(i)]
    if not pairs:
        return None
    return lax.ppermute(value, axis, pairs)


class Shifts:
    def __init__(self, rows, lanes):
        self.rows = rows
        self.lanes = lanes
        self.lane = lax.broadcasted_iota(jnp.int32, (rows, lanes), 1)
        self.row = lax.broadcasted_iota(jnp.int32, (rows, lanes), 0)
        self.xpos = self.lane % CX
        self.zpos = self.row % 4

    def roll(self, a, shift, axis):
        n = a.shape[axis]
        return pltpu.roll(a, shift % n, a.ndim + axis)

    def ahead(self, direction, a, nbr, placed=False):
        if direction == 0:
            return jnp.where(self.xpos == CX - 1, self.roll(a, CX - 1, -1), self.roll(a, -1, -1))
        if direction == 1:
            half = self.lanes // 2
            if placed and nbr is not None:
                return jnp.where(self.lane >= half, self.roll(nbr, half, -1), self.roll(a, half, -1))
            filled = jnp.where(self.lane < half, 0.0 if nbr is None else nbr, a)
            return self.roll(filled, half, -1)
        if direction == 2:
            inner = self.roll(a, -1, -2)
            outer = 0.0 if nbr is None else (nbr if placed else self.roll(nbr, 3, -2))
            return jnp.where(self.zpos == 3, outer, inner)
        filled = jnp.where(self.row < 4, 0.0 if nbr is None else nbr, a)
        return self.roll(filled, -4, -2)

    def behind(self, direction, a, nbr, placed=False):
        if direction == 0:
            return jnp.where(self.xpos == 0, self.roll(a, 1 - CX, -1), self.roll(a, 1, -1))
        if direction == 1:
            half = self.lanes // 2
            if placed and nbr is not None:
                return jnp.where(self.lane < half, nbr, self.roll(a, half, -1))
            filled = jnp.where(self.lane >= half, 0.0 if nbr is None else nbr, a)
            return self.roll(filled, half, -1)
        if direction == 2:
            inner = self.roll(a, 1, -2)
            outer = 0.0 if nbr is None else (nbr if placed else self.roll(nbr, -3, -2))
            return jnp.where(self.zpos == 0, outer, inner)
        filled = jnp.where(self.row >= self.rows - 4, 0.0 if nbr is None else nbr, a)
        return self.roll(filled, 4, -2)


def hopping(spinor, links, back_links, ahead_list, behind_list):
    hop_total = None
    for direction in range(4):
        ahead_half = colour_product(links[direction], project_minus(direction, ahead_list[direction]), False)
        behind_half = colour_product(back_links[direction], project_plus(direction, behind_list[direction]), True)
        term = rebuild_minus(direction, ahead_half) + rebuild_plus(direction, behind_half)
        hop_total = term if hop_total is None else hop_total + term
    return 4.5 * spinor - 0.5 * hop_total


FACES = ("y_low", "y_high", "z_low", "z_high", "t_low", "t_high")
HALO_KEYS = tuple((side, d) for d in (1, 2, 3) for side in ("ahead", "behind"))


def face_rows(name):
    return {"z_low": (0, 4), "z_high": (3, 4), "t_low": (0, 1), "t_high": (12, 1)}[name]


def place(scratch, value, side, direction):
    if direction == 1:
        scratch[..., pl.ds(0, value.shape[-1])] = value
        return
    start, stride = {("ahead", 2): (3, 4), ("behind", 2): (0, 4), ("ahead", 3): (0, 1), ("behind", 3): (12, 1)}[
        (side, direction)
    ]
    scratch[:, pl.ds(start, 4, stride=stride), :] = value


def pass_kernel(*refs, first, residual_only, present, faces):
    refs = list(refs)
    ghost_scratch = {}
    for direction in reversed([d for d in (1, 2, 3) if present["ghost"][d]]):
        ghost_scratch[direction] = refs.pop()
    scratch_refs = {}
    for key in reversed([k for k in HALO_KEYS if present[k[0]][k[1]]]):
        scratch_refs[key] = refs.pop()
    face_refs = {}
    for name in reversed(faces):
        face_refs[name] = refs.pop()
    out_ref = refs.pop()

    def take():
        return refs.pop(0)

    src_ref = take()
    links_ref = take()
    ghost_refs = [None, None, None, None]
    for direction in (1, 2, 3):
        if present["ghost"][direction]:
            ghost_refs[direction] = take()
    labels_ref = take()
    member_ref = take()
    cmask_ref = None if residual_only else take()
    spinor_ref = None
    halo_refs = {}
    if not first:
        spinor_ref = take()
        for direction in (1, 2, 3):
            for side in ("ahead", "behind"):
                if present[side][direction]:
                    halo_refs[(side, direction)] = take()

    rows, lanes = src_ref.shape[-2], src_ref.shape[-1]
    sh = Shifts(rows, lanes)
    shape = (2, 4, 3, rows, lanes)
    source = src_ref[...].reshape(shape)
    link_all = links_ref[...].astype(jnp.float32)
    links = [link_all[d].reshape(2, 3, 3, rows, lanes) for d in range(4)]
    back_links = []
    for direction in range(4):
        ghost = None
        if ghost_refs[direction] is not None:
            place(ghost_scratch[direction], ghost_refs[direction][...].astype(jnp.float32), "behind", direction)
            ghost = ghost_scratch[direction][...].reshape(2, 3, 3, rows, lanes)
        back_links.append(sh.behind(direction, links[direction], ghost, True))

    for key, scratch in scratch_refs.items():
        place(scratch, halo_refs[key][...], key[0], key[1])

    def load_halo(side, direction):
        ref = scratch_refs.get((side, direction), halo_refs.get((side, direction)))
        return None if ref is None else ref[...].reshape(shape)

    def wilson_global(spinor):
        ahead_list = [sh.ahead(d, spinor, load_halo("ahead", d), True) for d in range(4)]
        behind_list = [sh.behind(d, spinor, load_halo("behind", d), True) for d in range(4)]
        return hopping(spinor, links, back_links, ahead_list, behind_list)

    if first:
        residue = source
        current = None
    else:
        current = spinor_ref[...].reshape(shape)
        residue = source - wilson_global(current)
    if residual_only:
        out_ref[...] = residue.reshape(out_ref.shape)
        return

    labels = labels_ref[...]
    ahead_masks = [(sh.ahead(d, labels, None) == labels).astype(jnp.float32) for d in range(4)]
    behind_masks = [(sh.behind(d, labels, None) == labels).astype(jnp.float32) for d in range(4)]
    member = member_ref[...]

    def wilson_block(spinor):
        ahead_list = [sh.ahead(d, spinor, None) * ahead_masks[d] for d in range(4)]
        behind_list = [sh.behind(d, spinor, None) * behind_masks[d] for d in range(4)]
        return hopping(spinor, links, back_links, ahead_list, behind_list)

    def block_total(values):
        return jnp.sum(jnp.sum(member * values[None], axis=2, keepdims=True), axis=1, keepdims=True)

    update = None
    remainder = residue
    for repeat in range(MR_STEPS):
        image = wilson_block(remainder)
        image_flat = image.reshape(2, 12, rows, lanes)
        rest_flat = remainder.reshape(2, 12, rows, lanes)
        dot_real = jnp.sum(image_flat[0] * rest_flat[0] + image_flat[1] * rest_flat[1], axis=0)
        dot_imag = jnp.sum(image_flat[0] * rest_flat[1] - image_flat[1] * rest_flat[0], axis=0)
        norm = jnp.sum(image_flat[0] * image_flat[0] + image_flat[1] * image_flat[1], axis=0)
        denominator = block_total(norm) + 1e-06
        factor_real = jnp.sum(member * (block_total(dot_real) / denominator), axis=0)
        factor_imag = jnp.sum(member * (block_total(dot_imag) / denominator), axis=0)
        step = complex_scale(factor_real, factor_imag, remainder)
        update = step if update is None else update + step
        remainder = remainder - complex_scale(factor_real, factor_imag, image)
    update = update * cmask_ref[...]
    result = update if current is None else current + update
    out_ref[...] = result.reshape(out_ref.shape)
    for name, face_ref in face_refs.items():
        if name == "y_low":
            face_ref[...] = out_ref[:, :, pl.ds(0, lanes // 2)]
        elif name == "y_high":
            face_ref[...] = pltpu.roll(out_ref[...], lanes // 2, 2)[:, :, : lanes // 2]
        else:
            start, stride = face_rows(name)
            face_ref[...] = out_ref[:, pl.ds(start, 4, stride=stride), :]


def run_pass(source, links, ghosts, labels, member, cmask, spinor, halos, residual_only=False, faces=()):
    first = spinor is None
    if first:
        ghosts = [None, None, None, None]
    present = {
        "ghost": [g is not None for g in ghosts],
        "ahead": [h is not None for h in halos["ahead"]] if not first else [False] * 4,
        "behind": [h is not None for h in halos["behind"]] if not first else [False] * 4,
    }
    operands = [source, links] + [g for g in ghosts[1:] if g is not None] + [labels, member]
    if not residual_only:
        operands.append(cmask)
    if not first:
        operands.append(spinor)
        for direction in (1, 2, 3):
            for side in ("ahead", "behind"):
                if present[side][direction]:
                    operands.append(halos[side][direction])
    kernel = functools.partial(
        pass_kernel, first=first, residual_only=residual_only, present=present, faces=faces
    )
    def face_shape(name):
        if name.startswith("y"):
            return (source.shape[0], source.shape[1], source.shape[2] // 2)
        return (source.shape[0], 4, source.shape[2])

    out_shape = [jax.ShapeDtypeStruct(source.shape, jnp.float32)]
    out_shape += [jax.ShapeDtypeStruct(face_shape(name), jnp.float32) for name in faces]
    scratch = [pltpu.VMEM(source.shape, jnp.float32) for k in HALO_KEYS if present[k[0]][k[1]]]
    scratch += [pltpu.VMEM(links.shape[1:], jnp.float32) for d in (1, 2, 3) if present["ghost"][d]]
    results = pl.pallas_call(kernel, out_shape=out_shape, scratch_shapes=scratch)(*operands)
    return results[0], dict(zip(faces, results[1:]))


def coarse_kernel(*refs, present):
    refs = list(refs)
    out_ref = refs.pop()
    source_ref, inverse_ref = refs[0], refs[1]
    first = len(refs) == 2
    width = source_ref.shape[-1]
    chunks = width // 128
    lane = lax.broadcasted_iota(jnp.int32, (1, width), 1)
    position = lane % AGG
    selector = (
        lax.broadcasted_iota(jnp.int32, (8, 128), 1) // AGG == lax.broadcasted_iota(jnp.int32, (8, 128), 0)
    ).astype(jnp.float32)

    def reduce_flat(product):
        partial = product[:, 0:128]
        for q in range(1, chunks):
            partial = partial + product[:, q * 128:(q + 1) * 128]
        for shift in (64, 32, 16):
            partial = partial + pltpu.roll(partial, shift, 1)
        pieces = [
            jnp.sum(partial[8 * q:8 * q + 8] * selector, axis=0, keepdims=True) for q in range(chunks)
        ]
        return jnp.concatenate(pieces, axis=1)

    def roll_within(vector, shift):
        pieces = [pltpu.roll(vector[:, q * 128:(q + 1) * 128], shift % 128, 1) for q in range(chunks)]
        return jnp.concatenate(pieces, axis=1)

    def accumulate(acc, blocks_ref, index, vector):
        block_real = blocks_ref[index + (0,)].astype(jnp.float32)
        block_imag = blocks_ref[index + (1,)].astype(jnp.float32)
        real_part = block_real * vector[0] - block_imag * vector[1]
        imag_part = block_real * vector[1] + block_imag * vector[0]
        if acc is None:
            return [real_part, imag_part]
        return [acc[0] + real_part, acc[1] + imag_part]

    def precondition(vector):
        acc = accumulate(None, inverse_ref, (), vector)
        return [reduce_flat(acc[0]), reduce_flat(acc[1])]

    source = [source_ref[0], source_ref[1]]
    if first:
        result = precondition(source)
    else:
        operator_ref, current_ref = refs[2], refs[3]
        nearby_refs = refs[4:]
        current = [current_ref[0], current_ref[1]]
        ahead = [
            jnp.where(position == AGG - 1, roll_within(c, AGG - 1), roll_within(c, -1)) for c in current
        ]
        behind = [jnp.where(position == 0, roll_within(c, 1 - AGG), roll_within(c, 1)) for c in current]
        vectors = [current, ahead, behind]
        taken = 0
        for flag in present:
            if flag:
                vectors.append([nearby_refs[taken][0], nearby_refs[taken][1]])
                taken += 1
            else:
                vectors.append(None)
        acc = None
        for direction, vector in enumerate(vectors):
            if vector is not None:
                acc = accumulate(acc, operator_ref, (direction,), vector)
        residue = [source[0] - reduce_flat(acc[0]), source[1] - reduce_flat(acc[1])]
        step = precondition(residue)
        result = [current[0] + step[0], current[1] + step[1]]
    out_ref[0] = result[0]
    out_ref[1] = result[1]


def run_coarse(source, inverse_blocks, operator_blocks, current, nearby):
    operands = [source, inverse_blocks]
    present = ()
    if current is not None:
        present = tuple(v is not None for v in nearby)
        operands += [operator_blocks, current] + [v for v in nearby if v is not None]
    kernel = functools.partial(coarse_kernel, present=present)
    return pl.pallas_call(kernel, out_shape=jax.ShapeDtypeStruct(source.shape, jnp.float32))(*operands)


def body(
    fine_source, links, test_vectors, aggregate_map, colouring, coarse_operator, block_inverse
):
    time_extent = fine_source.shape[2]
    plane_extent = fine_source.shape[3]
    line_extent = fine_source.shape[4]
    rows = time_extent * plane_extent
    site_count = rows * line_extent
    domain_index = lax.axis_index("lat")
    domain_count = lax.axis_size("lat")
    plane_position = (domain_index + 2) % PZ
    upper_valid = plane_position < PZ - 1
    lower_valid = plane_position > 0
    later_valid = domain_index < domain_count - PZ
    earlier_valid = domain_index >= PZ

    source = fine_source.reshape(24, rows, line_extent)
    link_rows = links.reshape(4, 18, rows, line_extent)
    label_rows = aggregate_map.reshape(rows, line_extent)
    member = (label_rows[None] == jnp.arange(AGG, dtype=jnp.int32)[:, None, None]).astype(jnp.float32)
    colour_list = colouring.reshape(AGG)
    colour_masks = [
        jnp.sum(member * (colour_list == k).astype(jnp.float32)[:, None, None], axis=0) for k in range(2)
    ]
    labels = (label_rows + 1).astype(jnp.float32)

    def z_up_ok(i):
        return (i + 2) % PZ != PZ - 1

    def z_down_ok(i):
        return (i + 2) % PZ != 0

    def t_up_ok(i):
        return i + PZ < domain_count

    def t_down_ok(i):
        return i - PZ >= 0

    half = line_extent // 2
    ghosts = [
        None,
        permute_from(link_rows[1][..., half:], "grp", -1, lambda i: True),
        permute_from(lax.slice_in_dim(link_rows[2], 3, 16, 4, axis=1), "lat", -1, z_down_ok),
        permute_from(lax.slice_in_dim(link_rows[3], 12, 16, 1, axis=1), "lat", -PZ, t_down_ok),
    ]

    needed = ["y_low", "y_high"] + [
        name for name, ok in zip(FACES[2:], (z_up_ok, z_down_ok, t_up_ok, t_down_ok))
        if any(ok(i) for i in range(domain_count))
    ]

    def faces_of(spinor):
        result = {"y_low": spinor[..., :half], "y_high": spinor[..., half:]}
        for name in needed[2:]:
            start, stride = face_rows(name)
            result[name] = lax.slice_in_dim(spinor, start, start + 3 * stride + 1, stride, axis=1)
        return result

    def halos_of(spinor, faces):
        def face(name):
            return faces[name] if name in faces else None

        return {
            "ahead": [
                None,
                permute_from(faces["y_low"], "grp", 1, lambda i: True),
                permute_from(face("z_low"), "lat", 1, z_up_ok) if face("z_low") is not None else None,
                permute_from(face("t_low"), "lat", PZ, t_up_ok) if face("t_low") is not None else None,
            ],
            "behind": [
                None,
                permute_from(faces["y_high"], "grp", -1, lambda i: True),
                permute_from(face("z_high"), "lat", -1, z_down_ok) if face("z_high") is not None else None,
                permute_from(face("t_high"), "lat", -PZ, t_down_ok) if face("t_high") is not None else None,
            ],
        }

    def smoother_pass(spinor, faces, colour_pass, out_faces):
        halos = None if spinor is None else halos_of(spinor, faces)
        return run_pass(
            source, link_rows, ghosts, labels, member, colour_masks[colour_pass], spinor, halos,
            faces=out_faces,
        )

    def sweep(start, faces, last_faces):
        current, current_faces = smoother_pass(start, faces, 0, tuple(needed))
        return smoother_pass(current, current_faces, 1, last_faces)

    smoothed, smoothed_faces = sweep(None, None, tuple(needed))
    residue, _ = run_pass(
        source, link_rows, ghosts, labels, member, None, smoothed, halos_of(smoothed, smoothed_faces),
        residual_only=True,
    )
    residual = residue.astype(jnp.bfloat16)
    membership = member.reshape(AGG, site_count).T
    member_weights = membership.astype(jnp.bfloat16)
    weighted = residual.reshape(2, 2, 6, site_count)[..., None] * member_weights
    vectors = test_vectors.reshape(NVEC, 2, 2, 6, site_count)

    def contract(left, right):
        return jnp.einsum("kxqn,xqnj->xkj", left, right, preferred_element_type=jnp.float32)

    real_part = contract(vectors[:, 0], weighted[0]) + contract(vectors[:, 1], weighted[1])
    imag_part = contract(vectors[:, 0], weighted[1]) - contract(vectors[:, 1], weighted[0])
    coarse_source = jnp.stack([real_part, imag_part]).reshape(2, CDOF, AGG)
    flat_source = coarse_source.reshape(2, 1, CDOF * AGG)
    operator_blocks = coarse_operator.reshape(9, 2, CDOF, CDOF * AGG)
    inverse_blocks = block_inverse.reshape(2, CDOF, CDOF * AGG)
    correction = run_coarse(flat_source, inverse_blocks, operator_blocks, None, None)
    for repeat in range(2):
        nearby = [
            permute_from(correction, "grp", 1, lambda i: True),
            permute_from(correction, "grp", -1, lambda i: True),
            permute_from(correction, "lat", 1, z_up_ok),
            permute_from(correction, "lat", -1, z_down_ok),
            permute_from(correction, "lat", PZ, t_up_ok),
            permute_from(correction, "lat", -PZ, t_down_ok),
        ]
        correction = run_coarse(flat_source, inverse_blocks, operator_blocks, correction, nearby)
    correction = correction.reshape(2, CDOF, AGG)
    expanded = jnp.dot(
        correction.reshape(2 * CDOF, AGG), membership.T, precision=lax.Precision.HIGHEST
    ).reshape(2, 2, NVEC, site_count)
    spread_real = jnp.swapaxes(expanded[0], 0, 1)[:, :, None]
    spread_imag = jnp.swapaxes(expanded[1], 0, 1)[:, :, None]
    real_part = jnp.sum(vectors[:, 0] * spread_real - vectors[:, 1] * spread_imag, axis=0)
    imag_part = jnp.sum(vectors[:, 0] * spread_imag + vectors[:, 1] * spread_real, axis=0)
    corrected = smoothed + jnp.stack([real_part, imag_part]).reshape(24, rows, line_extent)
    solution, _ = sweep(corrected, faces_of(corrected), ())
    return (
        solution.reshape(1, 24, time_extent, plane_extent, line_extent),
        correction.reshape(1, 1, 2, CDOF, AGG),
    )


def solution(mesh):
    return jax.shard_map(
        body,
        mesh=mesh,
        in_specs=(
            P("lat", None, None, None, "grp"),
            P("lat", None, None, None, None, "grp"),
            P("lat", None, None, None, None, "grp"),
            P("lat", None, None, "grp", None),
            P("lat", "grp", None),
            P("lat", "grp", None, None, None, None),
            P("lat", "grp", None, None, None),
        ),
        out_specs=(P("lat", None, None, None, "grp"), P("lat", "grp", None, None, None)),
        check_vma=False,
    )
```

```python
import functools

import jax
import jax.numpy as jnp
from jax import lax
from jax.experimental import pallas as pl
from jax.experimental.pallas import tpu as pltpu
from jax.sharding import PartitionSpec as P

CX = 64
PZ = 8
NVEC = 24
AGG = 16
MR_STEPS = 2
CDOF = 48


def passed_along(shard, axis, by):
    size = lax.axis_size(axis)
    return lax.ppermute(shard, axis, [(i, (i + by) % size) for i in range(size)])


def padded_2(shard, sides, width):
    for axis, dim in sides:
        size, length = (lax.axis_size(axis), shard.shape[dim])
        up = [(i, (i + 1) % size) for i in range(size)]
        down = [(j, i) for i, j in up]
        last = lax.slice_in_dim(shard, length - width, length, axis=dim)
        first = lax.slice_in_dim(shard, 0, width, axis=dim)
        before = lax.ppermute(last, axis, up)
        after = lax.ppermute(first, axis, down)
        shard = jnp.concatenate([before, shard, after], axis=dim)
    return shard


def times_minus_i(values):
    return jnp.stack([values[1], -values[0]])


def times_plus_i(values):
    return jnp.stack([-values[1], values[0]])


def spin_factor(direction, spin_pair):
    if direction == 0:
        return jnp.stack([times_minus_i(spin_pair[:, 1]), times_minus_i(spin_pair[:, 0])], axis=1)
    if direction == 1:
        return jnp.stack([-spin_pair[:, 1], spin_pair[:, 0]], axis=1)
    if direction == 2:
        return jnp.stack([times_minus_i(spin_pair[:, 0]), times_plus_i(spin_pair[:, 1])], axis=1)
    return spin_pair


def project_minus(direction, spinor):
    return spinor[:, :2] - spin_factor(direction, spinor[:, 2:])


def project_plus(direction, spinor):
    return spinor[:, :2] + spin_factor(direction, spinor[:, 2:])


def rebuild_minus(direction, half_spinor):
    lower_part = spin_factor(direction, half_spinor) if direction < 3 else -half_spinor
    return jnp.concatenate([half_spinor, lower_part], axis=1)


def rebuild_plus(direction, half_spinor):
    lower_part = -spin_factor(direction, half_spinor) if direction < 3 else half_spinor
    return jnp.concatenate([half_spinor, lower_part], axis=1)


def colour_product(gauge_link, half_spinor, adjoint):
    link_real = gauge_link[0]
    link_imag = gauge_link[1]
    if adjoint:
        link_real = jnp.swapaxes(link_real, 0, 1)
        link_imag = -jnp.swapaxes(link_imag, 0, 1)
    spin_real = half_spinor[0][:, None]
    spin_imag = half_spinor[1][:, None]
    real_part = jnp.sum(link_real[None] * spin_real - link_imag[None] * spin_imag, axis=2)
    imag_part = jnp.sum(link_real[None] * spin_imag + link_imag[None] * spin_real, axis=2)
    return jnp.stack([real_part, imag_part])


def complex_scale(factor_real, factor_imag, lattice):
    return jnp.stack(
        [
            factor_real * lattice[0] - factor_imag * lattice[1],
            factor_real * lattice[1] + factor_imag * lattice[0],
        ]
    )


def apply_blocks(blocks, nearby):
    matrices = blocks.reshape(blocks.shape[0], 2, CDOF, CDOF, AGG)
    vector_real = nearby[:, 0][:, None]
    vector_imag = nearby[:, 1][:, None]
    real_part = jnp.sum(matrices[:, 0] * vector_real - matrices[:, 1] * vector_imag, axis=(0, 2))
    imag_part = jnp.sum(matrices[:, 0] * vector_imag + matrices[:, 1] * vector_real, axis=(0, 2))
    return jnp.stack([real_part, imag_part])


def keep_if(allowed, values):
    return jnp.where(allowed, values, jnp.zeros_like(values))


def permute_from(value, axis, offset, allowed):
    size = lax.axis_size(axis)
    pairs = [((i + offset) % size, i) for i in range(size) if allowed(i)]
    if not pairs:
        return None
    return lax.ppermute(value, axis, pairs)


class Shifts:
    def __init__(self, rows, lanes):
        self.rows = rows
        self.lanes = lanes
        self.lane = lax.broadcasted_iota(jnp.int32, (rows, lanes), 1)
        self.row = lax.broadcasted_iota(jnp.int32, (rows, lanes), 0)
        self.xpos = self.lane % CX
        self.zpos = self.row % 4

    def roll(self, a, shift, axis):
        n = a.shape[axis]
        return pltpu.roll(a, shift % n, a.ndim + axis)

    def ahead(self, direction, a, nbr, placed=False):
        if direction == 0:
            return jnp.where(self.xpos == CX - 1, self.roll(a, CX - 1, -1), self.roll(a, -1, -1))
        if direction == 1:
            half = self.lanes // 2
            if placed and nbr is not None:
                return jnp.where(self.lane >= half, self.roll(nbr, half, -1), self.roll(a, half, -1))
            filled = jnp.where(self.lane < half, 0.0 if nbr is None else nbr, a)
            return self.roll(filled, half, -1)
        if direction == 2:
            inner = self.roll(a, -1, -2)
            outer = 0.0 if nbr is None else (nbr if placed else self.roll(nbr, 3, -2))
            return jnp.where(self.zpos == 3, outer, inner)
        filled = jnp.where(self.row < 4, 0.0 if nbr is None else nbr, a)
        return self.roll(filled, -4, -2)

    def behind(self, direction, a, nbr, placed=False):
        if direction == 0:
            return jnp.where(self.xpos == 0, self.roll(a, 1 - CX, -1), self.roll(a, 1, -1))
        if direction == 1:
            half = self.lanes // 2
            if placed and nbr is not None:
                return jnp.where(self.lane < half, nbr, self.roll(a, half, -1))
            filled = jnp.where(self.lane >= half, 0.0 if nbr is None else nbr, a)
            return self.roll(filled, half, -1)
        if direction == 2:
            inner = self.roll(a, 1, -2)
            outer = 0.0 if nbr is None else (nbr if placed else self.roll(nbr, -3, -2))
            return jnp.where(self.zpos == 0, outer, inner)
        filled = jnp.where(self.row >= self.rows - 4, 0.0 if nbr is None else nbr, a)
        return self.roll(filled, 4, -2)


def hopping(spinor, links, back_links, ahead_list, behind_list):
    hop_total = None
    for direction in range(4):
        ahead_half = colour_product(links[direction], project_minus(direction, ahead_list[direction]), False)
        behind_half = colour_product(back_links[direction], project_plus(direction, behind_list[direction]), True)
        term = rebuild_minus(direction, ahead_half) + rebuild_plus(direction, behind_half)
        hop_total = term if hop_total is None else hop_total + term
    return 4.5 * spinor - 0.5 * hop_total


FACES = ("y_low", "y_high", "z_low", "z_high", "t_low", "t_high")
HALO_KEYS = tuple((side, d) for d in (1, 2, 3) for side in ("ahead", "behind"))


def face_rows(name):
    return {"z_low": (0, 4), "z_high": (3, 4), "t_low": (0, 1), "t_high": (12, 1)}[name]


def place(scratch, value, side, direction):
    if direction == 1:
        scratch[..., pl.ds(0, value.shape[-1])] = value
        return
    start, stride = {("ahead", 2): (3, 4), ("behind", 2): (0, 4), ("ahead", 3): (0, 1), ("behind", 3): (12, 1)}[
        (side, direction)
    ]
    scratch[:, pl.ds(start, 4, stride=stride), :] = value


def pass_kernel(*refs, first, residual_only, present, faces, link_mode, append_links, emit_back):
    refs = list(refs)
    width = 24
    ghost_dirs = [d for d in (1, 2, 3) if link_mode == "combined" and present["behind"][d]]
    link_face_scratch = refs.pop() if append_links and "z_high" in faces else None
    ghost_scratch = {}
    for direction in reversed(ghost_dirs):
        ghost_scratch[direction] = refs.pop()
    scratch_refs = {}
    for key in reversed([k for k in HALO_KEYS if present[k[0]][k[1]]]):
        scratch_refs[key] = refs.pop()
    back_out_ref = refs.pop() if emit_back else None
    face_refs = {}
    for name in reversed(faces):
        face_refs[name] = refs.pop()
    out_ref = refs.pop()

    def take():
        return refs.pop(0)

    src_ref = take()
    links_ref = take()
    back_ref = take() if link_mode == "given" else None
    labels_ref = take()
    member_ref = take()
    cmask_ref = None if residual_only else take()
    spinor_ref = None
    halo_refs = {}
    if not first:
        spinor_ref = take()
        for key in HALO_KEYS:
            if present[key[0]][key[1]]:
                halo_refs[key] = take()

    rows, lanes = src_ref.shape[-2], src_ref.shape[-1]
    sh = Shifts(rows, lanes)
    shape = (2, 4, 3, rows, lanes)
    source = src_ref[...].reshape(shape)
    link_all = links_ref[...].astype(jnp.float32)
    links = [link_all[d].reshape(2, 3, 3, rows, lanes) for d in range(4)]
    if back_ref is not None:
        back_all = back_ref[...].astype(jnp.float32)
        back_links = [back_all[d].reshape(2, 3, 3, rows, lanes) for d in range(4)]
    else:
        back_links = []
        for direction in range(4):
            ghost = None
            if direction in ghost_scratch:
                halo = halo_refs[("behind", direction)]
                place(ghost_scratch[direction], halo[width:], "behind", direction)
                ghost = ghost_scratch[direction][...].reshape(2, 3, 3, rows, lanes)
            back_links.append(sh.behind(direction, links[direction], ghost, True))
    if back_out_ref is not None:
        for direction in range(4):
            back_out_ref[direction] = back_links[direction].reshape(18, rows, lanes).astype(back_out_ref.dtype)

    for key, scratch in scratch_refs.items():
        halo = halo_refs[key]
        value = halo[:width] if (key[0] == "behind" and key[1] in ghost_scratch) else halo[...]
        place(scratch, value, key[0], key[1])

    def load_halo(side, direction):
        ref = scratch_refs.get((side, direction), halo_refs.get((side, direction)))
        return None if ref is None else ref[...].reshape(shape)

    def wilson_global(spinor):
        ahead_list = [sh.ahead(d, spinor, load_halo("ahead", d), True) for d in range(4)]
        behind_list = [sh.behind(d, spinor, load_halo("behind", d), True) for d in range(4)]
        return hopping(spinor, links, back_links, ahead_list, behind_list)

    if first:
        residue = source
        current = None
    else:
        current = spinor_ref[...].reshape(shape)
        residue = source - wilson_global(current)
    if residual_only:
        out_ref[...] = residue.reshape(out_ref.shape)
        return

    labels = labels_ref[...]
    ahead_masks = [(sh.ahead(d, labels, None) == labels).astype(jnp.float32) for d in range(4)]
    behind_masks = [(sh.behind(d, labels, None) == labels).astype(jnp.float32) for d in range(4)]
    member = member_ref[...]

    def wilson_block(spinor):
        ahead_list = [sh.ahead(d, spinor, None) * ahead_masks[d] for d in range(4)]
        behind_list = [sh.behind(d, spinor, None) * behind_masks[d] for d in range(4)]
        return hopping(spinor, links, back_links, ahead_list, behind_list)

    def block_total(values):
        return jnp.sum(jnp.sum(member * values[None], axis=2, keepdims=True), axis=1, keepdims=True)

    update = None
    remainder = residue
    for repeat in range(MR_STEPS):
        image = wilson_block(remainder)
        image_flat = image.reshape(2, 12, rows, lanes)
        rest_flat = remainder.reshape(2, 12, rows, lanes)
        dot_real = jnp.sum(image_flat[0] * rest_flat[0] + image_flat[1] * rest_flat[1], axis=0)
        dot_imag = jnp.sum(image_flat[0] * rest_flat[1] - image_flat[1] * rest_flat[0], axis=0)
        norm = jnp.sum(image_flat[0] * image_flat[0] + image_flat[1] * image_flat[1], axis=0)
        denominator = block_total(norm) + 1e-06
        factor_real = jnp.sum(member * (block_total(dot_real) / denominator), axis=0)
        factor_imag = jnp.sum(member * (block_total(dot_imag) / denominator), axis=0)
        step = complex_scale(factor_real, factor_imag, remainder)
        update = step if update is None else update + step
        remainder = remainder - complex_scale(factor_real, factor_imag, image)
    update = update * cmask_ref[...]
    result = update if current is None else current + update
    out_ref[...] = result.reshape(out_ref.shape)
    if link_face_scratch is not None:
        link_face_scratch[...] = link_all[2]
    for name, face_ref in face_refs.items():
        if name == "y_low":
            face_ref[...] = out_ref[:, :, pl.ds(0, lanes // 2)]
        elif name == "y_high":
            face_ref[0:width] = pltpu.roll(out_ref[...], lanes // 2, 2)[:, :, : lanes // 2]
            if append_links:
                face_ref[width:] = pltpu.roll(link_all[1], lanes // 2, 2)[:, :, : lanes // 2]
        else:
            start, stride = face_rows(name)
            face_ref[0:width] = out_ref[:, pl.ds(start, 4, stride=stride), :]
            if append_links and name == "z_high":
                face_ref[width:] = link_face_scratch[:, pl.ds(start, 4, stride=stride), :]
            elif append_links and name == "t_high":
                face_ref[width:] = link_all[3][:, start:start + 4, :]


def run_pass(source, links, back, labels, member, cmask, spinor, halos, residual_only=False, faces=(),
             link_mode="given", append_links=False, emit_back=False):
    first = spinor is None
    present = {
        "ahead": [h is not None for h in halos["ahead"]] if not first else [False] * 4,
        "behind": [h is not None for h in halos["behind"]] if not first else [False] * 4,
    }
    operands = [source, links] + ([back] if link_mode == "given" else []) + [labels, member]
    if not residual_only:
        operands.append(cmask)
    if not first:
        operands.append(spinor)
        for key in HALO_KEYS:
            if present[key[0]][key[1]]:
                operands.append(halos[key[0]][key[1]])
    kernel = functools.partial(
        pass_kernel, first=first, residual_only=residual_only, present=present, faces=faces,
        link_mode=link_mode, append_links=append_links, emit_back=emit_back,
    )
    width = source.shape[0]

    def face_shape(name):
        rows = width + (18 if append_links and name.endswith("high") else 0)
        if name.startswith("y"):
            return (rows, source.shape[1], source.shape[2] // 2)
        return (rows, 4, source.shape[2])

    out_shape = [jax.ShapeDtypeStruct(source.shape, jnp.float32)]
    out_shape += [jax.ShapeDtypeStruct(face_shape(name), jnp.float32) for name in faces]
    if emit_back:
        out_shape.append(jax.ShapeDtypeStruct(links.shape, links.dtype))
    scratch = [pltpu.VMEM(source.shape, jnp.float32) for k in HALO_KEYS if present[k[0]][k[1]]]
    if link_mode == "combined":
        scratch += [pltpu.VMEM(links.shape[1:], jnp.float32) for d in (1, 2, 3) if present["behind"][d]]
    if append_links and "z_high" in faces:
        scratch.append(pltpu.VMEM(links.shape[1:], jnp.float32))
    results = pl.pallas_call(kernel, out_shape=out_shape, scratch_shapes=scratch)(*operands)
    face_values = dict(zip(faces, results[1:1 + len(faces)]))
    return results[0], face_values, (results[-1] if emit_back else None)


def coarse_kernel(*refs, present):
    refs = list(refs)
    out_ref = refs.pop()
    source_ref, inverse_ref = refs[0], refs[1]
    first = len(refs) == 2
    width = source_ref.shape[-1]
    chunks = width // 128
    lane = lax.broadcasted_iota(jnp.int32, (1, width), 1)
    position = lane % AGG
    selector = (
        lax.broadcasted_iota(jnp.int32, (8, 128), 1) // AGG == lax.broadcasted_iota(jnp.int32, (8, 128), 0)
    ).astype(jnp.float32)

    def reduce_flat(product):
        partial = product[:, 0:128]
        for q in range(1, chunks):
            partial = partial + product[:, q * 128:(q + 1) * 128]
        for shift in (64, 32, 16):
            partial = partial + pltpu.roll(partial, shift, 1)
        pieces = [
            jnp.sum(partial[8 * q:8 * q + 8] * selector, axis=0, keepdims=True) for q in range(chunks)
        ]
        return jnp.concatenate(pieces, axis=1)

    def roll_within(vector, shift):
        pieces = [pltpu.roll(vector[:, q * 128:(q + 1) * 128], shift % 128, 1) for q in range(chunks)]
        return jnp.concatenate(pieces, axis=1)

    def accumulate(acc, blocks_ref, index, vector):
        block_real = blocks_ref[index + (0,)].astype(jnp.float32)
        block_imag = blocks_ref[index + (1,)].astype(jnp.float32)
        real_part = block_real * vector[0] - block_imag * vector[1]
        imag_part = block_real * vector[1] + block_imag * vector[0]
        if acc is None:
            return [real_part, imag_part]
        return [acc[0] + real_part, acc[1] + imag_part]

    def precondition(vector):
        acc = accumulate(None, inverse_ref, (), vector)
        return [reduce_flat(acc[0]), reduce_flat(acc[1])]

    source = [source_ref[0], source_ref[1]]
    if first:
        result = precondition(source)
    else:
        operator_ref, current_ref = refs[2], refs[3]
        nearby_refs = refs[4:]
        current = [current_ref[0], current_ref[1]]
        ahead = [
            jnp.where(position == AGG - 1, roll_within(c, AGG - 1), roll_within(c, -1)) for c in current
        ]
        behind = [jnp.where(position == 0, roll_within(c, 1 - AGG), roll_within(c, 1)) for c in current]
        vectors = [current, ahead, behind]
        taken = 0
        for flag in present:
            if flag:
                vectors.append([nearby_refs[taken][0], nearby_refs[taken][1]])
                taken += 1
            else:
                vectors.append(None)
        acc = None
        for direction, vector in enumerate(vectors):
            if vector is not None:
                acc = accumulate(acc, operator_ref, (direction,), vector)
        residue = [source[0] - reduce_flat(acc[0]), source[1] - reduce_flat(acc[1])]
        step = precondition(residue)
        result = [current[0] + step[0], current[1] + step[1]]
    out_ref[0] = result[0]
    out_ref[1] = result[1]


def run_coarse(source, inverse_blocks, operator_blocks, current, nearby):
    operands = [source, inverse_blocks]
    present = ()
    if current is not None:
        present = tuple(v is not None for v in nearby)
        operands += [operator_blocks, current] + [v for v in nearby if v is not None]
    kernel = functools.partial(coarse_kernel, present=present)
    return pl.pallas_call(kernel, out_shape=jax.ShapeDtypeStruct(source.shape, jnp.float32))(*operands)


def body(
    fine_source, links, test_vectors, aggregate_map, colouring, coarse_operator, block_inverse
):
    time_extent = fine_source.shape[2]
    plane_extent = fine_source.shape[3]
    line_extent = fine_source.shape[4]
    rows = time_extent * plane_extent
    site_count = rows * line_extent
    domain_index = lax.axis_index("lat")
    domain_count = lax.axis_size("lat")
    plane_position = (domain_index + 2) % PZ
    upper_valid = plane_position < PZ - 1
    lower_valid = plane_position > 0
    later_valid = domain_index < domain_count - PZ
    earlier_valid = domain_index >= PZ

    source = fine_source.reshape(24, rows, line_extent)
    link_rows = links.reshape(4, 18, rows, line_extent)
    label_rows = aggregate_map.reshape(rows, line_extent)
    member = (label_rows[None] == jnp.arange(AGG, dtype=jnp.int32)[:, None, None]).astype(jnp.float32)
    colour_list = colouring.reshape(AGG)
    colour_masks = [
        jnp.sum(member * (colour_list == k).astype(jnp.float32)[:, None, None], axis=0) for k in range(2)
    ]
    labels = (label_rows + 1).astype(jnp.float32)

    def z_up_ok(i):
        return (i + 2) % PZ != PZ - 1

    def z_down_ok(i):
        return (i + 2) % PZ != 0

    def t_up_ok(i):
        return i + PZ < domain_count

    def t_down_ok(i):
        return i - PZ >= 0

    half = line_extent // 2

    needed = ["y_low", "y_high"] + [
        name for name, ok in zip(FACES[2:], (z_up_ok, z_down_ok, t_up_ok, t_down_ok))
        if any(ok(i) for i in range(domain_count))
    ]

    def faces_of(spinor):
        result = {"y_low": spinor[..., :half], "y_high": spinor[..., half:]}
        for name in needed[2:]:
            start, stride = face_rows(name)
            result[name] = lax.slice_in_dim(spinor, start, start + 3 * stride + 1, stride, axis=1)
        return result

    def halos_of(spinor, faces):
        def face(name):
            return faces[name] if name in faces else None

        return {
            "ahead": [
                None,
                permute_from(faces["y_low"], "grp", 1, lambda i: True),
                permute_from(face("z_low"), "lat", 1, z_up_ok) if face("z_low") is not None else None,
                permute_from(face("t_low"), "lat", PZ, t_up_ok) if face("t_low") is not None else None,
            ],
            "behind": [
                None,
                permute_from(faces["y_high"], "grp", -1, lambda i: True),
                permute_from(face("z_high"), "lat", -1, z_down_ok) if face("z_high") is not None else None,
                permute_from(face("t_high"), "lat", -PZ, t_down_ok) if face("t_high") is not None else None,
            ],
        }

    smoothed_first, first_faces, _ = run_pass(
        source, link_rows, None, labels, member, colour_masks[0], None, None,
        faces=tuple(needed), link_mode="none", append_links=True,
    )
    smoothed, smoothed_faces, back_rows = run_pass(
        source, link_rows, None, labels, member, colour_masks[1], smoothed_first,
        halos_of(smoothed_first, first_faces), faces=tuple(needed), link_mode="combined", emit_back=True,
    )

    def sweep(start, faces):
        current, current_faces, _ = run_pass(
            source, link_rows, back_rows, labels, member, colour_masks[0], start, halos_of(start, faces),
            faces=tuple(needed),
        )
        result, _, _ = run_pass(
            source, link_rows, back_rows, labels, member, colour_masks[1], current,
            halos_of(current, current_faces),
        )
        return result

    residue, _, _ = run_pass(
        source, link_rows, back_rows, labels, member, None, smoothed, halos_of(smoothed, smoothed_faces),
        residual_only=True,
    )
    residual = residue.astype(jnp.bfloat16)
    membership = member.reshape(AGG, site_count).T
    member_weights = membership.astype(jnp.bfloat16)
    weighted = residual.reshape(2, 2, 6, site_count)[..., None] * member_weights
    vectors = test_vectors.reshape(NVEC, 2, 2, 6, site_count)

    def contract(left, right):
        return jnp.einsum("kxqn,xqnj->xkj", left, right, preferred_element_type=jnp.float32)

    real_part = contract(vectors[:, 0], weighted[0]) + contract(vectors[:, 1], weighted[1])
    imag_part = contract(vectors[:, 0], weighted[1]) - contract(vectors[:, 1], weighted[0])
    coarse_source = jnp.stack([real_part, imag_part]).reshape(2, CDOF, AGG)
    flat_source = coarse_source.reshape(2, 1, CDOF * AGG)
    operator_blocks = coarse_operator.reshape(9, 2, CDOF, CDOF * AGG)
    inverse_blocks = block_inverse.reshape(2, CDOF, CDOF * AGG)
    correction = run_coarse(flat_source, inverse_blocks, operator_blocks, None, None)
    for repeat in range(2):
        nearby = [
            permute_from(correction, "grp", 1, lambda i: True),
            permute_from(correction, "grp", -1, lambda i: True),
            permute_from(correction, "lat", 1, z_up_ok),
            permute_from(correction, "lat", -1, z_down_ok),
            permute_from(correction, "lat", PZ, t_up_ok),
            permute_from(correction, "lat", -PZ, t_down_ok),
        ]
        correction = run_coarse(flat_source, inverse_blocks, operator_blocks, correction, nearby)
    correction = correction.reshape(2, CDOF, AGG)
    expanded = jnp.dot(
        correction.reshape(2 * CDOF, AGG), membership.T, precision=lax.Precision.HIGHEST
    ).reshape(2, 2, NVEC, site_count)
    spread_real = jnp.swapaxes(expanded[0], 0, 1)[:, :, None]
    spread_imag = jnp.swapaxes(expanded[1], 0, 1)[:, :, None]
    real_part = jnp.sum(vectors[:, 0] * spread_real - vectors[:, 1] * spread_imag, axis=0)
    imag_part = jnp.sum(vectors[:, 0] * spread_imag + vectors[:, 1] * spread_real, axis=0)
    corrected = smoothed + jnp.stack([real_part, imag_part]).reshape(24, rows, line_extent)
    solution = sweep(corrected, faces_of(corrected))
    return (
        solution.reshape(1, 24, time_extent, plane_extent, line_extent),
        correction.reshape(1, 1, 2, CDOF, AGG),
    )


def solution(mesh):
    return jax.shard_map(
        body,
        mesh=mesh,
        in_specs=(
            P("lat", None, None, None, "grp"),
            P("lat", None, None, None, None, "grp"),
            P("lat", None, None, None, None, "grp"),
            P("lat", None, None, "grp", None),
            P("lat", "grp", None),
            P("lat", "grp", None, None, None, None),
            P("lat", "grp", None, None, None),
        ),
        out_specs=(P("lat", None, None, None, "grp"), P("lat", "grp", None, None, None)),
        check_vma=False,
    )
```

```python
import functools

import jax
import jax.numpy as jnp
from jax import lax
from jax.experimental import pallas as pl
from jax.experimental.pallas import tpu as pltpu
from jax.sharding import PartitionSpec as P

CX = 64
PZ = 8
NVEC = 24
AGG = 16
MR_STEPS = 2
CDOF = 48


def passed_along(shard, axis, by):
    size = lax.axis_size(axis)
    return lax.ppermute(shard, axis, [(i, (i + by) % size) for i in range(size)])


def padded_2(shard, sides, width):
    for axis, dim in sides:
        size, length = (lax.axis_size(axis), shard.shape[dim])
        up = [(i, (i + 1) % size) for i in range(size)]
        down = [(j, i) for i, j in up]
        last = lax.slice_in_dim(shard, length - width, length, axis=dim)
        first = lax.slice_in_dim(shard, 0, width, axis=dim)
        before = lax.ppermute(last, axis, up)
        after = lax.ppermute(first, axis, down)
        shard = jnp.concatenate([before, shard, after], axis=dim)
    return shard


def times_minus_i(values):
    return jnp.stack([values[1], -values[0]])


def times_plus_i(values):
    return jnp.stack([-values[1], values[0]])


def spin_factor(direction, spin_pair):
    if direction == 0:
        return jnp.stack([times_minus_i(spin_pair[:, 1]), times_minus_i(spin_pair[:, 0])], axis=1)
    if direction == 1:
        return jnp.stack([-spin_pair[:, 1], spin_pair[:, 0]], axis=1)
    if direction == 2:
        return jnp.stack([times_minus_i(spin_pair[:, 0]), times_plus_i(spin_pair[:, 1])], axis=1)
    return spin_pair


def project_minus(direction, spinor):
    return spinor[:, :2] - spin_factor(direction, spinor[:, 2:])


def project_plus(direction, spinor):
    return spinor[:, :2] + spin_factor(direction, spinor[:, 2:])


def rebuild_minus(direction, half_spinor):
    lower_part = spin_factor(direction, half_spinor) if direction < 3 else -half_spinor
    return jnp.concatenate([half_spinor, lower_part], axis=1)


def rebuild_plus(direction, half_spinor):
    lower_part = -spin_factor(direction, half_spinor) if direction < 3 else half_spinor
    return jnp.concatenate([half_spinor, lower_part], axis=1)


def colour_product(gauge_link, half_spinor, adjoint):
    link_real = gauge_link[0]
    link_imag = gauge_link[1]
    if adjoint:
        link_real = jnp.swapaxes(link_real, 0, 1)
        link_imag = -jnp.swapaxes(link_imag, 0, 1)
    spin_real = half_spinor[0][:, None]
    spin_imag = half_spinor[1][:, None]
    real_part = jnp.sum(link_real[None] * spin_real - link_imag[None] * spin_imag, axis=2)
    imag_part = jnp.sum(link_real[None] * spin_imag + link_imag[None] * spin_real, axis=2)
    return jnp.stack([real_part, imag_part])


def complex_scale(factor_real, factor_imag, lattice):
    return jnp.stack(
        [
            factor_real * lattice[0] - factor_imag * lattice[1],
            factor_real * lattice[1] + factor_imag * lattice[0],
        ]
    )


def apply_blocks(blocks, nearby):
    matrices = blocks.reshape(blocks.shape[0], 2, CDOF, CDOF, AGG)
    vector_real = nearby[:, 0][:, None]
    vector_imag = nearby[:, 1][:, None]
    real_part = jnp.sum(matrices[:, 0] * vector_real - matrices[:, 1] * vector_imag, axis=(0, 2))
    imag_part = jnp.sum(matrices[:, 0] * vector_imag + matrices[:, 1] * vector_real, axis=(0, 2))
    return jnp.stack([real_part, imag_part])


def keep_if(allowed, values):
    return jnp.where(allowed, values, jnp.zeros_like(values))


def permute_from(value, axis, offset, allowed):
    size = lax.axis_size(axis)
    pairs = [((i + offset) % size, i) for i in range(size) if allowed(i)]
    if not pairs:
        return None
    return lax.ppermute(value, axis, pairs)


class Shifts:
    def __init__(self, rows, lanes):
        self.rows = rows
        self.lanes = lanes
        self.lane = lax.broadcasted_iota(jnp.int32, (rows, lanes), 1)
        self.row = lax.broadcasted_iota(jnp.int32, (rows, lanes), 0)
        self.xpos = self.lane % CX
        self.zpos = self.row % 4

    def roll(self, a, shift, axis):
        n = a.shape[axis]
        return pltpu.roll(a, shift % n, a.ndim + axis)

    def ahead(self, direction, a, nbr, placed=False):
        if direction == 0:
            return jnp.where(self.xpos == CX - 1, self.roll(a, CX - 1, -1), self.roll(a, -1, -1))
        if direction == 1:
            half = self.lanes // 2
            if placed and nbr is not None:
                return jnp.where(self.lane >= half, self.roll(nbr, half, -1), self.roll(a, half, -1))
            filled = jnp.where(self.lane < half, 0.0 if nbr is None else nbr, a)
            return self.roll(filled, half, -1)
        if direction == 2:
            inner = self.roll(a, -1, -2)
            outer = 0.0 if nbr is None else (nbr if placed else self.roll(nbr, 3, -2))
            return jnp.where(self.zpos == 3, outer, inner)
        filled = jnp.where(self.row < 4, 0.0 if nbr is None else nbr, a)
        return self.roll(filled, -4, -2)

    def behind(self, direction, a, nbr, placed=False):
        if direction == 0:
            return jnp.where(self.xpos == 0, self.roll(a, 1 - CX, -1), self.roll(a, 1, -1))
        if direction == 1:
            half = self.lanes // 2
            if placed and nbr is not None:
                return jnp.where(self.lane < half, nbr, self.roll(a, half, -1))
            filled = jnp.where(self.lane >= half, 0.0 if nbr is None else nbr, a)
            return self.roll(filled, half, -1)
        if direction == 2:
            inner = self.roll(a, 1, -2)
            outer = 0.0 if nbr is None else (nbr if placed else self.roll(nbr, -3, -2))
            return jnp.where(self.zpos == 0, outer, inner)
        filled = jnp.where(self.row >= self.rows - 4, 0.0 if nbr is None else nbr, a)
        return self.roll(filled, 4, -2)


def hopping(spinor, links, back_links, ahead_list, behind_list):
    hop_total = None
    for direction in range(4):
        ahead_half = colour_product(links[direction], project_minus(direction, ahead_list[direction]), False)
        behind_half = colour_product(back_links[direction], project_plus(direction, behind_list[direction]), True)
        term = rebuild_minus(direction, ahead_half) + rebuild_plus(direction, behind_half)
        hop_total = term if hop_total is None else hop_total + term
    return 4.5 * spinor - 0.5 * hop_total


FACES = ("y_low", "y_high", "z_low", "z_high", "t_low", "t_high")
HALO_KEYS = tuple((side, d) for d in (1, 2, 3) for side in ("ahead", "behind"))


def face_rows(name):
    return {"z_low": (0, 4), "z_high": (3, 4), "t_low": (0, 1), "t_high": (12, 1)}[name]


def place(scratch, value, side, direction):
    if direction == 1:
        scratch[..., pl.ds(0, value.shape[-1])] = value
        return
    start, stride = {("ahead", 2): (3, 4), ("behind", 2): (0, 4), ("ahead", 3): (0, 1), ("behind", 3): (12, 1)}[
        (side, direction)
    ]
    scratch[:, pl.ds(start, 4, stride=stride), :] = value


def pass_kernel(*refs, first, residual_only, present, faces, link_mode, append_links, emit_back, colour_pass):
    refs = list(refs)
    width = 24
    ghost_dirs = [d for d in (1, 2, 3) if link_mode == "combined" and present["behind"][d]]
    link_face_scratch = refs.pop() if append_links and "z_high" in faces else None
    ghost_scratch = {}
    for direction in reversed(ghost_dirs):
        ghost_scratch[direction] = refs.pop()
    scratch_refs = {}
    for key in reversed([k for k in HALO_KEYS if present[k[0]][k[1]]]):
        scratch_refs[key] = refs.pop()
    back_out_ref = refs.pop() if emit_back else None
    face_refs = {}
    for name in reversed(faces):
        face_refs[name] = refs.pop()
    out_ref = refs.pop()

    def take():
        return refs.pop(0)

    src_ref = take()
    links_ref = take()
    back_ref = take() if link_mode == "given" else None
    labels_ref = take()
    colouring_ref = None if residual_only else take()
    spinor_ref = None
    halo_refs = {}
    if not first:
        spinor_ref = take()
        for key in HALO_KEYS:
            if present[key[0]][key[1]]:
                halo_refs[key] = take()

    rows, lanes = src_ref.shape[-2], src_ref.shape[-1]
    sh = Shifts(rows, lanes)
    shape = (2, 4, 3, rows, lanes)
    source = src_ref[...].reshape(shape)
    link_all = links_ref[...].astype(jnp.float32)
    links = [link_all[d].reshape(2, 3, 3, rows, lanes) for d in range(4)]
    if back_ref is not None:
        back_all = back_ref[...].astype(jnp.float32)
        back_links = [back_all[d].reshape(2, 3, 3, rows, lanes) for d in range(4)]
    else:
        back_links = []
        for direction in range(4):
            ghost = None
            if direction in ghost_scratch:
                halo = halo_refs[("behind", direction)]
                place(ghost_scratch[direction], halo[width:], "behind", direction)
                ghost = ghost_scratch[direction][...].reshape(2, 3, 3, rows, lanes)
            back_links.append(sh.behind(direction, links[direction], ghost, True))
    if back_out_ref is not None:
        for direction in range(4):
            back_out_ref[direction] = back_links[direction].reshape(18, rows, lanes).astype(back_out_ref.dtype)

    for key, scratch in scratch_refs.items():
        halo = halo_refs[key]
        value = halo[:width] if (key[0] == "behind" and key[1] in ghost_scratch) else halo[...]
        place(scratch, value, key[0], key[1])

    def load_halo(side, direction):
        ref = scratch_refs.get((side, direction), halo_refs.get((side, direction)))
        return None if ref is None else ref[...].reshape(shape)

    def wilson_global(spinor):
        ahead_list = [sh.ahead(d, spinor, load_halo("ahead", d), True) for d in range(4)]
        behind_list = [sh.behind(d, spinor, load_halo("behind", d), True) for d in range(4)]
        return hopping(spinor, links, back_links, ahead_list, behind_list)

    if first:
        residue = source
        current = None
    else:
        current = spinor_ref[...].reshape(shape)
        residue = source - wilson_global(current)
    if residual_only:
        out_ref[...] = residue.reshape(out_ref.shape).astype(out_ref.dtype)
        return

    label_index = labels_ref[...]
    labels = (label_index + 1).astype(jnp.float32)
    ahead_masks = [(sh.ahead(d, labels, None) == labels).astype(jnp.float32) for d in range(4)]
    behind_masks = [(sh.behind(d, labels, None) == labels).astype(jnp.float32) for d in range(4)]
    member_bool = label_index[None] == lax.broadcasted_iota(jnp.int32, (AGG, 1, 1), 0)
    member = member_bool.astype(jnp.float32)
    site_colour = jnp.zeros((rows, lanes), jnp.int32)
    for block in range(AGG):
        site_colour = jnp.where(label_index == block, colouring_ref[block], site_colour)
    colour_mask = (site_colour == colour_pass).astype(jnp.float32)

    def wilson_block(spinor):
        ahead_list = [sh.ahead(d, spinor, None) * ahead_masks[d] for d in range(4)]
        behind_list = [sh.behind(d, spinor, None) * behind_masks[d] for d in range(4)]
        return hopping(spinor, links, back_links, ahead_list, behind_list)

    def block_total(values):
        return jnp.sum(jnp.sum(member * values[None], axis=2, keepdims=True), axis=1, keepdims=True)

    update = None
    remainder = residue
    for repeat in range(MR_STEPS):
        image = wilson_block(remainder)
        image_flat = image.reshape(2, 12, rows, lanes)
        rest_flat = remainder.reshape(2, 12, rows, lanes)
        dot_real = jnp.sum(image_flat[0] * rest_flat[0] + image_flat[1] * rest_flat[1], axis=0)
        dot_imag = jnp.sum(image_flat[0] * rest_flat[1] - image_flat[1] * rest_flat[0], axis=0)
        norm = jnp.sum(image_flat[0] * image_flat[0] + image_flat[1] * image_flat[1], axis=0)
        denominator = block_total(norm) + 1e-06
        factor_real = jnp.sum(member * (block_total(dot_real) / denominator), axis=0)
        factor_imag = jnp.sum(member * (block_total(dot_imag) / denominator), axis=0)
        step = complex_scale(factor_real, factor_imag, remainder)
        update = step if update is None else update + step
        remainder = remainder - complex_scale(factor_real, factor_imag, image)
    update = update * colour_mask
    result = update if current is None else current + update
    out_ref[...] = result.reshape(out_ref.shape)
    if link_face_scratch is not None:
        link_face_scratch[...] = link_all[2]
    for name, face_ref in face_refs.items():
        if name == "y_low":
            face_ref[...] = out_ref[:, :, pl.ds(0, lanes // 2)]
        elif name == "y_high":
            face_ref[0:width] = pltpu.roll(out_ref[...], lanes // 2, 2)[:, :, : lanes // 2]
            if append_links:
                face_ref[width:] = pltpu.roll(link_all[1], lanes // 2, 2)[:, :, : lanes // 2]
        else:
            start, stride = face_rows(name)
            face_ref[0:width] = out_ref[:, pl.ds(start, 4, stride=stride), :]
            if append_links and name == "z_high":
                face_ref[width:] = link_face_scratch[:, pl.ds(start, 4, stride=stride), :]
            elif append_links and name == "t_high":
                face_ref[width:] = link_all[3][:, start:start + 4, :]


def run_pass(source, links, back, labels, colouring, colour_pass, spinor, halos, residual_only=False, faces=(),
             link_mode="given", append_links=False, emit_back=False):
    first = spinor is None
    present = {
        "ahead": [h is not None for h in halos["ahead"]] if not first else [False] * 4,
        "behind": [h is not None for h in halos["behind"]] if not first else [False] * 4,
    }
    operands = [source, links] + ([back] if link_mode == "given" else []) + [labels]
    spaces = [pltpu.VMEM] * len(operands)
    if not residual_only:
        operands.append(colouring)
        spaces.append(pltpu.SMEM)
    if not first:
        operands.append(spinor)
        for key in HALO_KEYS:
            if present[key[0]][key[1]]:
                operands.append(halos[key[0]][key[1]])
    spaces += [pltpu.VMEM] * (len(operands) - len(spaces))
    kernel = functools.partial(
        pass_kernel, first=first, residual_only=residual_only, present=present, faces=faces,
        link_mode=link_mode, append_links=append_links, emit_back=emit_back, colour_pass=colour_pass,
    )
    width = source.shape[0]

    def face_shape(name):
        rows = width + (18 if append_links and name.endswith("high") else 0)
        if name.startswith("y"):
            return (rows, source.shape[1], source.shape[2] // 2)
        return (rows, 4, source.shape[2])

    out_shape = [jax.ShapeDtypeStruct(source.shape, jnp.bfloat16 if residual_only else jnp.float32)]
    out_shape += [jax.ShapeDtypeStruct(face_shape(name), jnp.float32) for name in faces]
    if emit_back:
        out_shape.append(jax.ShapeDtypeStruct(links.shape, links.dtype))
    scratch = [pltpu.VMEM(source.shape, jnp.float32) for k in HALO_KEYS if present[k[0]][k[1]]]
    if link_mode == "combined":
        scratch += [pltpu.VMEM(links.shape[1:], jnp.float32) for d in (1, 2, 3) if present["behind"][d]]
    if append_links and "z_high" in faces:
        scratch.append(pltpu.VMEM(links.shape[1:], jnp.float32))
    in_specs = [pl.BlockSpec(memory_space=space) for space in spaces]
    results = pl.pallas_call(kernel, out_shape=out_shape, scratch_shapes=scratch, in_specs=in_specs)(*operands)
    face_values = dict(zip(faces, results[1:1 + len(faces)]))
    return results[0], face_values, (results[-1] if emit_back else None)


def coarse_kernel(*refs, present):
    refs = list(refs)
    out_ref = refs.pop()
    source_ref, inverse_ref = refs[0], refs[1]
    first = len(refs) == 2
    width = source_ref.shape[-1]
    chunks = width // 128
    lane = lax.broadcasted_iota(jnp.int32, (1, width), 1)
    position = lane % AGG
    selector = (
        lax.broadcasted_iota(jnp.int32, (8, 128), 1) // AGG == lax.broadcasted_iota(jnp.int32, (8, 128), 0)
    ).astype(jnp.float32)

    def reduce_flat(product):
        partial = product[:, 0:128]
        for q in range(1, chunks):
            partial = partial + product[:, q * 128:(q + 1) * 128]
        for shift in (64, 32, 16):
            partial = partial + pltpu.roll(partial, shift, 1)
        pieces = [
            jnp.sum(partial[8 * q:8 * q + 8] * selector, axis=0, keepdims=True) for q in range(chunks)
        ]
        return jnp.concatenate(pieces, axis=1)

    def roll_within(vector, shift):
        pieces = [pltpu.roll(vector[:, q * 128:(q + 1) * 128], shift % 128, 1) for q in range(chunks)]
        return jnp.concatenate(pieces, axis=1)

    def accumulate(acc, blocks_ref, index, vector):
        block_real = blocks_ref[index + (0,)].astype(jnp.float32)
        block_imag = blocks_ref[index + (1,)].astype(jnp.float32)
        real_part = block_real * vector[0] - block_imag * vector[1]
        imag_part = block_real * vector[1] + block_imag * vector[0]
        if acc is None:
            return [real_part, imag_part]
        return [acc[0] + real_part, acc[1] + imag_part]

    def precondition(vector):
        acc = accumulate(None, inverse_ref, (), vector)
        return [reduce_flat(acc[0]), reduce_flat(acc[1])]

    source = [source_ref[0], source_ref[1]]
    if first:
        result = precondition(source)
    else:
        operator_ref, current_ref = refs[2], refs[3]
        nearby_refs = refs[4:]
        current = [current_ref[0], current_ref[1]]
        ahead = [
            jnp.where(position == AGG - 1, roll_within(c, AGG - 1), roll_within(c, -1)) for c in current
        ]
        behind = [jnp.where(position == 0, roll_within(c, 1 - AGG), roll_within(c, 1)) for c in current]
        vectors = [current, ahead, behind]
        taken = 0
        for flag in present:
            if flag:
                vectors.append([nearby_refs[taken][0], nearby_refs[taken][1]])
                taken += 1
            else:
                vectors.append(None)
        acc = None
        for direction, vector in enumerate(vectors):
            if vector is not None:
                acc = accumulate(acc, operator_ref, (direction,), vector)
        residue = [source[0] - reduce_flat(acc[0]), source[1] - reduce_flat(acc[1])]
        step = precondition(residue)
        result = [current[0] + step[0], current[1] + step[1]]
    out_ref[0] = result[0]
    out_ref[1] = result[1]


def run_coarse(source, inverse_blocks, operator_blocks, current, nearby):
    operands = [source, inverse_blocks]
    present = ()
    if current is not None:
        present = tuple(v is not None for v in nearby)
        operands += [operator_blocks, current] + [v for v in nearby if v is not None]
    kernel = functools.partial(coarse_kernel, present=present)
    return pl.pallas_call(kernel, out_shape=jax.ShapeDtypeStruct(source.shape, jnp.float32))(*operands)


def body(
    fine_source, links, test_vectors, aggregate_map, colouring, coarse_operator, block_inverse
):
    time_extent = fine_source.shape[2]
    plane_extent = fine_source.shape[3]
    line_extent = fine_source.shape[4]
    rows = time_extent * plane_extent
    site_count = rows * line_extent
    domain_index = lax.axis_index("lat")
    domain_count = lax.axis_size("lat")
    plane_position = (domain_index + 2) % PZ
    upper_valid = plane_position < PZ - 1
    lower_valid = plane_position > 0
    later_valid = domain_index < domain_count - PZ
    earlier_valid = domain_index >= PZ

    source = fine_source.reshape(24, rows, line_extent)
    link_rows = links.reshape(4, 18, rows, line_extent)
    label_rows = aggregate_map.reshape(rows, line_extent)
    member = (label_rows[None] == jnp.arange(AGG, dtype=jnp.int32)[:, None, None]).astype(jnp.float32)
    colour_list = colouring.reshape(AGG)

    def z_up_ok(i):
        return (i + 2) % PZ != PZ - 1

    def z_down_ok(i):
        return (i + 2) % PZ != 0

    def t_up_ok(i):
        return i + PZ < domain_count

    def t_down_ok(i):
        return i - PZ >= 0

    half = line_extent // 2

    needed = ["y_low", "y_high"] + [
        name for name, ok in zip(FACES[2:], (z_up_ok, z_down_ok, t_up_ok, t_down_ok))
        if any(ok(i) for i in range(domain_count))
    ]

    def faces_of(spinor):
        result = {"y_low": spinor[..., :half], "y_high": spinor[..., half:]}
        for name in needed[2:]:
            start, stride = face_rows(name)
            result[name] = lax.slice_in_dim(spinor, start, start + 3 * stride + 1, stride, axis=1)
        return result

    def halos_of(spinor, faces):
        def face(name):
            return faces[name] if name in faces else None

        return {
            "ahead": [
                None,
                permute_from(faces["y_low"], "grp", 1, lambda i: True),
                permute_from(face("z_low"), "lat", 1, z_up_ok) if face("z_low") is not None else None,
                permute_from(face("t_low"), "lat", PZ, t_up_ok) if face("t_low") is not None else None,
            ],
            "behind": [
                None,
                permute_from(faces["y_high"], "grp", -1, lambda i: True),
                permute_from(face("z_high"), "lat", -1, z_down_ok) if face("z_high") is not None else None,
                permute_from(face("t_high"), "lat", -PZ, t_down_ok) if face("t_high") is not None else None,
            ],
        }

    smoothed_first, first_faces, _ = run_pass(
        source, link_rows, None, label_rows, colour_list, 0, None, None,
        faces=tuple(needed), link_mode="none", append_links=True,
    )
    vectors = test_vectors.reshape(NVEC, 2, 2, 6, site_count)
    vectors, smoothed_first = lax.optimization_barrier((vectors, smoothed_first))
    smoothed, smoothed_faces, back_rows = run_pass(
        source, link_rows, None, label_rows, colour_list, 1, smoothed_first,
        halos_of(smoothed_first, first_faces), faces=tuple(needed), link_mode="combined", emit_back=True,
    )

    def sweep(start, faces):
        current, current_faces, _ = run_pass(
            source, link_rows, back_rows, label_rows, colour_list, 0, start, halos_of(start, faces),
            faces=tuple(needed),
        )
        result, _, _ = run_pass(
            source, link_rows, back_rows, label_rows, colour_list, 1, current,
            halos_of(current, current_faces),
        )
        return result

    residue, _, _ = run_pass(
        source, link_rows, back_rows, label_rows, None, None, smoothed, halos_of(smoothed, smoothed_faces),
        residual_only=True,
    )
    residual = residue
    membership = member.reshape(AGG, site_count).T
    member_weights = membership.astype(jnp.bfloat16)
    weighted = residual.reshape(2, 2, 6, site_count)[..., None] * member_weights

    def contract(left, right):
        return jnp.einsum("kxqn,xqnj->xkj", left, right, preferred_element_type=jnp.float32)

    real_part = contract(vectors[:, 0], weighted[0]) + contract(vectors[:, 1], weighted[1])
    imag_part = contract(vectors[:, 0], weighted[1]) - contract(vectors[:, 1], weighted[0])
    coarse_source = jnp.stack([real_part, imag_part]).reshape(2, CDOF, AGG)
    flat_source = coarse_source.reshape(2, 1, CDOF * AGG)
    operator_blocks = coarse_operator.reshape(9, 2, CDOF, CDOF * AGG)
    inverse_blocks = block_inverse.reshape(2, CDOF, CDOF * AGG)
    correction = run_coarse(flat_source, inverse_blocks, operator_blocks, None, None)
    for repeat in range(2):
        nearby = [
            permute_from(correction, "grp", 1, lambda i: True),
            permute_from(correction, "grp", -1, lambda i: True),
            permute_from(correction, "lat", 1, z_up_ok),
            permute_from(correction, "lat", -1, z_down_ok),
            permute_from(correction, "lat", PZ, t_up_ok),
            permute_from(correction, "lat", -PZ, t_down_ok),
        ]
        correction = run_coarse(flat_source, inverse_blocks, operator_blocks, correction, nearby)
    correction = correction.reshape(2, CDOF, AGG)
    expanded = jnp.dot(
        correction.reshape(2 * CDOF, AGG), membership.T, precision=lax.Precision.HIGHEST
    ).reshape(2, 2, NVEC, site_count)
    spread_real = jnp.swapaxes(expanded[0], 0, 1)[:, :, None]
    spread_imag = jnp.swapaxes(expanded[1], 0, 1)[:, :, None]
    real_part = jnp.sum(vectors[:, 0] * spread_real - vectors[:, 1] * spread_imag, axis=0)
    imag_part = jnp.sum(vectors[:, 0] * spread_imag + vectors[:, 1] * spread_real, axis=0)
    corrected = smoothed + jnp.stack([real_part, imag_part]).reshape(24, rows, line_extent)
    solution = sweep(corrected, faces_of(corrected))
    return (
        solution.reshape(1, 24, time_extent, plane_extent, line_extent),
        correction.reshape(1, 1, 2, CDOF, AGG),
    )


def solution(mesh):
    return jax.shard_map(
        body,
        mesh=mesh,
        in_specs=(
            P("lat", None, None, None, "grp"),
            P("lat", None, None, None, None, "grp"),
            P("lat", None, None, None, None, "grp"),
            P("lat", None, None, "grp", None),
            P("lat", "grp", None),
            P("lat", "grp", None, None, None, None),
            P("lat", "grp", None, None, None),
        ),
        out_specs=(P("lat", None, None, None, "grp"), P("lat", "grp", None, None, None)),
        check_vma=False,
    )
```

```python
import functools

import jax
import jax.numpy as jnp
from jax import lax
from jax.experimental import pallas as pl
from jax.experimental.pallas import tpu as pltpu
from jax.sharding import PartitionSpec as P

CX = 64
PZ = 8
NVEC = 24
AGG = 16
MR_STEPS = 2
CDOF = 48


def passed_along(shard, axis, by):
    size = lax.axis_size(axis)
    return lax.ppermute(shard, axis, [(i, (i + by) % size) for i in range(size)])


def padded_2(shard, sides, width):
    for axis, dim in sides:
        size, length = (lax.axis_size(axis), shard.shape[dim])
        up = [(i, (i + 1) % size) for i in range(size)]
        down = [(j, i) for i, j in up]
        last = lax.slice_in_dim(shard, length - width, length, axis=dim)
        first = lax.slice_in_dim(shard, 0, width, axis=dim)
        before = lax.ppermute(last, axis, up)
        after = lax.ppermute(first, axis, down)
        shard = jnp.concatenate([before, shard, after], axis=dim)
    return shard


def times_minus_i(values):
    return jnp.stack([values[1], -values[0]])


def times_plus_i(values):
    return jnp.stack([-values[1], values[0]])


def spin_factor(direction, spin_pair):
    if direction == 0:
        return jnp.stack([times_minus_i(spin_pair[:, 1]), times_minus_i(spin_pair[:, 0])], axis=1)
    if direction == 1:
        return jnp.stack([-spin_pair[:, 1], spin_pair[:, 0]], axis=1)
    if direction == 2:
        return jnp.stack([times_minus_i(spin_pair[:, 0]), times_plus_i(spin_pair[:, 1])], axis=1)
    return spin_pair


def project_minus(direction, spinor):
    return spinor[:, :2] - spin_factor(direction, spinor[:, 2:])


def project_plus(direction, spinor):
    return spinor[:, :2] + spin_factor(direction, spinor[:, 2:])


def rebuild_minus(direction, half_spinor):
    lower_part = spin_factor(direction, half_spinor) if direction < 3 else -half_spinor
    return jnp.concatenate([half_spinor, lower_part], axis=1)


def rebuild_plus(direction, half_spinor):
    lower_part = -spin_factor(direction, half_spinor) if direction < 3 else half_spinor
    return jnp.concatenate([half_spinor, lower_part], axis=1)


def colour_product(gauge_link, half_spinor, adjoint):
    link_real = gauge_link[0]
    link_imag = gauge_link[1]
    if adjoint:
        link_real = jnp.swapaxes(link_real, 0, 1)
        link_imag = -jnp.swapaxes(link_imag, 0, 1)
    spin_real = half_spinor[0][:, None]
    spin_imag = half_spinor[1][:, None]
    real_part = jnp.sum(link_real[None] * spin_real - link_imag[None] * spin_imag, axis=2)
    imag_part = jnp.sum(link_real[None] * spin_imag + link_imag[None] * spin_real, axis=2)
    return jnp.stack([real_part, imag_part])


def complex_scale(factor_real, factor_imag, lattice):
    return jnp.stack(
        [
            factor_real * lattice[0] - factor_imag * lattice[1],
            factor_real * lattice[1] + factor_imag * lattice[0],
        ]
    )


def apply_blocks(blocks, nearby):
    matrices = blocks.reshape(blocks.shape[0], 2, CDOF, CDOF, AGG)
    vector_real = nearby[:, 0][:, None]
    vector_imag = nearby[:, 1][:, None]
    real_part = jnp.sum(matrices[:, 0] * vector_real - matrices[:, 1] * vector_imag, axis=(0, 2))
    imag_part = jnp.sum(matrices[:, 0] * vector_imag + matrices[:, 1] * vector_real, axis=(0, 2))
    return jnp.stack([real_part, imag_part])


def keep_if(allowed, values):
    return jnp.where(allowed, values, jnp.zeros_like(values))


def permute_from(value, axis, offset, allowed):
    size = lax.axis_size(axis)
    pairs = [((i + offset) % size, i) for i in range(size) if allowed(i)]
    if not pairs:
        return None
    return lax.ppermute(value, axis, pairs)


class Shifts:
    def __init__(self, rows, lanes):
        self.rows = rows
        self.lanes = lanes
        self.lane = lax.broadcasted_iota(jnp.int32, (rows, lanes), 1)
        self.row = lax.broadcasted_iota(jnp.int32, (rows, lanes), 0)
        self.xpos = self.lane % CX
        self.zpos = self.row % 4

    def roll(self, a, shift, axis):
        n = a.shape[axis]
        return pltpu.roll(a, shift % n, a.ndim + axis)

    def ahead(self, direction, a, nbr, placed=False):
        if direction == 0:
            return jnp.where(self.xpos == CX - 1, self.roll(a, CX - 1, -1), self.roll(a, -1, -1))
        if direction == 1:
            half = self.lanes // 2
            if placed and nbr is not None:
                return jnp.where(self.lane >= half, self.roll(nbr, half, -1), self.roll(a, half, -1))
            filled = jnp.where(self.lane < half, 0.0 if nbr is None else nbr, a)
            return self.roll(filled, half, -1)
        if direction == 2:
            inner = self.roll(a, -1, -2)
            outer = 0.0 if nbr is None else (nbr if placed else self.roll(nbr, 3, -2))
            return jnp.where(self.zpos == 3, outer, inner)
        filled = jnp.where(self.row < 4, 0.0 if nbr is None else nbr, a)
        return self.roll(filled, -4, -2)

    def behind(self, direction, a, nbr, placed=False):
        if direction == 0:
            return jnp.where(self.xpos == 0, self.roll(a, 1 - CX, -1), self.roll(a, 1, -1))
        if direction == 1:
            half = self.lanes // 2
            if placed and nbr is not None:
                return jnp.where(self.lane < half, nbr, self.roll(a, half, -1))
            filled = jnp.where(self.lane >= half, 0.0 if nbr is None else nbr, a)
            return self.roll(filled, half, -1)
        if direction == 2:
            inner = self.roll(a, 1, -2)
            outer = 0.0 if nbr is None else (nbr if placed else self.roll(nbr, -3, -2))
            return jnp.where(self.zpos == 0, outer, inner)
        filled = jnp.where(self.row >= self.rows - 4, 0.0 if nbr is None else nbr, a)
        return self.roll(filled, 4, -2)


def hopping(spinor, links, back_links, ahead_list, behind_list):
    hop_total = None
    for direction in range(4):
        ahead_half = colour_product(links[direction], project_minus(direction, ahead_list[direction]), False)
        behind_half = colour_product(back_links[direction], project_plus(direction, behind_list[direction]), True)
        term = rebuild_minus(direction, ahead_half) + rebuild_plus(direction, behind_half)
        hop_total = term if hop_total is None else hop_total + term
    return 4.5 * spinor - 0.5 * hop_total


FACES = ("y_low", "y_high", "z_low", "z_high", "t_low", "t_high")
HALO_KEYS = tuple((side, d) for d in (1, 2, 3) for side in ("ahead", "behind"))


def face_rows(name):
    return {"z_low": (0, 4), "z_high": (3, 4), "t_low": (0, 1), "t_high": (12, 1)}[name]


def place(scratch, value, side, direction):
    if direction == 1:
        scratch[..., pl.ds(0, value.shape[-1])] = value
        return
    start, stride = {("ahead", 2): (3, 4), ("behind", 2): (0, 4), ("ahead", 3): (0, 1), ("behind", 3): (12, 1)}[
        (side, direction)
    ]
    scratch[:, pl.ds(start, 4, stride=stride), :] = value


def pass_kernel(*refs, first, residual_only, present, faces, link_mode, append_links, emit_back, colour_pass):
    refs = list(refs)
    width = 24
    ghost_dirs = [d for d in (1, 2, 3) if link_mode == "combined" and present["behind"][d]]
    link_face_scratch = refs.pop() if append_links and "z_high" in faces else None
    ghost_scratch = {}
    for direction in reversed(ghost_dirs):
        ghost_scratch[direction] = refs.pop()
    scratch_refs = {}
    for key in reversed([k for k in HALO_KEYS if present[k[0]][k[1]]]):
        scratch_refs[key] = refs.pop()
    back_out_ref = refs.pop() if emit_back else None
    face_refs = {}
    for name in reversed(faces):
        face_refs[name] = refs.pop()
    out_ref = refs.pop()

    def take():
        return refs.pop(0)

    src_ref = take()
    links_ref = take()
    back_ref = take() if link_mode == "given" else None
    labels_ref = take()
    colouring_ref = None if residual_only else take()
    spinor_ref = None
    halo_refs = {}
    if not first:
        spinor_ref = take()
        for key in HALO_KEYS:
            if present[key[0]][key[1]]:
                halo_refs[key] = take()

    rows, lanes = src_ref.shape[-2], src_ref.shape[-1]
    sh = Shifts(rows, lanes)
    shape = (2, 4, 3, rows, lanes)
    source = src_ref[...].reshape(shape)
    link_all = links_ref[...].astype(jnp.float32)
    links = [link_all[d].reshape(2, 3, 3, rows, lanes) for d in range(4)]
    if back_ref is not None:
        back_all = back_ref[...].astype(jnp.float32)
        back_links = [back_all[d].reshape(2, 3, 3, rows, lanes) for d in range(4)]
    else:
        back_links = []
        for direction in range(4):
            ghost = None
            if direction in ghost_scratch:
                halo = halo_refs[("behind", direction)]
                place(ghost_scratch[direction], halo[width:], "behind", direction)
                ghost = ghost_scratch[direction][...].reshape(2, 3, 3, rows, lanes)
            back_links.append(sh.behind(direction, links[direction], ghost, True))
    if back_out_ref is not None:
        for direction in range(4):
            back_out_ref[direction] = back_links[direction].reshape(18, rows, lanes).astype(back_out_ref.dtype)

    for key, scratch in scratch_refs.items():
        halo = halo_refs[key]
        value = halo[:width] if (key[0] == "behind" and key[1] in ghost_scratch) else halo[...]
        place(scratch, value, key[0], key[1])

    def load_halo(side, direction):
        ref = scratch_refs.get((side, direction), halo_refs.get((side, direction)))
        return None if ref is None else ref[...].reshape(shape)

    def wilson_global(spinor):
        ahead_list = [sh.ahead(d, spinor, load_halo("ahead", d), True) for d in range(4)]
        behind_list = [sh.behind(d, spinor, load_halo("behind", d), True) for d in range(4)]
        return hopping(spinor, links, back_links, ahead_list, behind_list)

    if first:
        residue = source
        current = None
    else:
        current = spinor_ref[...].reshape(shape)
        residue = source - wilson_global(current)
    if residual_only:
        out_ref[...] = residue.reshape(out_ref.shape).astype(out_ref.dtype)
        return

    label_index = labels_ref[...]
    labels = (label_index + 1).astype(jnp.float32)
    ahead_masks = [(sh.ahead(d, labels, None) == labels).astype(jnp.float32) for d in range(4)]
    behind_masks = [(sh.behind(d, labels, None) == labels).astype(jnp.float32) for d in range(4)]
    member_bool = label_index[None] == lax.broadcasted_iota(jnp.int32, (AGG, 1, 1), 0)
    member = member_bool.astype(jnp.float32)
    site_colour = jnp.zeros((rows, lanes), jnp.int32)
    for block in range(AGG):
        site_colour = jnp.where(label_index == block, colouring_ref[block], site_colour)
    colour_mask = (site_colour == colour_pass).astype(jnp.float32)

    def wilson_block(spinor):
        ahead_list = [sh.ahead(d, spinor, None) * ahead_masks[d] for d in range(4)]
        behind_list = [sh.behind(d, spinor, None) * behind_masks[d] for d in range(4)]
        return hopping(spinor, links, back_links, ahead_list, behind_list)

    def block_total(values):
        return jnp.sum(jnp.sum(member * values[None], axis=2, keepdims=True), axis=1, keepdims=True)

    update = None
    remainder = residue
    for repeat in range(MR_STEPS):
        image = wilson_block(remainder)
        image_flat = image.reshape(2, 12, rows, lanes)
        rest_flat = remainder.reshape(2, 12, rows, lanes)
        dot_real = jnp.sum(image_flat[0] * rest_flat[0] + image_flat[1] * rest_flat[1], axis=0)
        dot_imag = jnp.sum(image_flat[0] * rest_flat[1] - image_flat[1] * rest_flat[0], axis=0)
        norm = jnp.sum(image_flat[0] * image_flat[0] + image_flat[1] * image_flat[1], axis=0)
        denominator = block_total(norm) + 1e-06
        factor_real = jnp.sum(member * (block_total(dot_real) / denominator), axis=0)
        factor_imag = jnp.sum(member * (block_total(dot_imag) / denominator), axis=0)
        step = complex_scale(factor_real, factor_imag, remainder)
        update = step if update is None else update + step
        remainder = remainder - complex_scale(factor_real, factor_imag, image)
    update = update * colour_mask
    result = update if current is None else current + update
    out_ref[...] = result.reshape(out_ref.shape)
    if link_face_scratch is not None:
        link_face_scratch[...] = link_all[2]
    for name, face_ref in face_refs.items():
        if name == "y_low":
            face_ref[...] = out_ref[:, :, pl.ds(0, lanes // 2)]
        elif name == "y_high":
            face_ref[0:width] = pltpu.roll(out_ref[...], lanes // 2, 2)[:, :, : lanes // 2]
            if append_links:
                face_ref[width:] = pltpu.roll(link_all[1], lanes // 2, 2)[:, :, : lanes // 2]
        else:
            start, stride = face_rows(name)
            face_ref[0:width] = out_ref[:, pl.ds(start, 4, stride=stride), :]
            if append_links and name == "z_high":
                face_ref[width:] = link_face_scratch[:, pl.ds(start, 4, stride=stride), :]
            elif append_links and name == "t_high":
                face_ref[width:] = link_all[3][:, start:start + 4, :]


def run_pass(source, links, back, labels, colouring, colour_pass, spinor, halos, residual_only=False, faces=(),
             link_mode="given", append_links=False, emit_back=False):
    first = spinor is None
    present = {
        "ahead": [h is not None for h in halos["ahead"]] if not first else [False] * 4,
        "behind": [h is not None for h in halos["behind"]] if not first else [False] * 4,
    }
    operands = [source, links] + ([back] if link_mode == "given" else []) + [labels]
    spaces = [pltpu.VMEM] * len(operands)
    if not residual_only:
        operands.append(colouring)
        spaces.append(pltpu.SMEM)
    if not first:
        operands.append(spinor)
        for key in HALO_KEYS:
            if present[key[0]][key[1]]:
                operands.append(halos[key[0]][key[1]])
    spaces += [pltpu.VMEM] * (len(operands) - len(spaces))
    kernel = functools.partial(
        pass_kernel, first=first, residual_only=residual_only, present=present, faces=faces,
        link_mode=link_mode, append_links=append_links, emit_back=emit_back, colour_pass=colour_pass,
    )
    width = source.shape[0]

    def face_shape(name):
        rows = width + (18 if append_links and name.endswith("high") else 0)
        if name.startswith("y"):
            return (rows, source.shape[1], source.shape[2] // 2)
        return (rows, 4, source.shape[2])

    out_shape = [jax.ShapeDtypeStruct(source.shape, jnp.bfloat16 if residual_only else jnp.float32)]
    out_shape += [jax.ShapeDtypeStruct(face_shape(name), jnp.float32) for name in faces]
    if emit_back:
        out_shape.append(jax.ShapeDtypeStruct(links.shape, links.dtype))
    scratch = [pltpu.VMEM(source.shape, jnp.float32) for k in HALO_KEYS if present[k[0]][k[1]]]
    if link_mode == "combined":
        scratch += [pltpu.VMEM(links.shape[1:], jnp.float32) for d in (1, 2, 3) if present["behind"][d]]
    if append_links and "z_high" in faces:
        scratch.append(pltpu.VMEM(links.shape[1:], jnp.float32))
    in_specs = [pl.BlockSpec(memory_space=space) for space in spaces]
    results = pl.pallas_call(kernel, out_shape=out_shape, scratch_shapes=scratch, in_specs=in_specs)(*operands)
    face_values = dict(zip(faces, results[1:1 + len(faces)]))
    return results[0], face_values, (results[-1] if emit_back else None)


def coarse_kernel(*refs, present):
    refs = list(refs)
    out_ref = refs.pop()
    source_ref, inverse_ref = refs[0], refs[1]
    first = len(refs) == 2
    width = source_ref.shape[-1]
    chunks = width // 128
    lane = lax.broadcasted_iota(jnp.int32, (1, width), 1)
    position = lane % AGG
    selector = (
        lax.broadcasted_iota(jnp.int32, (8, 128), 1) // AGG == lax.broadcasted_iota(jnp.int32, (8, 128), 0)
    ).astype(jnp.float32)

    def reduce_flat(product):
        partial = product[:, 0:128]
        for q in range(1, chunks):
            partial = partial + product[:, q * 128:(q + 1) * 128]
        for shift in (64, 32, 16):
            partial = partial + pltpu.roll(partial, shift, 1)
        pieces = [
            jnp.sum(partial[8 * q:8 * q + 8] * selector, axis=0, keepdims=True) for q in range(chunks)
        ]
        return jnp.concatenate(pieces, axis=1)

    def roll_within(vector, shift):
        pieces = [pltpu.roll(vector[:, q * 128:(q + 1) * 128], shift % 128, 1) for q in range(chunks)]
        return jnp.concatenate(pieces, axis=1)

    def accumulate(acc, blocks_ref, index, vector):
        block_real = blocks_ref[index + (0,)].astype(jnp.float32)
        block_imag = blocks_ref[index + (1,)].astype(jnp.float32)
        real_part = block_real * vector[0] - block_imag * vector[1]
        imag_part = block_real * vector[1] + block_imag * vector[0]
        if acc is None:
            return [real_part, imag_part]
        return [acc[0] + real_part, acc[1] + imag_part]

    def precondition(vector):
        acc = accumulate(None, inverse_ref, (), vector)
        return [reduce_flat(acc[0]), reduce_flat(acc[1])]

    source = [source_ref[0], source_ref[1]]
    if first:
        result = precondition(source)
    else:
        operator_ref, current_ref = refs[2], refs[3]
        nearby_refs = refs[4:]
        current = [current_ref[0], current_ref[1]]
        ahead = [
            jnp.where(position == AGG - 1, roll_within(c, AGG - 1), roll_within(c, -1)) for c in current
        ]
        behind = [jnp.where(position == 0, roll_within(c, 1 - AGG), roll_within(c, 1)) for c in current]
        vectors = [current, ahead, behind]
        taken = 0
        for flag in present:
            if flag:
                vectors.append([nearby_refs[taken][0], nearby_refs[taken][1]])
                taken += 1
            else:
                vectors.append(None)
        acc = None
        for direction, vector in enumerate(vectors):
            if vector is not None:
                acc = accumulate(acc, operator_ref, (direction,), vector)
        residue = [source[0] - reduce_flat(acc[0]), source[1] - reduce_flat(acc[1])]
        step = precondition(residue)
        result = [current[0] + step[0], current[1] + step[1]]
    out_ref[0] = result[0]
    out_ref[1] = result[1]


def run_coarse(source, inverse_blocks, operator_blocks, current, nearby):
    operands = [source, inverse_blocks]
    present = ()
    if current is not None:
        present = tuple(v is not None for v in nearby)
        operands += [operator_blocks, current] + [v for v in nearby if v is not None]
    kernel = functools.partial(coarse_kernel, present=present)
    return pl.pallas_call(kernel, out_shape=jax.ShapeDtypeStruct(source.shape, jnp.float32))(*operands)


def body(
    fine_source, links, test_vectors, aggregate_map, colouring, coarse_operator, block_inverse
):
    time_extent = fine_source.shape[2]
    plane_extent = fine_source.shape[3]
    line_extent = fine_source.shape[4]
    rows = time_extent * plane_extent
    site_count = rows * line_extent
    domain_index = lax.axis_index("lat")
    domain_count = lax.axis_size("lat")
    plane_position = (domain_index + 2) % PZ
    upper_valid = plane_position < PZ - 1
    lower_valid = plane_position > 0
    later_valid = domain_index < domain_count - PZ
    earlier_valid = domain_index >= PZ

    source = fine_source.reshape(24, rows, line_extent)
    link_rows = links.reshape(4, 18, rows, line_extent)
    label_rows = aggregate_map.reshape(rows, line_extent)
    colour_list = colouring.reshape(AGG)

    def z_up_ok(i):
        return (i + 2) % PZ != PZ - 1

    def z_down_ok(i):
        return (i + 2) % PZ != 0

    def t_up_ok(i):
        return i + PZ < domain_count

    def t_down_ok(i):
        return i - PZ >= 0

    half = line_extent // 2

    needed = ["y_low", "y_high"] + [
        name for name, ok in zip(FACES[2:], (z_up_ok, z_down_ok, t_up_ok, t_down_ok))
        if any(ok(i) for i in range(domain_count))
    ]

    def faces_of(spinor):
        result = {"y_low": spinor[..., :half], "y_high": spinor[..., half:]}
        for name in needed[2:]:
            start, stride = face_rows(name)
            result[name] = lax.slice_in_dim(spinor, start, start + 3 * stride + 1, stride, axis=1)
        return result

    def halos_of(spinor, faces):
        def face(name):
            return faces[name] if name in faces else None

        return {
            "ahead": [
                None,
                permute_from(faces["y_low"], "grp", 1, lambda i: True),
                permute_from(face("z_low"), "lat", 1, z_up_ok) if face("z_low") is not None else None,
                permute_from(face("t_low"), "lat", PZ, t_up_ok) if face("t_low") is not None else None,
            ],
            "behind": [
                None,
                permute_from(faces["y_high"], "grp", -1, lambda i: True),
                permute_from(face("z_high"), "lat", -1, z_down_ok) if face("z_high") is not None else None,
                permute_from(face("t_high"), "lat", -PZ, t_down_ok) if face("t_high") is not None else None,
            ],
        }

    smoothed_first, first_faces, _ = run_pass(
        source, link_rows, None, label_rows, colour_list, 0, None, None,
        faces=tuple(needed), link_mode="none", append_links=True,
    )
    smoothed, smoothed_faces, back_rows = run_pass(
        source, link_rows, None, label_rows, colour_list, 1, smoothed_first,
        halos_of(smoothed_first, first_faces), faces=tuple(needed), link_mode="combined", emit_back=True,
    )

    def sweep(start, faces):
        current, current_faces, _ = run_pass(
            source, link_rows, back_rows, label_rows, colour_list, 0, start, halos_of(start, faces),
            faces=tuple(needed),
        )
        result, _, _ = run_pass(
            source, link_rows, back_rows, label_rows, colour_list, 1, current,
            halos_of(current, current_faces),
        )
        return result

    residue, _, _ = run_pass(
        source, link_rows, back_rows, label_rows, None, None, smoothed, halos_of(smoothed, smoothed_faces),
        residual_only=True,
    )
    site_dims = (time_extent, plane_extent, line_extent)
    vectors = test_vectors.reshape((NVEC, 2, 2, 6) + site_dims)
    residual = residue.reshape((2, 2, 6) + site_dims)
    member_sites = (
        aggregate_map.reshape(site_dims)[None] == jnp.arange(AGG, dtype=jnp.int32)[:, None, None, None]
    )
    weighted = residual[:, :, None] * member_sites.astype(jnp.bfloat16)[None, None, :, None]

    def contract(left, right):
        return jnp.einsum("khqtzl,hjqtzl->hkj", left, right, preferred_element_type=jnp.float32)

    real_part = contract(vectors[:, 0], weighted[0]) + contract(vectors[:, 1], weighted[1])
    imag_part = contract(vectors[:, 0], weighted[1]) - contract(vectors[:, 1], weighted[0])
    coarse_source = jnp.stack([real_part, imag_part]).reshape(2, CDOF, AGG)
    flat_source = coarse_source.reshape(2, 1, CDOF * AGG)
    operator_blocks = coarse_operator.reshape(9, 2, CDOF, CDOF * AGG)
    inverse_blocks = block_inverse.reshape(2, CDOF, CDOF * AGG)
    correction = run_coarse(flat_source, inverse_blocks, operator_blocks, None, None)
    for repeat in range(2):
        nearby = [
            permute_from(correction, "grp", 1, lambda i: True),
            permute_from(correction, "grp", -1, lambda i: True),
            permute_from(correction, "lat", 1, z_up_ok),
            permute_from(correction, "lat", -1, z_down_ok),
            permute_from(correction, "lat", PZ, t_up_ok),
            permute_from(correction, "lat", -PZ, t_down_ok),
        ]
        correction = run_coarse(flat_source, inverse_blocks, operator_blocks, correction, nearby)
    correction = correction.reshape(2, CDOF, AGG)
    expanded = jnp.einsum(
        "ahkj,jtzl->akhtzl",
        correction.reshape(2, 2, NVEC, AGG),
        member_sites.astype(jnp.float32),
        precision=lax.Precision.HIGHEST,
    )
    spread_real = expanded[0][:, :, None]
    spread_imag = expanded[1][:, :, None]
    real_part = jnp.sum(vectors[:, 0] * spread_real - vectors[:, 1] * spread_imag, axis=0)
    imag_part = jnp.sum(vectors[:, 0] * spread_imag + vectors[:, 1] * spread_real, axis=0)
    corrected = smoothed + jnp.stack([real_part, imag_part]).reshape(24, rows, line_extent)
    solution = sweep(corrected, faces_of(corrected))
    return (
        solution.reshape(1, 24, time_extent, plane_extent, line_extent),
        correction.reshape(1, 1, 2, CDOF, AGG),
    )


def solution(mesh):
    return jax.shard_map(
        body,
        mesh=mesh,
        in_specs=(
            P("lat", None, None, None, "grp"),
            P("lat", None, None, None, None, "grp"),
            P("lat", None, None, None, None, "grp"),
            P("lat", None, None, "grp", None),
            P("lat", "grp", None),
            P("lat", "grp", None, None, None, None),
            P("lat", "grp", None, None, None),
        ),
        out_specs=(P("lat", None, None, None, "grp"), P("lat", "grp", None, None, None)),
        check_vma=False,
    )
```

```python
import functools

import jax
import jax.numpy as jnp
from jax import lax
from jax.experimental import pallas as pl
from jax.experimental.pallas import tpu as pltpu
from jax.sharding import PartitionSpec as P

CX = 64
PZ = 8
NVEC = 24
AGG = 16
MR_STEPS = 2
CDOF = 48


def passed_along(shard, axis, by):
    size = lax.axis_size(axis)
    return lax.ppermute(shard, axis, [(i, (i + by) % size) for i in range(size)])


def padded_2(shard, sides, width):
    for axis, dim in sides:
        size, length = (lax.axis_size(axis), shard.shape[dim])
        up = [(i, (i + 1) % size) for i in range(size)]
        down = [(j, i) for i, j in up]
        last = lax.slice_in_dim(shard, length - width, length, axis=dim)
        first = lax.slice_in_dim(shard, 0, width, axis=dim)
        before = lax.ppermute(last, axis, up)
        after = lax.ppermute(first, axis, down)
        shard = jnp.concatenate([before, shard, after], axis=dim)
    return shard


def times_minus_i(values):
    return jnp.stack([values[1], -values[0]])


def times_plus_i(values):
    return jnp.stack([-values[1], values[0]])


def spin_factor(direction, spin_pair):
    if direction == 0:
        return jnp.stack([times_minus_i(spin_pair[:, 1]), times_minus_i(spin_pair[:, 0])], axis=1)
    if direction == 1:
        return jnp.stack([-spin_pair[:, 1], spin_pair[:, 0]], axis=1)
    if direction == 2:
        return jnp.stack([times_minus_i(spin_pair[:, 0]), times_plus_i(spin_pair[:, 1])], axis=1)
    return spin_pair


def project_minus(direction, spinor):
    return spinor[:, :2] - spin_factor(direction, spinor[:, 2:])


def project_plus(direction, spinor):
    return spinor[:, :2] + spin_factor(direction, spinor[:, 2:])


def rebuild_minus(direction, half_spinor):
    lower_part = spin_factor(direction, half_spinor) if direction < 3 else -half_spinor
    return jnp.concatenate([half_spinor, lower_part], axis=1)


def rebuild_plus(direction, half_spinor):
    lower_part = -spin_factor(direction, half_spinor) if direction < 3 else half_spinor
    return jnp.concatenate([half_spinor, lower_part], axis=1)


def colour_product(gauge_link, half_spinor, adjoint):
    link_real = gauge_link[0]
    link_imag = gauge_link[1]
    if adjoint:
        link_real = jnp.swapaxes(link_real, 0, 1)
        link_imag = -jnp.swapaxes(link_imag, 0, 1)
    spin_real = half_spinor[0][:, None]
    spin_imag = half_spinor[1][:, None]
    real_part = jnp.sum(link_real[None] * spin_real - link_imag[None] * spin_imag, axis=2)
    imag_part = jnp.sum(link_real[None] * spin_imag + link_imag[None] * spin_real, axis=2)
    return jnp.stack([real_part, imag_part])


def complex_scale(factor_real, factor_imag, lattice):
    return jnp.stack(
        [
            factor_real * lattice[0] - factor_imag * lattice[1],
            factor_real * lattice[1] + factor_imag * lattice[0],
        ]
    )


def apply_blocks(blocks, nearby):
    matrices = blocks.reshape(blocks.shape[0], 2, CDOF, CDOF, AGG)
    vector_real = nearby[:, 0][:, None]
    vector_imag = nearby[:, 1][:, None]
    real_part = jnp.sum(matrices[:, 0] * vector_real - matrices[:, 1] * vector_imag, axis=(0, 2))
    imag_part = jnp.sum(matrices[:, 0] * vector_imag + matrices[:, 1] * vector_real, axis=(0, 2))
    return jnp.stack([real_part, imag_part])


def keep_if(allowed, values):
    return jnp.where(allowed, values, jnp.zeros_like(values))


def permute_from(value, axis, offset, allowed):
    size = lax.axis_size(axis)
    pairs = [((i + offset) % size, i) for i in range(size) if allowed(i)]
    if not pairs:
        return None
    return lax.ppermute(value, axis, pairs)


class Shifts:
    def __init__(self, rows, lanes):
        self.rows = rows
        self.lanes = lanes
        self.lane = lax.broadcasted_iota(jnp.int32, (rows, lanes), 1)
        self.row = lax.broadcasted_iota(jnp.int32, (rows, lanes), 0)
        self.xpos = self.lane % CX
        self.zpos = self.row % 4

    def roll(self, a, shift, axis):
        n = a.shape[axis]
        return pltpu.roll(a, shift % n, a.ndim + axis)

    def ahead(self, direction, a, nbr, placed=False):
        if direction == 0:
            return jnp.where(self.xpos == CX - 1, self.roll(a, CX - 1, -1), self.roll(a, -1, -1))
        if direction == 1:
            half = self.lanes // 2
            if placed and nbr is not None:
                return jnp.where(self.lane >= half, self.roll(nbr, half, -1), self.roll(a, half, -1))
            filled = jnp.where(self.lane < half, 0.0 if nbr is None else nbr, a)
            return self.roll(filled, half, -1)
        if direction == 2:
            inner = self.roll(a, -1, -2)
            outer = 0.0 if nbr is None else (nbr if placed else self.roll(nbr, 3, -2))
            return jnp.where(self.zpos == 3, outer, inner)
        filled = jnp.where(self.row < 4, 0.0 if nbr is None else nbr, a)
        return self.roll(filled, -4, -2)

    def behind(self, direction, a, nbr, placed=False):
        if direction == 0:
            return jnp.where(self.xpos == 0, self.roll(a, 1 - CX, -1), self.roll(a, 1, -1))
        if direction == 1:
            half = self.lanes // 2
            if placed and nbr is not None:
                return jnp.where(self.lane < half, nbr, self.roll(a, half, -1))
            filled = jnp.where(self.lane >= half, 0.0 if nbr is None else nbr, a)
            return self.roll(filled, half, -1)
        if direction == 2:
            inner = self.roll(a, 1, -2)
            outer = 0.0 if nbr is None else (nbr if placed else self.roll(nbr, -3, -2))
            return jnp.where(self.zpos == 0, outer, inner)
        filled = jnp.where(self.row >= self.rows - 4, 0.0 if nbr is None else nbr, a)
        return self.roll(filled, 4, -2)


def hopping(spinor, links, back_links, ahead_list, behind_list):
    hop_total = None
    for direction in range(4):
        ahead_half = colour_product(links[direction], project_minus(direction, ahead_list[direction]), False)
        behind_half = colour_product(back_links[direction], project_plus(direction, behind_list[direction]), True)
        term = rebuild_minus(direction, ahead_half) + rebuild_plus(direction, behind_half)
        hop_total = term if hop_total is None else hop_total + term
    return 4.5 * spinor - 0.5 * hop_total


FACES = ("y_low", "y_high", "z_low", "z_high", "t_low", "t_high")
HALO_KEYS = tuple((side, d) for d in (1, 2, 3) for side in ("ahead", "behind"))


def face_rows(name):
    return {"z_low": (0, 4), "z_high": (3, 4), "t_low": (0, 1), "t_high": (12, 1)}[name]


def place(scratch, value, side, direction):
    if direction == 1:
        scratch[..., pl.ds(0, value.shape[-1])] = value
        return
    start, stride = {("ahead", 2): (3, 4), ("behind", 2): (0, 4), ("ahead", 3): (0, 1), ("behind", 3): (12, 1)}[
        (side, direction)
    ]
    scratch[:, pl.ds(start, 4, stride=stride), :] = value


def pass_kernel(*refs, first, residual_only, present, faces, link_mode, append_links, emit_back, colour_pass):
    refs = list(refs)
    width = 24
    ghost_dirs = [d for d in (1, 2, 3) if link_mode == "combined" and present["behind"][d]]
    link_face_scratch = refs.pop() if append_links and "z_high" in faces else None
    ghost_scratch = {}
    for direction in reversed(ghost_dirs):
        ghost_scratch[direction] = refs.pop()
    scratch_refs = {}
    for key in reversed([k for k in HALO_KEYS if present[k[0]][k[1]]]):
        scratch_refs[key] = refs.pop()
    back_out_ref = refs.pop() if emit_back else None
    face_refs = {}
    for name in reversed(faces):
        face_refs[name] = refs.pop()
    out_ref = refs.pop()

    def take():
        return refs.pop(0)

    src_ref = take()
    links_ref = take()
    back_ref = take() if link_mode == "given" else None
    labels_ref = take()
    colouring_ref = None if residual_only else take()
    spinor_ref = None
    halo_refs = {}
    if not first:
        spinor_ref = take()
        for key in HALO_KEYS:
            if present[key[0]][key[1]]:
                halo_refs[key] = take()

    rows, lanes = src_ref.shape[-2], src_ref.shape[-1]
    sh = Shifts(rows, lanes)
    shape = (2, 4, 3, rows, lanes)
    source = src_ref[...].reshape(shape)
    link_all = links_ref[...].astype(jnp.float32)
    links = [link_all[d].reshape(2, 3, 3, rows, lanes) for d in range(4)]
    if back_ref is not None:
        back_all = back_ref[...].astype(jnp.float32)
        back_links = [back_all[d].reshape(2, 3, 3, rows, lanes) for d in range(4)]
    else:
        back_links = []
        for direction in range(4):
            ghost = None
            if direction in ghost_scratch:
                halo = halo_refs[("behind", direction)]
                place(ghost_scratch[direction], halo[width:], "behind", direction)
                ghost = ghost_scratch[direction][...].reshape(2, 3, 3, rows, lanes)
            back_links.append(sh.behind(direction, links[direction], ghost, True))
    if back_out_ref is not None:
        for direction in range(4):
            back_out_ref[direction] = back_links[direction].reshape(18, rows, lanes).astype(back_out_ref.dtype)

    for key, scratch in scratch_refs.items():
        halo = halo_refs[key]
        value = halo[:width] if (key[0] == "behind" and key[1] in ghost_scratch) else halo[...]
        place(scratch, value, key[0], key[1])

    def load_halo(side, direction):
        ref = scratch_refs.get((side, direction), halo_refs.get((side, direction)))
        return None if ref is None else ref[...].reshape(shape)

    def wilson_global(spinor):
        ahead_list = [sh.ahead(d, spinor, load_halo("ahead", d), True) for d in range(4)]
        behind_list = [sh.behind(d, spinor, load_halo("behind", d), True) for d in range(4)]
        return hopping(spinor, links, back_links, ahead_list, behind_list)

    if first:
        residue = source
        current = None
    else:
        current = spinor_ref[...].reshape(shape)
        residue = source - wilson_global(current)
    if residual_only:
        out_ref[...] = residue.reshape(out_ref.shape).astype(out_ref.dtype)
        return

    label_index = labels_ref[...]
    labels = (label_index + 1).astype(jnp.float32)
    ahead_masks = [(sh.ahead(d, labels, None) == labels).astype(jnp.float32) for d in range(4)]
    behind_masks = [(sh.behind(d, labels, None) == labels).astype(jnp.float32) for d in range(4)]
    member_bool = label_index[None] == lax.broadcasted_iota(jnp.int32, (AGG, 1, 1), 0)
    member = member_bool.astype(jnp.float32)
    site_colour = jnp.zeros((rows, lanes), jnp.int32)
    for block in range(AGG):
        site_colour = jnp.where(label_index == block, colouring_ref[block], site_colour)
    colour_mask = (site_colour == colour_pass).astype(jnp.float32)

    def wilson_block(spinor):
        ahead_list = [sh.ahead(d, spinor, None) * ahead_masks[d] for d in range(4)]
        behind_list = [sh.behind(d, spinor, None) * behind_masks[d] for d in range(4)]
        return hopping(spinor, links, back_links, ahead_list, behind_list)

    def block_total(values):
        return jnp.sum(jnp.sum(member * values[None], axis=2, keepdims=True), axis=1, keepdims=True)

    update = None
    remainder = residue
    for repeat in range(MR_STEPS):
        image = wilson_block(remainder)
        image_flat = image.reshape(2, 12, rows, lanes)
        rest_flat = remainder.reshape(2, 12, rows, lanes)
        dot_real = jnp.sum(image_flat[0] * rest_flat[0] + image_flat[1] * rest_flat[1], axis=0)
        dot_imag = jnp.sum(image_flat[0] * rest_flat[1] - image_flat[1] * rest_flat[0], axis=0)
        norm = jnp.sum(image_flat[0] * image_flat[0] + image_flat[1] * image_flat[1], axis=0)
        denominator = block_total(norm) + 1e-06
        factor_real = jnp.sum(member * (block_total(dot_real) / denominator), axis=0)
        factor_imag = jnp.sum(member * (block_total(dot_imag) / denominator), axis=0)
        step = complex_scale(factor_real, factor_imag, remainder)
        update = step if update is None else update + step
        remainder = remainder - complex_scale(factor_real, factor_imag, image)
    update = update * colour_mask
    result = update if current is None else current + update
    out_ref[...] = result.reshape(out_ref.shape)
    if link_face_scratch is not None:
        link_face_scratch[...] = link_all[2]
    for name, face_ref in face_refs.items():
        if name == "y_low":
            face_ref[...] = out_ref[:, :, pl.ds(0, lanes // 2)]
        elif name == "y_high":
            face_ref[0:width] = pltpu.roll(out_ref[...], lanes // 2, 2)[:, :, : lanes // 2]
            if append_links:
                face_ref[width:] = pltpu.roll(link_all[1], lanes // 2, 2)[:, :, : lanes // 2]
        else:
            start, stride = face_rows(name)
            face_ref[0:width] = out_ref[:, pl.ds(start, 4, stride=stride), :]
            if append_links and name == "z_high":
                face_ref[width:] = link_face_scratch[:, pl.ds(start, 4, stride=stride), :]
            elif append_links and name == "t_high":
                face_ref[width:] = link_all[3][:, start:start + 4, :]


def run_pass(source, links, back, labels, colouring, colour_pass, spinor, halos, residual_only=False, faces=(),
             link_mode="given", append_links=False, emit_back=False):
    first = spinor is None
    present = {
        "ahead": [h is not None for h in halos["ahead"]] if not first else [False] * 4,
        "behind": [h is not None for h in halos["behind"]] if not first else [False] * 4,
    }
    operands = [source, links] + ([back] if link_mode == "given" else []) + [labels]
    spaces = [pltpu.VMEM] * len(operands)
    if not residual_only:
        operands.append(colouring)
        spaces.append(pltpu.SMEM)
    if not first:
        operands.append(spinor)
        for key in HALO_KEYS:
            if present[key[0]][key[1]]:
                operands.append(halos[key[0]][key[1]])
    spaces += [pltpu.VMEM] * (len(operands) - len(spaces))
    kernel = functools.partial(
        pass_kernel, first=first, residual_only=residual_only, present=present, faces=faces,
        link_mode=link_mode, append_links=append_links, emit_back=emit_back, colour_pass=colour_pass,
    )
    width = source.shape[0]

    def face_shape(name):
        rows = width + (18 if append_links and name.endswith("high") else 0)
        if name.startswith("y"):
            return (rows, source.shape[1], source.shape[2] // 2)
        return (rows, 4, source.shape[2])

    out_shape = [jax.ShapeDtypeStruct(source.shape, jnp.bfloat16 if residual_only else jnp.float32)]
    out_shape += [jax.ShapeDtypeStruct(face_shape(name), jnp.float32) for name in faces]
    if emit_back:
        out_shape.append(jax.ShapeDtypeStruct(links.shape, links.dtype))
    scratch = [pltpu.VMEM(source.shape, jnp.float32) for k in HALO_KEYS if present[k[0]][k[1]]]
    if link_mode == "combined":
        scratch += [pltpu.VMEM(links.shape[1:], jnp.float32) for d in (1, 2, 3) if present["behind"][d]]
    if append_links and "z_high" in faces:
        scratch.append(pltpu.VMEM(links.shape[1:], jnp.float32))
    in_specs = [pl.BlockSpec(memory_space=space) for space in spaces]
    results = pl.pallas_call(kernel, out_shape=out_shape, scratch_shapes=scratch, in_specs=in_specs)(*operands)
    face_values = dict(zip(faces, results[1:1 + len(faces)]))
    return results[0], face_values, (results[-1] if emit_back else None)


def coarse_kernel(*refs, present):
    refs = list(refs)
    out_ref = refs.pop()
    source_ref, inverse_ref = refs[0], refs[1]
    first = len(refs) == 2
    width = source_ref.shape[-1]
    chunks = width // 128
    lane = lax.broadcasted_iota(jnp.int32, (1, width), 1)
    position = lane % AGG
    selector = (
        lax.broadcasted_iota(jnp.int32, (8, 128), 1) // AGG == lax.broadcasted_iota(jnp.int32, (8, 128), 0)
    ).astype(jnp.float32)

    def reduce_flat(product):
        partial = product[:, 0:128]
        for q in range(1, chunks):
            partial = partial + product[:, q * 128:(q + 1) * 128]
        for shift in (64, 32, 16):
            partial = partial + pltpu.roll(partial, shift, 1)
        pieces = [
            jnp.sum(partial[8 * q:8 * q + 8] * selector, axis=0, keepdims=True) for q in range(chunks)
        ]
        return jnp.concatenate(pieces, axis=1)

    def roll_within(vector, shift):
        pieces = [pltpu.roll(vector[:, q * 128:(q + 1) * 128], shift % 128, 1) for q in range(chunks)]
        return jnp.concatenate(pieces, axis=1)

    def accumulate(acc, blocks_ref, index, vector):
        block_real = blocks_ref[index + (0,)].astype(jnp.float32)
        block_imag = blocks_ref[index + (1,)].astype(jnp.float32)
        real_part = block_real * vector[0] - block_imag * vector[1]
        imag_part = block_real * vector[1] + block_imag * vector[0]
        if acc is None:
            return [real_part, imag_part]
        return [acc[0] + real_part, acc[1] + imag_part]

    def precondition(vector):
        acc = accumulate(None, inverse_ref, (), vector)
        return [reduce_flat(acc[0]), reduce_flat(acc[1])]

    source = [source_ref[0], source_ref[1]]
    if first:
        result = precondition(source)
    else:
        operator_ref, current_ref = refs[2], refs[3]
        nearby_refs = refs[4:]
        current = [current_ref[0], current_ref[1]]
        ahead = [
            jnp.where(position == AGG - 1, roll_within(c, AGG - 1), roll_within(c, -1)) for c in current
        ]
        behind = [jnp.where(position == 0, roll_within(c, 1 - AGG), roll_within(c, 1)) for c in current]
        vectors = [current, ahead, behind]
        taken = 0
        for flag in present:
            if flag:
                vectors.append([nearby_refs[taken][0], nearby_refs[taken][1]])
                taken += 1
            else:
                vectors.append(None)
        acc = None
        for direction, vector in enumerate(vectors):
            if vector is not None:
                acc = accumulate(acc, operator_ref, (direction,), vector)
        residue = [source[0] - reduce_flat(acc[0]), source[1] - reduce_flat(acc[1])]
        step = precondition(residue)
        result = [current[0] + step[0], current[1] + step[1]]
    out_ref[0] = result[0]
    out_ref[1] = result[1]


def run_coarse(source, inverse_blocks, operator_blocks, current, nearby):
    operands = [source, inverse_blocks]
    present = ()
    if current is not None:
        present = tuple(v is not None for v in nearby)
        operands += [operator_blocks, current] + [v for v in nearby if v is not None]
    kernel = functools.partial(coarse_kernel, present=present)
    return pl.pallas_call(kernel, out_shape=jax.ShapeDtypeStruct(source.shape, jnp.float32))(*operands)


def body(
    fine_source, links, test_vectors, aggregate_map, colouring, coarse_operator, block_inverse
):
    time_extent = fine_source.shape[2]
    plane_extent = fine_source.shape[3]
    line_extent = fine_source.shape[4]
    rows = time_extent * plane_extent
    site_count = rows * line_extent
    domain_index = lax.axis_index("lat")
    domain_count = lax.axis_size("lat")
    plane_position = (domain_index + 2) % PZ
    upper_valid = plane_position < PZ - 1
    lower_valid = plane_position > 0
    later_valid = domain_index < domain_count - PZ
    earlier_valid = domain_index >= PZ

    source = fine_source.reshape(24, rows, line_extent)
    link_rows = links.reshape(4, 18, rows, line_extent)
    label_rows = aggregate_map.reshape(rows, line_extent)
    member = (label_rows[None] == jnp.arange(AGG, dtype=jnp.int32)[:, None, None]).astype(jnp.float32)
    colour_list = colouring.reshape(AGG)

    def z_up_ok(i):
        return (i + 2) % PZ != PZ - 1

    def z_down_ok(i):
        return (i + 2) % PZ != 0

    def t_up_ok(i):
        return i + PZ < domain_count

    def t_down_ok(i):
        return i - PZ >= 0

    half = line_extent // 2

    needed = ["y_low", "y_high"] + [
        name for name, ok in zip(FACES[2:], (z_up_ok, z_down_ok, t_up_ok, t_down_ok))
        if any(ok(i) for i in range(domain_count))
    ]

    def faces_of(spinor):
        result = {"y_low": spinor[..., :half], "y_high": spinor[..., half:]}
        for name in needed[2:]:
            start, stride = face_rows(name)
            result[name] = lax.slice_in_dim(spinor, start, start + 3 * stride + 1, stride, axis=1)
        return result

    def halos_of(spinor, faces):
        def face(name):
            return faces[name] if name in faces else None

        return {
            "ahead": [
                None,
                permute_from(faces["y_low"], "grp", 1, lambda i: True),
                permute_from(face("z_low"), "lat", 1, z_up_ok) if face("z_low") is not None else None,
                permute_from(face("t_low"), "lat", PZ, t_up_ok) if face("t_low") is not None else None,
            ],
            "behind": [
                None,
                permute_from(faces["y_high"], "grp", -1, lambda i: True),
                permute_from(face("z_high"), "lat", -1, z_down_ok) if face("z_high") is not None else None,
                permute_from(face("t_high"), "lat", -PZ, t_down_ok) if face("t_high") is not None else None,
            ],
        }

    smoothed_first, first_faces, _ = run_pass(
        source, link_rows, None, label_rows, colour_list, 0, None, None,
        faces=tuple(needed), link_mode="none", append_links=True,
    )
    smoothed, smoothed_faces, back_rows = run_pass(
        source, link_rows, None, label_rows, colour_list, 1, smoothed_first,
        halos_of(smoothed_first, first_faces), faces=tuple(needed), link_mode="combined", emit_back=True,
    )

    def sweep(start, faces):
        current, current_faces, _ = run_pass(
            source, link_rows, back_rows, label_rows, colour_list, 0, start, halos_of(start, faces),
            faces=tuple(needed),
        )
        result, _, _ = run_pass(
            source, link_rows, back_rows, label_rows, colour_list, 1, current,
            halos_of(current, current_faces),
        )
        return result

    residue, _, _ = run_pass(
        source, link_rows, back_rows, label_rows, None, None, smoothed, halos_of(smoothed, smoothed_faces),
        residual_only=True,
    )
    residual = residue
    membership = member.reshape(AGG, site_count).T
    member_weights = membership.astype(jnp.bfloat16)
    weighted = residual.reshape(2, 2, 6, site_count)[..., None] * member_weights
    vectors = test_vectors.reshape(NVEC, 2, 2, 6, site_count)

    def contract(left, right):
        return jnp.einsum("kxqn,xqnj->xkj", left, right, preferred_element_type=jnp.float32)

    real_part = contract(vectors[:, 0], weighted[0]) + contract(vectors[:, 1], weighted[1])
    imag_part = contract(vectors[:, 0], weighted[1]) - contract(vectors[:, 1], weighted[0])
    coarse_source = jnp.stack([real_part, imag_part]).reshape(2, CDOF, AGG)
    flat_source = coarse_source.reshape(2, 1, CDOF * AGG)
    operator_blocks = coarse_operator.reshape(9, 2, CDOF, CDOF * AGG)
    inverse_blocks = block_inverse.reshape(2, CDOF, CDOF * AGG)
    correction = run_coarse(flat_source, inverse_blocks, operator_blocks, None, None)
    for repeat in range(2):
        nearby = [
            permute_from(correction, "grp", 1, lambda i: True),
            permute_from(correction, "grp", -1, lambda i: True),
            permute_from(correction, "lat", 1, z_up_ok),
            permute_from(correction, "lat", -1, z_down_ok),
            permute_from(correction, "lat", PZ, t_up_ok),
            permute_from(correction, "lat", -PZ, t_down_ok),
        ]
        correction = run_coarse(flat_source, inverse_blocks, operator_blocks, correction, nearby)
    correction = correction.reshape(2, CDOF, AGG)
    expanded = jnp.dot(
        correction.reshape(2 * CDOF, AGG), membership.T, precision=lax.Precision.HIGHEST
    ).reshape(2, 2, NVEC, site_count)
    spread_real = jnp.swapaxes(expanded[0], 0, 1)[:, :, None]
    spread_imag = jnp.swapaxes(expanded[1], 0, 1)[:, :, None]
    real_part = jnp.sum(vectors[:, 0] * spread_real - vectors[:, 1] * spread_imag, axis=0)
    imag_part = jnp.sum(vectors[:, 0] * spread_imag + vectors[:, 1] * spread_real, axis=0)
    corrected = smoothed + jnp.stack([real_part, imag_part]).reshape(24, rows, line_extent)
    solution = sweep(corrected, faces_of(corrected))
    return (
        solution.reshape(1, 24, time_extent, plane_extent, line_extent),
        correction.reshape(1, 1, 2, CDOF, AGG),
    )


def solution(mesh):
    return jax.shard_map(
        body,
        mesh=mesh,
        in_specs=(
            P("lat", None, None, None, "grp"),
            P("lat", None, None, None, None, "grp"),
            P("lat", None, None, None, None, "grp"),
            P("lat", None, None, "grp", None),
            P("lat", "grp", None),
            P("lat", "grp", None, None, None, None),
            P("lat", "grp", None, None, None),
        ),
        out_specs=(P("lat", None, None, None, "grp"), P("lat", "grp", None, None, None)),
        check_vma=False,
    )
```

```python
import functools

import jax
import jax.numpy as jnp
from jax import lax
from jax.experimental import pallas as pl
from jax.experimental.pallas import tpu as pltpu
from jax.sharding import PartitionSpec as P

CX = 64
PZ = 8
NVEC = 24
AGG = 16
MR_STEPS = 2
CDOF = 48


def passed_along(shard, axis, by):
    size = lax.axis_size(axis)
    return lax.ppermute(shard, axis, [(i, (i + by) % size) for i in range(size)])


def padded_2(shard, sides, width):
    for axis, dim in sides:
        size, length = (lax.axis_size(axis), shard.shape[dim])
        up = [(i, (i + 1) % size) for i in range(size)]
        down = [(j, i) for i, j in up]
        last = lax.slice_in_dim(shard, length - width, length, axis=dim)
        first = lax.slice_in_dim(shard, 0, width, axis=dim)
        before = lax.ppermute(last, axis, up)
        after = lax.ppermute(first, axis, down)
        shard = jnp.concatenate([before, shard, after], axis=dim)
    return shard


def times_minus_i(values):
    return jnp.stack([values[1], -values[0]])


def times_plus_i(values):
    return jnp.stack([-values[1], values[0]])


def spin_factor(direction, spin_pair):
    if direction == 0:
        return jnp.stack([times_minus_i(spin_pair[:, 1]), times_minus_i(spin_pair[:, 0])], axis=1)
    if direction == 1:
        return jnp.stack([-spin_pair[:, 1], spin_pair[:, 0]], axis=1)
    if direction == 2:
        return jnp.stack([times_minus_i(spin_pair[:, 0]), times_plus_i(spin_pair[:, 1])], axis=1)
    return spin_pair


def project_minus(direction, spinor):
    return spinor[:, :2] - spin_factor(direction, spinor[:, 2:])


def project_plus(direction, spinor):
    return spinor[:, :2] + spin_factor(direction, spinor[:, 2:])


def rebuild_minus(direction, half_spinor):
    lower_part = spin_factor(direction, half_spinor) if direction < 3 else -half_spinor
    return jnp.concatenate([half_spinor, lower_part], axis=1)


def rebuild_plus(direction, half_spinor):
    lower_part = -spin_factor(direction, half_spinor) if direction < 3 else half_spinor
    return jnp.concatenate([half_spinor, lower_part], axis=1)


def colour_product(gauge_link, half_spinor, adjoint):
    link_real = gauge_link[0]
    link_imag = gauge_link[1]
    if adjoint:
        link_real = jnp.swapaxes(link_real, 0, 1)
        link_imag = -jnp.swapaxes(link_imag, 0, 1)
    spin_real = half_spinor[0][:, None]
    spin_imag = half_spinor[1][:, None]
    real_part = jnp.sum(link_real[None] * spin_real - link_imag[None] * spin_imag, axis=2)
    imag_part = jnp.sum(link_real[None] * spin_imag + link_imag[None] * spin_real, axis=2)
    return jnp.stack([real_part, imag_part])


def complex_scale(factor_real, factor_imag, lattice):
    return jnp.stack(
        [
            factor_real * lattice[0] - factor_imag * lattice[1],
            factor_real * lattice[1] + factor_imag * lattice[0],
        ]
    )


def apply_blocks(blocks, nearby):
    matrices = blocks.reshape(blocks.shape[0], 2, CDOF, CDOF, AGG)
    vector_real = nearby[:, 0][:, None]
    vector_imag = nearby[:, 1][:, None]
    real_part = jnp.sum(matrices[:, 0] * vector_real - matrices[:, 1] * vector_imag, axis=(0, 2))
    imag_part = jnp.sum(matrices[:, 0] * vector_imag + matrices[:, 1] * vector_real, axis=(0, 2))
    return jnp.stack([real_part, imag_part])


def keep_if(allowed, values):
    return jnp.where(allowed, values, jnp.zeros_like(values))


def permute_from(value, axis, offset, allowed):
    size = lax.axis_size(axis)
    pairs = [((i + offset) % size, i) for i in range(size) if allowed(i)]
    if not pairs:
        return None
    return lax.ppermute(value, axis, pairs)


class Shifts:
    def __init__(self, rows, lanes):
        self.rows = rows
        self.lanes = lanes
        self.lane = lax.broadcasted_iota(jnp.int32, (rows, lanes), 1)
        self.row = lax.broadcasted_iota(jnp.int32, (rows, lanes), 0)
        self.xpos = self.lane % CX
        self.zpos = self.row % 4

    def roll(self, a, shift, axis):
        n = a.shape[axis]
        return pltpu.roll(a, shift % n, a.ndim + axis)

    def ahead(self, direction, a, nbr, placed=False):
        if direction == 0:
            return jnp.where(self.xpos == CX - 1, self.roll(a, CX - 1, -1), self.roll(a, -1, -1))
        if direction == 1:
            half = self.lanes // 2
            if placed and nbr is not None:
                return jnp.where(self.lane >= half, self.roll(nbr, half, -1), self.roll(a, half, -1))
            filled = jnp.where(self.lane < half, 0.0 if nbr is None else nbr, a)
            return self.roll(filled, half, -1)
        if direction == 2:
            inner = self.roll(a, -1, -2)
            outer = 0.0 if nbr is None else (nbr if placed else self.roll(nbr, 3, -2))
            return jnp.where(self.zpos == 3, outer, inner)
        filled = jnp.where(self.row < 4, 0.0 if nbr is None else nbr, a)
        return self.roll(filled, -4, -2)

    def behind(self, direction, a, nbr, placed=False):
        if direction == 0:
            return jnp.where(self.xpos == 0, self.roll(a, 1 - CX, -1), self.roll(a, 1, -1))
        if direction == 1:
            half = self.lanes // 2
            if placed and nbr is not None:
                return jnp.where(self.lane < half, nbr, self.roll(a, half, -1))
            filled = jnp.where(self.lane >= half, 0.0 if nbr is None else nbr, a)
            return self.roll(filled, half, -1)
        if direction == 2:
            inner = self.roll(a, 1, -2)
            outer = 0.0 if nbr is None else (nbr if placed else self.roll(nbr, -3, -2))
            return jnp.where(self.zpos == 0, outer, inner)
        filled = jnp.where(self.row >= self.rows - 4, 0.0 if nbr is None else nbr, a)
        return self.roll(filled, 4, -2)


def hopping(spinor, links, back_links, ahead_list, behind_list):
    hop_total = None
    for direction in range(4):
        ahead_half = colour_product(links[direction], project_minus(direction, ahead_list[direction]), False)
        behind_half = colour_product(back_links[direction], project_plus(direction, behind_list[direction]), True)
        term = rebuild_minus(direction, ahead_half) + rebuild_plus(direction, behind_half)
        hop_total = term if hop_total is None else hop_total + term
    return 4.5 * spinor - 0.5 * hop_total


FACES = ("y_low", "y_high", "z_low", "z_high", "t_low", "t_high")
HALO_KEYS = tuple((side, d) for d in (1, 2, 3) for side in ("ahead", "behind"))


def face_rows(name):
    return {"z_low": (0, 4), "z_high": (3, 4), "t_low": (0, 1), "t_high": (12, 1)}[name]


def place(scratch, value, side, direction):
    if direction == 1:
        scratch[..., pl.ds(0, value.shape[-1])] = value
        return
    start, stride = {("ahead", 2): (3, 4), ("behind", 2): (0, 4), ("ahead", 3): (0, 1), ("behind", 3): (12, 1)}[
        (side, direction)
    ]
    scratch[:, pl.ds(start, 4, stride=stride), :] = value


def pass_kernel(*refs, first, residual_only, present, faces, link_mode, append_links, emit_back, colour_pass):
    refs = list(refs)
    width = 24
    ghost_dirs = [d for d in (1, 2, 3) if link_mode == "combined" and present["behind"][d]]
    link_face_scratch = refs.pop() if append_links and "z_high" in faces else None
    ghost_scratch = {}
    for direction in reversed(ghost_dirs):
        ghost_scratch[direction] = refs.pop()
    scratch_refs = {}
    for key in reversed([k for k in HALO_KEYS if present[k[0]][k[1]]]):
        scratch_refs[key] = refs.pop()
    back_out_ref = refs.pop() if emit_back else None
    face_refs = {}
    for name in reversed(faces):
        face_refs[name] = refs.pop()
    out_ref = refs.pop()

    def take():
        return refs.pop(0)

    src_ref = take()
    links_ref = take()
    back_ref = take() if link_mode == "given" else None
    labels_ref = take()
    colouring_ref = None if residual_only else take()
    spinor_ref = None
    halo_refs = {}
    if not first:
        spinor_ref = take()
        for key in HALO_KEYS:
            if present[key[0]][key[1]]:
                halo_refs[key] = take()

    rows, lanes = src_ref.shape[-2], src_ref.shape[-1]
    sh = Shifts(rows, lanes)
    shape = (2, 4, 3, rows, lanes)
    source = src_ref[...].reshape(shape)
    link_all = links_ref[...].astype(jnp.float32)
    links = [link_all[d].reshape(2, 3, 3, rows, lanes) for d in range(4)]
    if back_ref is not None:
        back_all = back_ref[...].astype(jnp.float32)
        back_links = [back_all[d].reshape(2, 3, 3, rows, lanes) for d in range(4)]
    else:
        back_links = []
        for direction in range(4):
            ghost = None
            if direction in ghost_scratch:
                halo = halo_refs[("behind", direction)]
                place(ghost_scratch[direction], halo[width:], "behind", direction)
                ghost = ghost_scratch[direction][...].reshape(2, 3, 3, rows, lanes)
            back_links.append(sh.behind(direction, links[direction], ghost, True))
    if back_out_ref is not None:
        for direction in range(4):
            back_out_ref[direction] = back_links[direction].reshape(18, rows, lanes).astype(back_out_ref.dtype)

    for key, scratch in scratch_refs.items():
        halo = halo_refs[key]
        value = halo[:width] if (key[0] == "behind" and key[1] in ghost_scratch) else halo[...]
        place(scratch, value, key[0], key[1])

    def load_halo(side, direction):
        ref = scratch_refs.get((side, direction), halo_refs.get((side, direction)))
        return None if ref is None else ref[...].reshape(shape)

    def wilson_global(spinor):
        ahead_list = [sh.ahead(d, spinor, load_halo("ahead", d), True) for d in range(4)]
        behind_list = [sh.behind(d, spinor, load_halo("behind", d), True) for d in range(4)]
        return hopping(spinor, links, back_links, ahead_list, behind_list)

    if first:
        residue = source
        current = None
    else:
        current = spinor_ref[...].reshape(shape)
        residue = source - wilson_global(current)
    if residual_only:
        out_ref[...] = residue.reshape(out_ref.shape).astype(out_ref.dtype)
        return

    label_index = labels_ref[...]
    labels = (label_index + 1).astype(jnp.float32)
    ahead_masks = [(sh.ahead(d, labels, None) == labels).astype(jnp.float32) for d in range(4)]
    behind_masks = [(sh.behind(d, labels, None) == labels).astype(jnp.float32) for d in range(4)]
    member_bool = label_index[None] == lax.broadcasted_iota(jnp.int32, (AGG, 1, 1), 0)
    member = member_bool.astype(jnp.float32)
    site_colour = jnp.zeros((rows, lanes), jnp.int32)
    for block in range(AGG):
        site_colour = jnp.where(label_index == block, colouring_ref[block], site_colour)
    colour_mask = (site_colour == colour_pass).astype(jnp.float32)

    def wilson_block(spinor):
        ahead_list = [sh.ahead(d, spinor, None) * ahead_masks[d] for d in range(4)]
        behind_list = [sh.behind(d, spinor, None) * behind_masks[d] for d in range(4)]
        return hopping(spinor, links, back_links, ahead_list, behind_list)

    def block_total(values):
        return jnp.sum(jnp.sum(member * values[None], axis=2, keepdims=True), axis=1, keepdims=True)

    update = None
    remainder = residue
    for repeat in range(MR_STEPS):
        image = wilson_block(remainder)
        image_flat = image.reshape(2, 12, rows, lanes)
        rest_flat = remainder.reshape(2, 12, rows, lanes)
        dot_real = jnp.sum(image_flat[0] * rest_flat[0] + image_flat[1] * rest_flat[1], axis=0)
        dot_imag = jnp.sum(image_flat[0] * rest_flat[1] - image_flat[1] * rest_flat[0], axis=0)
        norm = jnp.sum(image_flat[0] * image_flat[0] + image_flat[1] * image_flat[1], axis=0)
        denominator = block_total(norm) + 1e-06
        factor_real = jnp.sum(member * (block_total(dot_real) / denominator), axis=0)
        factor_imag = jnp.sum(member * (block_total(dot_imag) / denominator), axis=0)
        step = complex_scale(factor_real, factor_imag, remainder)
        update = step if update is None else update + step
        remainder = remainder - complex_scale(factor_real, factor_imag, image)
    update = update * colour_mask
    result = update if current is None else current + update
    out_ref[...] = result.reshape(out_ref.shape)
    if link_face_scratch is not None:
        link_face_scratch[...] = link_all[2]
    for name, face_ref in face_refs.items():
        if name == "y_low":
            face_ref[...] = out_ref[:, :, pl.ds(0, lanes // 2)]
        elif name == "y_high":
            face_ref[0:width] = pltpu.roll(out_ref[...], lanes // 2, 2)[:, :, : lanes // 2]
            if append_links:
                face_ref[width:] = pltpu.roll(link_all[1], lanes // 2, 2)[:, :, : lanes // 2]
        else:
            start, stride = face_rows(name)
            face_ref[0:width] = out_ref[:, pl.ds(start, 4, stride=stride), :]
            if append_links and name == "z_high":
                face_ref[width:] = link_face_scratch[:, pl.ds(start, 4, stride=stride), :]
            elif append_links and name == "t_high":
                face_ref[width:] = link_all[3][:, start:start + 4, :]


def run_pass(source, links, back, labels, colouring, colour_pass, spinor, halos, residual_only=False, faces=(),
             link_mode="given", append_links=False, emit_back=False):
    first = spinor is None
    present = {
        "ahead": [h is not None for h in halos["ahead"]] if not first else [False] * 4,
        "behind": [h is not None for h in halos["behind"]] if not first else [False] * 4,
    }
    operands = [source, links] + ([back] if link_mode == "given" else []) + [labels]
    spaces = [pltpu.VMEM] * len(operands)
    if not residual_only:
        operands.append(colouring)
        spaces.append(pltpu.SMEM)
    if not first:
        operands.append(spinor)
        for key in HALO_KEYS:
            if present[key[0]][key[1]]:
                operands.append(halos[key[0]][key[1]])
    spaces += [pltpu.VMEM] * (len(operands) - len(spaces))
    kernel = functools.partial(
        pass_kernel, first=first, residual_only=residual_only, present=present, faces=faces,
        link_mode=link_mode, append_links=append_links, emit_back=emit_back, colour_pass=colour_pass,
    )
    width = source.shape[0]

    def face_shape(name):
        rows = width + (18 if append_links and name.endswith("high") else 0)
        if name.startswith("y"):
            return (rows, source.shape[1], source.shape[2] // 2)
        return (rows, 4, source.shape[2])

    out_shape = [jax.ShapeDtypeStruct(source.shape, jnp.bfloat16 if residual_only else jnp.float32)]
    out_shape += [jax.ShapeDtypeStruct(face_shape(name), jnp.float32) for name in faces]
    if emit_back:
        out_shape.append(jax.ShapeDtypeStruct(links.shape, links.dtype))
    scratch = [pltpu.VMEM(source.shape, jnp.float32) for k in HALO_KEYS if present[k[0]][k[1]]]
    if link_mode == "combined":
        scratch += [pltpu.VMEM(links.shape[1:], jnp.float32) for d in (1, 2, 3) if present["behind"][d]]
    if append_links and "z_high" in faces:
        scratch.append(pltpu.VMEM(links.shape[1:], jnp.float32))
    in_specs = [pl.BlockSpec(memory_space=space) for space in spaces]
    results = pl.pallas_call(kernel, out_shape=out_shape, scratch_shapes=scratch, in_specs=in_specs)(*operands)
    face_values = dict(zip(faces, results[1:1 + len(faces)]))
    return results[0], face_values, (results[-1] if emit_back else None)


def coarse_kernel(*refs, present):
    refs = list(refs)
    out_ref = refs.pop()
    source_ref, inverse_ref = refs[0], refs[1]
    first = len(refs) == 2
    width = source_ref.shape[-1]
    chunks = width // 128
    lane = lax.broadcasted_iota(jnp.int32, (1, width), 1)
    position = lane % AGG
    selector = (
        lax.broadcasted_iota(jnp.int32, (8, 128), 1) // AGG == lax.broadcasted_iota(jnp.int32, (8, 128), 0)
    ).astype(jnp.float32)

    def reduce_flat(product):
        partial = product[:, 0:128]
        for q in range(1, chunks):
            partial = partial + product[:, q * 128:(q + 1) * 128]
        for shift in (64, 32, 16):
            partial = partial + pltpu.roll(partial, shift, 1)
        pieces = [
            jnp.sum(partial[8 * q:8 * q + 8] * selector, axis=0, keepdims=True) for q in range(chunks)
        ]
        return jnp.concatenate(pieces, axis=1)

    def roll_within(vector, shift):
        pieces = [pltpu.roll(vector[:, q * 128:(q + 1) * 128], shift % 128, 1) for q in range(chunks)]
        return jnp.concatenate(pieces, axis=1)

    def accumulate(acc, blocks_ref, index, vector):
        block_real = blocks_ref[index + (0,)].astype(jnp.float32)
        block_imag = blocks_ref[index + (1,)].astype(jnp.float32)
        real_part = block_real * vector[0] - block_imag * vector[1]
        imag_part = block_real * vector[1] + block_imag * vector[0]
        if acc is None:
            return [real_part, imag_part]
        return [acc[0] + real_part, acc[1] + imag_part]

    def precondition(vector):
        acc = accumulate(None, inverse_ref, (), vector)
        return [reduce_flat(acc[0]), reduce_flat(acc[1])]

    source = [source_ref[0], source_ref[1]]
    if first:
        result = precondition(source)
    else:
        operator_ref, current_ref = refs[2], refs[3]
        nearby_refs = refs[4:]
        current = [current_ref[0], current_ref[1]]
        ahead = [
            jnp.where(position == AGG - 1, roll_within(c, AGG - 1), roll_within(c, -1)) for c in current
        ]
        behind = [jnp.where(position == 0, roll_within(c, 1 - AGG), roll_within(c, 1)) for c in current]
        vectors = [current, ahead, behind]
        taken = 0
        for flag in present:
            if flag:
                vectors.append([nearby_refs[taken][0], nearby_refs[taken][1]])
                taken += 1
            else:
                vectors.append(None)
        acc = None
        for direction, vector in enumerate(vectors):
            if vector is not None:
                acc = accumulate(acc, operator_ref, (direction,), vector)
        residue = [source[0] - reduce_flat(acc[0]), source[1] - reduce_flat(acc[1])]
        step = precondition(residue)
        result = [current[0] + step[0], current[1] + step[1]]
    out_ref[0] = result[0]
    out_ref[1] = result[1]


def run_coarse(source, inverse_blocks, operator_blocks, current, nearby):
    operands = [source, inverse_blocks]
    present = ()
    if current is not None:
        present = tuple(v is not None for v in nearby)
        operands += [operator_blocks, current] + [v for v in nearby if v is not None]
    kernel = functools.partial(coarse_kernel, present=present)
    return pl.pallas_call(kernel, out_shape=jax.ShapeDtypeStruct(source.shape, jnp.float32))(*operands)


def body(
    fine_source, links, test_vectors, aggregate_map, colouring, coarse_operator, block_inverse
):
    time_extent = fine_source.shape[2]
    plane_extent = fine_source.shape[3]
    line_extent = fine_source.shape[4]
    rows = time_extent * plane_extent
    site_count = rows * line_extent
    domain_index = lax.axis_index("lat")
    domain_count = lax.axis_size("lat")
    plane_position = (domain_index + 2) % PZ
    upper_valid = plane_position < PZ - 1
    lower_valid = plane_position > 0
    later_valid = domain_index < domain_count - PZ
    earlier_valid = domain_index >= PZ

    source = fine_source.reshape(24, rows, line_extent)
    link_rows = links.reshape(4, 18, rows, line_extent)
    label_rows = aggregate_map.reshape(rows, line_extent)
    member = (label_rows[None] == jnp.arange(AGG, dtype=jnp.int32)[:, None, None]).astype(jnp.float32)
    colour_list = colouring.reshape(AGG)

    def z_up_ok(i):
        return (i + 2) % PZ != PZ - 1

    def z_down_ok(i):
        return (i + 2) % PZ != 0

    def t_up_ok(i):
        return i + PZ < domain_count

    def t_down_ok(i):
        return i - PZ >= 0

    half = line_extent // 2

    needed = ["y_low", "y_high"] + [
        name for name, ok in zip(FACES[2:], (z_up_ok, z_down_ok, t_up_ok, t_down_ok))
        if any(ok(i) for i in range(domain_count))
    ]

    def faces_of(spinor):
        result = {"y_low": spinor[..., :half], "y_high": spinor[..., half:]}
        for name in needed[2:]:
            start, stride = face_rows(name)
            result[name] = lax.slice_in_dim(spinor, start, start + 3 * stride + 1, stride, axis=1)
        return result

    def halos_of(spinor, faces):
        def face(name):
            return faces[name] if name in faces else None

        return {
            "ahead": [
                None,
                permute_from(faces["y_low"], "grp", 1, lambda i: True),
                permute_from(face("z_low"), "lat", 1, z_up_ok) if face("z_low") is not None else None,
                permute_from(face("t_low"), "lat", PZ, t_up_ok) if face("t_low") is not None else None,
            ],
            "behind": [
                None,
                permute_from(faces["y_high"], "grp", -1, lambda i: True),
                permute_from(face("z_high"), "lat", -1, z_down_ok) if face("z_high") is not None else None,
                permute_from(face("t_high"), "lat", -PZ, t_down_ok) if face("t_high") is not None else None,
            ],
        }

    smoothed_first, first_faces, _ = run_pass(
        source, link_rows, None, label_rows, colour_list, 0, None, None,
        faces=tuple(needed), link_mode="none", append_links=True,
    )
    vectors = test_vectors.reshape(NVEC, 2, 2, 6, site_count)
    vectors, smoothed_first = lax.optimization_barrier((vectors, smoothed_first))
    smoothed, smoothed_faces, back_rows = run_pass(
        source, link_rows, None, label_rows, colour_list, 1, smoothed_first,
        halos_of(smoothed_first, first_faces), faces=tuple(needed), link_mode="combined", emit_back=True,
    )

    def sweep(start, faces):
        current, current_faces, _ = run_pass(
            source, link_rows, back_rows, label_rows, colour_list, 0, start, halos_of(start, faces),
            faces=tuple(needed),
        )
        result, _, _ = run_pass(
            source, link_rows, back_rows, label_rows, colour_list, 1, current,
            halos_of(current, current_faces),
        )
        return result

    residue, _, _ = run_pass(
        source, link_rows, back_rows, label_rows, None, None, smoothed, halos_of(smoothed, smoothed_faces),
        residual_only=True,
    )
    residual = residue
    membership = member.reshape(AGG, site_count).T
    member_weights = membership.astype(jnp.bfloat16)
    weighted = residual.reshape(2, 2, 6, site_count)[..., None] * member_weights

    pairs = jnp.einsum("krxqn,sxqnj->rsxkj", vectors, weighted, preferred_element_type=jnp.float32)
    real_part = pairs[0, 0] + pairs[1, 1]
    imag_part = pairs[0, 1] - pairs[1, 0]
    coarse_source = jnp.stack([real_part, imag_part]).reshape(2, CDOF, AGG)
    flat_source = coarse_source.reshape(2, 1, CDOF * AGG)
    operator_blocks = coarse_operator.reshape(9, 2, CDOF, CDOF * AGG)
    inverse_blocks = block_inverse.reshape(2, CDOF, CDOF * AGG)
    correction = run_coarse(flat_source, inverse_blocks, operator_blocks, None, None)
    for repeat in range(2):
        nearby = [
            permute_from(correction, "grp", 1, lambda i: True),
            permute_from(correction, "grp", -1, lambda i: True),
            permute_from(correction, "lat", 1, z_up_ok),
            permute_from(correction, "lat", -1, z_down_ok),
            permute_from(correction, "lat", PZ, t_up_ok),
            permute_from(correction, "lat", -PZ, t_down_ok),
        ]
        correction = run_coarse(flat_source, inverse_blocks, operator_blocks, correction, nearby)
    correction = correction.reshape(2, CDOF, AGG)
    expanded = jnp.dot(
        correction.reshape(2 * CDOF, AGG), membership.T, precision=lax.Precision.HIGHEST
    ).reshape(2, 2, NVEC, site_count)
    spread_real = jnp.swapaxes(expanded[0], 0, 1)[:, :, None]
    spread_imag = jnp.swapaxes(expanded[1], 0, 1)[:, :, None]
    real_part = jnp.sum(vectors[:, 0] * spread_real - vectors[:, 1] * spread_imag, axis=0)
    imag_part = jnp.sum(vectors[:, 0] * spread_imag + vectors[:, 1] * spread_real, axis=0)
    corrected = smoothed + jnp.stack([real_part, imag_part]).reshape(24, rows, line_extent)
    solution = sweep(corrected, faces_of(corrected))
    return (
        solution.reshape(1, 24, time_extent, plane_extent, line_extent),
        correction.reshape(1, 1, 2, CDOF, AGG),
    )


def solution(mesh):
    return jax.shard_map(
        body,
        mesh=mesh,
        in_specs=(
            P("lat", None, None, None, "grp"),
            P("lat", None, None, None, None, "grp"),
            P("lat", None, None, None, None, "grp"),
            P("lat", None, None, "grp", None),
            P("lat", "grp", None),
            P("lat", "grp", None, None, None, None),
            P("lat", "grp", None, None, None),
        ),
        out_specs=(P("lat", None, None, None, "grp"), P("lat", "grp", None, None, None)),
        check_vma=False,
    )
```

```python
import functools

import jax
import jax.numpy as jnp
from jax import lax
from jax.experimental import pallas as pl
from jax.experimental.pallas import tpu as pltpu
from jax.sharding import PartitionSpec as P

CX = 64
PZ = 8
NVEC = 24
AGG = 16
MR_STEPS = 2
CDOF = 48


def passed_along(shard, axis, by):
    size = lax.axis_size(axis)
    return lax.ppermute(shard, axis, [(i, (i + by) % size) for i in range(size)])


def padded_2(shard, sides, width):
    for axis, dim in sides:
        size, length = (lax.axis_size(axis), shard.shape[dim])
        up = [(i, (i + 1) % size) for i in range(size)]
        down = [(j, i) for i, j in up]
        last = lax.slice_in_dim(shard, length - width, length, axis=dim)
        first = lax.slice_in_dim(shard, 0, width, axis=dim)
        before = lax.ppermute(last, axis, up)
        after = lax.ppermute(first, axis, down)
        shard = jnp.concatenate([before, shard, after], axis=dim)
    return shard


def times_minus_i(values):
    return jnp.stack([values[1], -values[0]])


def times_plus_i(values):
    return jnp.stack([-values[1], values[0]])


def spin_factor(direction, spin_pair):
    if direction == 0:
        return jnp.stack([times_minus_i(spin_pair[:, 1]), times_minus_i(spin_pair[:, 0])], axis=1)
    if direction == 1:
        return jnp.stack([-spin_pair[:, 1], spin_pair[:, 0]], axis=1)
    if direction == 2:
        return jnp.stack([times_minus_i(spin_pair[:, 0]), times_plus_i(spin_pair[:, 1])], axis=1)
    return spin_pair


def project_minus(direction, spinor):
    return spinor[:, :2] - spin_factor(direction, spinor[:, 2:])


def project_plus(direction, spinor):
    return spinor[:, :2] + spin_factor(direction, spinor[:, 2:])


def rebuild_minus(direction, half_spinor):
    lower_part = spin_factor(direction, half_spinor) if direction < 3 else -half_spinor
    return jnp.concatenate([half_spinor, lower_part], axis=1)


def rebuild_plus(direction, half_spinor):
    lower_part = -spin_factor(direction, half_spinor) if direction < 3 else half_spinor
    return jnp.concatenate([half_spinor, lower_part], axis=1)


def colour_product(gauge_link, half_spinor, adjoint):
    link_real = gauge_link[0]
    link_imag = gauge_link[1]
    if adjoint:
        link_real = jnp.swapaxes(link_real, 0, 1)
        link_imag = -jnp.swapaxes(link_imag, 0, 1)
    spin_real = half_spinor[0][:, None]
    spin_imag = half_spinor[1][:, None]
    real_part = jnp.sum(link_real[None] * spin_real - link_imag[None] * spin_imag, axis=2)
    imag_part = jnp.sum(link_real[None] * spin_imag + link_imag[None] * spin_real, axis=2)
    return jnp.stack([real_part, imag_part])


def complex_scale(factor_real, factor_imag, lattice):
    return jnp.stack(
        [
            factor_real * lattice[0] - factor_imag * lattice[1],
            factor_real * lattice[1] + factor_imag * lattice[0],
        ]
    )


def apply_blocks(blocks, nearby):
    matrices = blocks.reshape(blocks.shape[0], 2, CDOF, CDOF, AGG)
    vector_real = nearby[:, 0][:, None]
    vector_imag = nearby[:, 1][:, None]
    real_part = jnp.sum(matrices[:, 0] * vector_real - matrices[:, 1] * vector_imag, axis=(0, 2))
    imag_part = jnp.sum(matrices[:, 0] * vector_imag + matrices[:, 1] * vector_real, axis=(0, 2))
    return jnp.stack([real_part, imag_part])


def keep_if(allowed, values):
    return jnp.where(allowed, values, jnp.zeros_like(values))


def permute_from(value, axis, offset, allowed):
    size = lax.axis_size(axis)
    pairs = [((i + offset) % size, i) for i in range(size) if allowed(i)]
    if not pairs:
        return None
    return lax.ppermute(value, axis, pairs)


class Shifts:
    def __init__(self, rows, lanes):
        self.rows = rows
        self.lanes = lanes
        self.lane = lax.broadcasted_iota(jnp.int32, (rows, lanes), 1)
        self.row = lax.broadcasted_iota(jnp.int32, (rows, lanes), 0)
        self.xpos = self.lane % CX
        self.zpos = self.row % 4

    def roll(self, a, shift, axis):
        n = a.shape[axis]
        return pltpu.roll(a, shift % n, a.ndim + axis)

    def ahead(self, direction, a, nbr, placed=False):
        if direction == 0:
            return jnp.where(self.xpos == CX - 1, self.roll(a, CX - 1, -1), self.roll(a, -1, -1))
        if direction == 1:
            half = self.lanes // 2
            if placed and nbr is not None:
                return jnp.where(self.lane >= half, self.roll(nbr, half, -1), self.roll(a, half, -1))
            filled = jnp.where(self.lane < half, 0.0 if nbr is None else nbr, a)
            return self.roll(filled, half, -1)
        if direction == 2:
            inner = self.roll(a, -1, -2)
            outer = 0.0 if nbr is None else (nbr if placed else self.roll(nbr, 3, -2))
            return jnp.where(self.zpos == 3, outer, inner)
        filled = jnp.where(self.row < 4, 0.0 if nbr is None else nbr, a)
        return self.roll(filled, -4, -2)

    def behind(self, direction, a, nbr, placed=False):
        if direction == 0:
            return jnp.where(self.xpos == 0, self.roll(a, 1 - CX, -1), self.roll(a, 1, -1))
        if direction == 1:
            half = self.lanes // 2
            if placed and nbr is not None:
                return jnp.where(self.lane < half, nbr, self.roll(a, half, -1))
            filled = jnp.where(self.lane >= half, 0.0 if nbr is None else nbr, a)
            return self.roll(filled, half, -1)
        if direction == 2:
            inner = self.roll(a, 1, -2)
            outer = 0.0 if nbr is None else (nbr if placed else self.roll(nbr, -3, -2))
            return jnp.where(self.zpos == 0, outer, inner)
        filled = jnp.where(self.row >= self.rows - 4, 0.0 if nbr is None else nbr, a)
        return self.roll(filled, 4, -2)


def hopping(spinor, links, back_links, ahead_list, behind_list):
    hop_total = None
    for direction in range(4):
        ahead_half = colour_product(links[direction], project_minus(direction, ahead_list[direction]), False)
        behind_half = colour_product(back_links[direction], project_plus(direction, behind_list[direction]), True)
        term = rebuild_minus(direction, ahead_half) + rebuild_plus(direction, behind_half)
        hop_total = term if hop_total is None else hop_total + term
    return 4.5 * spinor - 0.5 * hop_total


FACES = ("y_low", "y_high", "z_low", "z_high", "t_low", "t_high")
HALO_KEYS = tuple((side, d) for d in (1, 2, 3) for side in ("ahead", "behind"))


def face_rows(name):
    return {"z_low": (0, 4), "z_high": (3, 4), "t_low": (0, 1), "t_high": (12, 1)}[name]


def place(scratch, value, side, direction):
    if direction == 1:
        scratch[..., pl.ds(0, value.shape[-1])] = value
        return
    start, stride = {("ahead", 2): (3, 4), ("behind", 2): (0, 4), ("ahead", 3): (0, 1), ("behind", 3): (12, 1)}[
        (side, direction)
    ]
    scratch[:, pl.ds(start, 4, stride=stride), :] = value


def pass_kernel(*refs, first, residual_only, present, faces, link_mode, append_links, emit_back, colour_pass):
    refs = list(refs)
    width = 24
    ghost_dirs = [d for d in (1, 2, 3) if link_mode == "combined" and present["behind"][d]]
    link_face_scratch = refs.pop() if append_links and "z_high" in faces else None
    ghost_scratch = {}
    for direction in reversed(ghost_dirs):
        ghost_scratch[direction] = refs.pop()
    scratch_refs = {}
    for key in reversed([k for k in HALO_KEYS if present[k[0]][k[1]]]):
        scratch_refs[key] = refs.pop()
    back_out_ref = refs.pop() if emit_back else None
    face_refs = {}
    for name in reversed(faces):
        face_refs[name] = refs.pop()
    out_ref = refs.pop()

    def take():
        return refs.pop(0)

    src_ref = take()
    links_ref = take()
    back_ref = take() if link_mode == "given" else None
    labels_ref = take()
    colouring_ref = None if residual_only else take()
    spinor_ref = None
    halo_refs = {}
    if not first:
        spinor_ref = take()
        for key in HALO_KEYS:
            if present[key[0]][key[1]]:
                halo_refs[key] = take()

    rows, lanes = src_ref.shape[-2], src_ref.shape[-1]
    sh = Shifts(rows, lanes)
    shape = (2, 4, 3, rows, lanes)
    source = src_ref[...].reshape(shape)
    link_all = links_ref[...].astype(jnp.float32)
    links = [link_all[d].reshape(2, 3, 3, rows, lanes) for d in range(4)]
    if back_ref is not None:
        back_all = back_ref[...].astype(jnp.float32)
        back_links = [back_all[d].reshape(2, 3, 3, rows, lanes) for d in range(4)]
    else:
        back_links = []
        for direction in range(4):
            ghost = None
            if direction in ghost_scratch:
                halo = halo_refs[("behind", direction)]
                place(ghost_scratch[direction], halo[width:], "behind", direction)
                ghost = ghost_scratch[direction][...].reshape(2, 3, 3, rows, lanes)
            back_links.append(sh.behind(direction, links[direction], ghost, True))
    if back_out_ref is not None:
        for direction in range(4):
            back_out_ref[direction] = back_links[direction].reshape(18, rows, lanes).astype(back_out_ref.dtype)

    for key, scratch in scratch_refs.items():
        halo = halo_refs[key]
        value = halo[:width] if (key[0] == "behind" and key[1] in ghost_scratch) else halo[...]
        place(scratch, value, key[0], key[1])

    def load_halo(side, direction):
        ref = scratch_refs.get((side, direction), halo_refs.get((side, direction)))
        return None if ref is None else ref[...].reshape(shape)

    def wilson_global(spinor):
        ahead_list = [sh.ahead(d, spinor, load_halo("ahead", d), True) for d in range(4)]
        behind_list = [sh.behind(d, spinor, load_halo("behind", d), True) for d in range(4)]
        return hopping(spinor, links, back_links, ahead_list, behind_list)

    if first:
        residue = source
        current = None
    else:
        current = spinor_ref[...].reshape(shape)
        residue = source - wilson_global(current)
    if residual_only:
        out_ref[...] = residue.reshape(out_ref.shape).astype(out_ref.dtype)
        return

    label_index = labels_ref[...]
    labels = (label_index + 1).astype(jnp.float32)
    ahead_masks = [(sh.ahead(d, labels, None) == labels).astype(jnp.float32) for d in range(4)]
    behind_masks = [(sh.behind(d, labels, None) == labels).astype(jnp.float32) for d in range(4)]
    member_bool = label_index[None] == lax.broadcasted_iota(jnp.int32, (AGG, 1, 1), 0)
    member = member_bool.astype(jnp.float32)
    site_colour = jnp.zeros((rows, lanes), jnp.int32)
    for block in range(AGG):
        site_colour = jnp.where(label_index == block, colouring_ref[block], site_colour)
    colour_mask = (site_colour == colour_pass).astype(jnp.float32)

    def wilson_block(spinor):
        ahead_list = [sh.ahead(d, spinor, None) * ahead_masks[d] for d in range(4)]
        behind_list = [sh.behind(d, spinor, None) * behind_masks[d] for d in range(4)]
        return hopping(spinor, links, back_links, ahead_list, behind_list)

    def block_total(values):
        return jnp.sum(jnp.sum(member * values[None], axis=2, keepdims=True), axis=1, keepdims=True)

    update = None
    remainder = residue
    for repeat in range(MR_STEPS):
        image = wilson_block(remainder)
        image_flat = image.reshape(2, 12, rows, lanes)
        rest_flat = remainder.reshape(2, 12, rows, lanes)
        dot_real = jnp.sum(image_flat[0] * rest_flat[0] + image_flat[1] * rest_flat[1], axis=0)
        dot_imag = jnp.sum(image_flat[0] * rest_flat[1] - image_flat[1] * rest_flat[0], axis=0)
        norm = jnp.sum(image_flat[0] * image_flat[0] + image_flat[1] * image_flat[1], axis=0)
        denominator = block_total(norm) + 1e-06
        factor_real = jnp.sum(member * (block_total(dot_real) / denominator), axis=0)
        factor_imag = jnp.sum(member * (block_total(dot_imag) / denominator), axis=0)
        step = complex_scale(factor_real, factor_imag, remainder)
        update = step if update is None else update + step
        remainder = remainder - complex_scale(factor_real, factor_imag, image)
    update = update * colour_mask
    result = update if current is None else current + update
    out_ref[...] = result.reshape(out_ref.shape)
    if link_face_scratch is not None:
        link_face_scratch[...] = link_all[2]
    for name, face_ref in face_refs.items():
        if name == "y_low":
            face_ref[...] = out_ref[:, :, pl.ds(0, lanes // 2)]
        elif name == "y_high":
            face_ref[0:width] = pltpu.roll(out_ref[...], lanes // 2, 2)[:, :, : lanes // 2]
            if append_links:
                face_ref[width:] = pltpu.roll(link_all[1], lanes // 2, 2)[:, :, : lanes // 2]
        else:
            start, stride = face_rows(name)
            face_ref[0:width] = out_ref[:, pl.ds(start, 4, stride=stride), :]
            if append_links and name == "z_high":
                face_ref[width:] = link_face_scratch[:, pl.ds(start, 4, stride=stride), :]
            elif append_links and name == "t_high":
                face_ref[width:] = link_all[3][:, start:start + 4, :]


def run_pass(source, links, back, labels, colouring, colour_pass, spinor, halos, residual_only=False, faces=(),
             link_mode="given", append_links=False, emit_back=False):
    first = spinor is None
    present = {
        "ahead": [h is not None for h in halos["ahead"]] if not first else [False] * 4,
        "behind": [h is not None for h in halos["behind"]] if not first else [False] * 4,
    }
    operands = [source, links] + ([back] if link_mode == "given" else []) + [labels]
    spaces = [pltpu.VMEM] * len(operands)
    if not residual_only:
        operands.append(colouring)
        spaces.append(pltpu.SMEM)
    if not first:
        operands.append(spinor)
        for key in HALO_KEYS:
            if present[key[0]][key[1]]:
                operands.append(halos[key[0]][key[1]])
    spaces += [pltpu.VMEM] * (len(operands) - len(spaces))
    kernel = functools.partial(
        pass_kernel, first=first, residual_only=residual_only, present=present, faces=faces,
        link_mode=link_mode, append_links=append_links, emit_back=emit_back, colour_pass=colour_pass,
    )
    width = source.shape[0]

    def face_shape(name):
        rows = width + (18 if append_links and name.endswith("high") else 0)
        if name.startswith("y"):
            return (rows, source.shape[1], source.shape[2] // 2)
        return (rows, 4, source.shape[2])

    out_shape = [jax.ShapeDtypeStruct(source.shape, jnp.bfloat16 if residual_only else jnp.float32)]
    out_shape += [jax.ShapeDtypeStruct(face_shape(name), jnp.float32) for name in faces]
    if emit_back:
        out_shape.append(jax.ShapeDtypeStruct(links.shape, links.dtype))
    scratch = [pltpu.VMEM(source.shape, jnp.float32) for k in HALO_KEYS if present[k[0]][k[1]]]
    if link_mode == "combined":
        scratch += [pltpu.VMEM(links.shape[1:], jnp.float32) for d in (1, 2, 3) if present["behind"][d]]
    if append_links and "z_high" in faces:
        scratch.append(pltpu.VMEM(links.shape[1:], jnp.float32))
    in_specs = [pl.BlockSpec(memory_space=space) for space in spaces]
    results = pl.pallas_call(kernel, out_shape=out_shape, scratch_shapes=scratch, in_specs=in_specs)(*operands)
    face_values = dict(zip(faces, results[1:1 + len(faces)]))
    return results[0], face_values, (results[-1] if emit_back else None)


def coarse_kernel(*refs, present):
    refs = list(refs)
    natural_ref = refs.pop()
    out_ref = refs.pop()
    source_ref, inverse_ref = refs[0], refs[1]
    first = len(refs) == 2
    width = source_ref.shape[-1]
    chunks = width // 128
    lane = lax.broadcasted_iota(jnp.int32, (1, width), 1)
    position = lane % AGG
    selector = (
        lax.broadcasted_iota(jnp.int32, (8, 128), 1) // AGG == lax.broadcasted_iota(jnp.int32, (8, 128), 0)
    ).astype(jnp.float32)

    def reduce_both(product):
        partial = product[:, 0:128]
        for q in range(1, chunks):
            partial = partial + product[:, q * 128:(q + 1) * 128]
        for shift in (64, 32, 16):
            partial = partial + pltpu.roll(partial, shift, 1)
        pieces = [
            jnp.sum(partial[8 * q:8 * q + 8] * selector, axis=0, keepdims=True) for q in range(chunks)
        ]
        return jnp.concatenate(pieces, axis=1), partial[:, :AGG]

    def reduce_flat(product):
        return reduce_both(product)[0]

    def roll_within(vector, shift):
        pieces = [pltpu.roll(vector[:, q * 128:(q + 1) * 128], shift % 128, 1) for q in range(chunks)]
        return jnp.concatenate(pieces, axis=1)

    def accumulate(acc, blocks_ref, index, vector):
        block_real = blocks_ref[index + (0,)].astype(jnp.float32)
        block_imag = blocks_ref[index + (1,)].astype(jnp.float32)
        real_part = block_real * vector[0] - block_imag * vector[1]
        imag_part = block_real * vector[1] + block_imag * vector[0]
        if acc is None:
            return [real_part, imag_part]
        return [acc[0] + real_part, acc[1] + imag_part]

    def precondition(vector):
        acc = accumulate(None, inverse_ref, (), vector)
        return [reduce_both(acc[0]), reduce_both(acc[1])]

    source = [source_ref[0], source_ref[1]]
    if first:
        step = precondition(source)
        result = [step[0][0], step[1][0]]
        natural = [step[0][1], step[1][1]]
    else:
        operator_ref, current_ref, current_natural_ref = refs[2], refs[3], refs[4]
        nearby_refs = refs[5:]
        current = [current_ref[0], current_ref[1]]
        ahead = [
            jnp.where(position == AGG - 1, roll_within(c, AGG - 1), roll_within(c, -1)) for c in current
        ]
        behind = [jnp.where(position == 0, roll_within(c, 1 - AGG), roll_within(c, 1)) for c in current]
        vectors = [current, ahead, behind]
        taken = 0
        for flag in present:
            if flag:
                vectors.append([nearby_refs[taken][0], nearby_refs[taken][1]])
                taken += 1
            else:
                vectors.append(None)
        acc = None
        for direction, vector in enumerate(vectors):
            if vector is not None:
                acc = accumulate(acc, operator_ref, (direction,), vector)
        residue = [source[0] - reduce_flat(acc[0]), source[1] - reduce_flat(acc[1])]
        step = precondition(residue)
        result = [current[0] + step[0][0], current[1] + step[1][0]]
        natural = [current_natural_ref[0] + step[0][1], current_natural_ref[1] + step[1][1]]
    out_ref[0] = result[0]
    out_ref[1] = result[1]
    natural_ref[0] = natural[0]
    natural_ref[1] = natural[1]


def run_coarse(source, inverse_blocks, operator_blocks, current, nearby):
    operands = [source, inverse_blocks]
    present = ()
    if current is not None:
        present = tuple(v is not None for v in nearby)
        operands += [operator_blocks, current[0], current[1]] + [v for v in nearby if v is not None]
    kernel = functools.partial(coarse_kernel, present=present)
    natural_shape = (2, inverse_blocks.shape[1], AGG)
    out_shape = [
        jax.ShapeDtypeStruct(source.shape, jnp.float32),
        jax.ShapeDtypeStruct(natural_shape, jnp.float32),
    ]
    return pl.pallas_call(kernel, out_shape=out_shape)(*operands)


def body(
    fine_source, links, test_vectors, aggregate_map, colouring, coarse_operator, block_inverse
):
    time_extent = fine_source.shape[2]
    plane_extent = fine_source.shape[3]
    line_extent = fine_source.shape[4]
    rows = time_extent * plane_extent
    site_count = rows * line_extent
    domain_index = lax.axis_index("lat")
    domain_count = lax.axis_size("lat")
    plane_position = (domain_index + 2) % PZ
    upper_valid = plane_position < PZ - 1
    lower_valid = plane_position > 0
    later_valid = domain_index < domain_count - PZ
    earlier_valid = domain_index >= PZ

    source = fine_source.reshape(24, rows, line_extent)
    link_rows = links.reshape(4, 18, rows, line_extent)
    label_rows = aggregate_map.reshape(rows, line_extent)
    member = (label_rows[None] == jnp.arange(AGG, dtype=jnp.int32)[:, None, None]).astype(jnp.float32)
    colour_list = colouring.reshape(AGG)

    def z_up_ok(i):
        return (i + 2) % PZ != PZ - 1

    def z_down_ok(i):
        return (i + 2) % PZ != 0

    def t_up_ok(i):
        return i + PZ < domain_count

    def t_down_ok(i):
        return i - PZ >= 0

    half = line_extent // 2

    needed = ["y_low", "y_high"] + [
        name for name, ok in zip(FACES[2:], (z_up_ok, z_down_ok, t_up_ok, t_down_ok))
        if any(ok(i) for i in range(domain_count))
    ]

    def faces_of(spinor):
        result = {"y_low": spinor[..., :half], "y_high": spinor[..., half:]}
        for name in needed[2:]:
            start, stride = face_rows(name)
            result[name] = lax.slice_in_dim(spinor, start, start + 3 * stride + 1, stride, axis=1)
        return result

    def halos_of(spinor, faces):
        def face(name):
            return faces[name] if name in faces else None

        return {
            "ahead": [
                None,
                permute_from(faces["y_low"], "grp", 1, lambda i: True),
                permute_from(face("z_low"), "lat", 1, z_up_ok) if face("z_low") is not None else None,
                permute_from(face("t_low"), "lat", PZ, t_up_ok) if face("t_low") is not None else None,
            ],
            "behind": [
                None,
                permute_from(faces["y_high"], "grp", -1, lambda i: True),
                permute_from(face("z_high"), "lat", -1, z_down_ok) if face("z_high") is not None else None,
                permute_from(face("t_high"), "lat", -PZ, t_down_ok) if face("t_high") is not None else None,
            ],
        }

    smoothed_first, first_faces, _ = run_pass(
        source, link_rows, None, label_rows, colour_list, 0, None, None,
        faces=tuple(needed), link_mode="none", append_links=True,
    )
    vectors = test_vectors.reshape(NVEC, 2, 2, 6, site_count)
    vectors, smoothed_first = lax.optimization_barrier((vectors, smoothed_first))
    smoothed, smoothed_faces, back_rows = run_pass(
        source, link_rows, None, label_rows, colour_list, 1, smoothed_first,
        halos_of(smoothed_first, first_faces), faces=tuple(needed), link_mode="combined", emit_back=True,
    )

    def sweep(start, faces):
        current, current_faces, _ = run_pass(
            source, link_rows, back_rows, label_rows, colour_list, 0, start, halos_of(start, faces),
            faces=tuple(needed),
        )
        result, _, _ = run_pass(
            source, link_rows, back_rows, label_rows, colour_list, 1, current,
            halos_of(current, current_faces),
        )
        return result

    residue, _, _ = run_pass(
        source, link_rows, back_rows, label_rows, None, None, smoothed, halos_of(smoothed, smoothed_faces),
        residual_only=True,
    )
    residual = residue
    membership = member.reshape(AGG, site_count).T
    member_weights = membership.astype(jnp.bfloat16)
    weighted = residual.reshape(2, 2, 6, site_count)[..., None] * member_weights

    pairs = jnp.einsum("krxqn,sxqnj->rsxkj", vectors, weighted, preferred_element_type=jnp.float32)
    real_part = pairs[0, 0] + pairs[1, 1]
    imag_part = pairs[0, 1] - pairs[1, 0]
    coarse_source = jnp.stack([real_part, imag_part]).reshape(2, CDOF, AGG)
    flat_source = coarse_source.reshape(2, 1, CDOF * AGG)
    operator_blocks = coarse_operator.reshape(9, 2, CDOF, CDOF * AGG)
    inverse_blocks = block_inverse.reshape(2, CDOF, CDOF * AGG)
    state = run_coarse(flat_source, inverse_blocks, operator_blocks, None, None)
    for repeat in range(2):
        flat = state[0]
        nearby = [
            permute_from(flat, "grp", 1, lambda i: True),
            permute_from(flat, "grp", -1, lambda i: True),
            permute_from(flat, "lat", 1, z_up_ok),
            permute_from(flat, "lat", -1, z_down_ok),
            permute_from(flat, "lat", PZ, t_up_ok),
            permute_from(flat, "lat", -PZ, t_down_ok),
        ]
        state = run_coarse(flat_source, inverse_blocks, operator_blocks, state, nearby)
    correction = state[1]
    expanded = jnp.dot(
        correction.reshape(2 * CDOF, AGG), membership.T, precision=lax.Precision.HIGHEST
    ).reshape(2, 2, NVEC, site_count)
    spread_real = jnp.swapaxes(expanded[0], 0, 1)[:, :, None]
    spread_imag = jnp.swapaxes(expanded[1], 0, 1)[:, :, None]
    real_part = jnp.sum(vectors[:, 0] * spread_real - vectors[:, 1] * spread_imag, axis=0)
    imag_part = jnp.sum(vectors[:, 0] * spread_imag + vectors[:, 1] * spread_real, axis=0)
    corrected = smoothed + jnp.stack([real_part, imag_part]).reshape(24, rows, line_extent)
    solution = sweep(corrected, faces_of(corrected))
    return (
        solution.reshape(1, 24, time_extent, plane_extent, line_extent),
        correction.reshape(1, 1, 2, CDOF, AGG),
    )


def solution(mesh):
    return jax.shard_map(
        body,
        mesh=mesh,
        in_specs=(
            P("lat", None, None, None, "grp"),
            P("lat", None, None, None, None, "grp"),
            P("lat", None, None, None, None, "grp"),
            P("lat", None, None, "grp", None),
            P("lat", "grp", None),
            P("lat", "grp", None, None, None, None),
            P("lat", "grp", None, None, None),
        ),
        out_specs=(P("lat", None, None, None, "grp"), P("lat", "grp", None, None, None)),
        check_vma=False,
    )
```

```python
import functools

import jax
import jax.numpy as jnp
from jax import lax
from jax.experimental import pallas as pl
from jax.experimental.pallas import tpu as pltpu
from jax.sharding import PartitionSpec as P

CX = 64
PZ = 8
NVEC = 24
AGG = 16
MR_STEPS = 2
CDOF = 48


def passed_along(shard, axis, by):
    size = lax.axis_size(axis)
    return lax.ppermute(shard, axis, [(i, (i + by) % size) for i in range(size)])


def padded_2(shard, sides, width):
    for axis, dim in sides:
        size, length = (lax.axis_size(axis), shard.shape[dim])
        up = [(i, (i + 1) % size) for i in range(size)]
        down = [(j, i) for i, j in up]
        last = lax.slice_in_dim(shard, length - width, length, axis=dim)
        first = lax.slice_in_dim(shard, 0, width, axis=dim)
        before = lax.ppermute(last, axis, up)
        after = lax.ppermute(first, axis, down)
        shard = jnp.concatenate([before, shard, after], axis=dim)
    return shard


def times_minus_i(values):
    return jnp.stack([values[1], -values[0]])


def times_plus_i(values):
    return jnp.stack([-values[1], values[0]])


def spin_factor(direction, spin_pair):
    if direction == 0:
        return jnp.stack([times_minus_i(spin_pair[:, 1]), times_minus_i(spin_pair[:, 0])], axis=1)
    if direction == 1:
        return jnp.stack([-spin_pair[:, 1], spin_pair[:, 0]], axis=1)
    if direction == 2:
        return jnp.stack([times_minus_i(spin_pair[:, 0]), times_plus_i(spin_pair[:, 1])], axis=1)
    return spin_pair


def project_minus(direction, spinor):
    return spinor[:, :2] - spin_factor(direction, spinor[:, 2:])


def project_plus(direction, spinor):
    return spinor[:, :2] + spin_factor(direction, spinor[:, 2:])


def rebuild_minus(direction, half_spinor):
    lower_part = spin_factor(direction, half_spinor) if direction < 3 else -half_spinor
    return jnp.concatenate([half_spinor, lower_part], axis=1)


def rebuild_plus(direction, half_spinor):
    lower_part = -spin_factor(direction, half_spinor) if direction < 3 else half_spinor
    return jnp.concatenate([half_spinor, lower_part], axis=1)


def colour_product(gauge_link, half_spinor, adjoint):
    link_real = gauge_link[0]
    link_imag = gauge_link[1]
    if adjoint:
        link_real = jnp.swapaxes(link_real, 0, 1)
        link_imag = -jnp.swapaxes(link_imag, 0, 1)
    spin_real = half_spinor[0][:, None]
    spin_imag = half_spinor[1][:, None]
    real_part = jnp.sum(link_real[None] * spin_real - link_imag[None] * spin_imag, axis=2)
    imag_part = jnp.sum(link_real[None] * spin_imag + link_imag[None] * spin_real, axis=2)
    return jnp.stack([real_part, imag_part])


def complex_scale(factor_real, factor_imag, lattice):
    return jnp.stack(
        [
            factor_real * lattice[0] - factor_imag * lattice[1],
            factor_real * lattice[1] + factor_imag * lattice[0],
        ]
    )


def apply_blocks(blocks, nearby):
    matrices = blocks.reshape(blocks.shape[0], 2, CDOF, CDOF, AGG)
    vector_real = nearby[:, 0][:, None]
    vector_imag = nearby[:, 1][:, None]
    real_part = jnp.sum(matrices[:, 0] * vector_real - matrices[:, 1] * vector_imag, axis=(0, 2))
    imag_part = jnp.sum(matrices[:, 0] * vector_imag + matrices[:, 1] * vector_real, axis=(0, 2))
    return jnp.stack([real_part, imag_part])


def keep_if(allowed, values):
    return jnp.where(allowed, values, jnp.zeros_like(values))


def permute_from(value, axis, offset, allowed):
    size = lax.axis_size(axis)
    pairs = [((i + offset) % size, i) for i in range(size) if allowed(i)]
    if not pairs:
        return None
    return lax.ppermute(value, axis, pairs)


class Shifts:
    def __init__(self, rows, lanes):
        self.rows = rows
        self.lanes = lanes
        self.lane = lax.broadcasted_iota(jnp.int32, (rows, lanes), 1)
        self.row = lax.broadcasted_iota(jnp.int32, (rows, lanes), 0)
        self.xpos = self.lane % CX
        self.zpos = self.row % 4

    def roll(self, a, shift, axis):
        n = a.shape[axis]
        return pltpu.roll(a, shift % n, a.ndim + axis)

    def ahead(self, direction, a, nbr, placed=False):
        if direction == 0:
            return jnp.where(self.xpos == CX - 1, self.roll(a, CX - 1, -1), self.roll(a, -1, -1))
        if direction == 1:
            half = self.lanes // 2
            if placed and nbr is not None:
                return jnp.where(self.lane >= half, self.roll(nbr, half, -1), self.roll(a, half, -1))
            filled = jnp.where(self.lane < half, 0.0 if nbr is None else nbr, a)
            return self.roll(filled, half, -1)
        if direction == 2:
            inner = self.roll(a, -1, -2)
            outer = 0.0 if nbr is None else (nbr if placed else self.roll(nbr, 3, -2))
            return jnp.where(self.zpos == 3, outer, inner)
        filled = jnp.where(self.row < 4, 0.0 if nbr is None else nbr, a)
        return self.roll(filled, -4, -2)

    def behind(self, direction, a, nbr, placed=False):
        if direction == 0:
            return jnp.where(self.xpos == 0, self.roll(a, 1 - CX, -1), self.roll(a, 1, -1))
        if direction == 1:
            half = self.lanes // 2
            if placed and nbr is not None:
                return jnp.where(self.lane < half, nbr, self.roll(a, half, -1))
            filled = jnp.where(self.lane >= half, 0.0 if nbr is None else nbr, a)
            return self.roll(filled, half, -1)
        if direction == 2:
            inner = self.roll(a, 1, -2)
            outer = 0.0 if nbr is None else (nbr if placed else self.roll(nbr, -3, -2))
            return jnp.where(self.zpos == 0, outer, inner)
        filled = jnp.where(self.row >= self.rows - 4, 0.0 if nbr is None else nbr, a)
        return self.roll(filled, 4, -2)


def hopping(spinor, links, back_links, ahead_list, behind_list):
    hop_total = None
    for direction in range(4):
        ahead_half = colour_product(links[direction], project_minus(direction, ahead_list[direction]), False)
        behind_half = colour_product(back_links[direction], project_plus(direction, behind_list[direction]), True)
        term = rebuild_minus(direction, ahead_half) + rebuild_plus(direction, behind_half)
        hop_total = term if hop_total is None else hop_total + term
    return 4.5 * spinor - 0.5 * hop_total


FACES = ("y_low", "y_high", "z_low", "z_high", "t_low", "t_high")
HALO_KEYS = tuple((side, d) for d in (1, 2, 3) for side in ("ahead", "behind"))


def face_rows(name):
    return {"z_low": (0, 4), "z_high": (3, 4), "t_low": (0, 1), "t_high": (12, 1)}[name]


def place(scratch, value, side, direction):
    if direction == 1:
        scratch[..., pl.ds(0, value.shape[-1])] = value
        return
    start, stride = {("ahead", 2): (3, 4), ("behind", 2): (0, 4), ("ahead", 3): (0, 1), ("behind", 3): (12, 1)}[
        (side, direction)
    ]
    scratch[:, pl.ds(start, 4, stride=stride), :] = value


def pass_kernel(*refs, first, residual_only, present, faces, link_mode, append_links, emit_back, colour_pass):
    refs = list(refs)
    width = 24
    ghost_dirs = [d for d in (1, 2, 3) if link_mode == "combined" and present["behind"][d]]
    link_face_scratch = refs.pop() if append_links and "z_high" in faces else None
    ghost_scratch = {}
    for direction in reversed(ghost_dirs):
        ghost_scratch[direction] = refs.pop()
    scratch_refs = {}
    for key in reversed([k for k in HALO_KEYS if present[k[0]][k[1]]]):
        scratch_refs[key] = refs.pop()
    back_out_ref = refs.pop() if emit_back else None
    face_refs = {}
    for name in reversed(faces):
        face_refs[name] = refs.pop()
    out_ref = refs.pop()

    def take():
        return refs.pop(0)

    src_ref = take()
    links_ref = take()
    back_ref = take() if link_mode == "given" else None
    labels_ref = take()
    colouring_ref = None if residual_only else take()
    spinor_ref = None
    halo_refs = {}
    if not first:
        spinor_ref = take()
        for key in HALO_KEYS:
            if present[key[0]][key[1]]:
                halo_refs[key] = take()

    rows, lanes = src_ref.shape[-2], src_ref.shape[-1]
    sh = Shifts(rows, lanes)
    shape = (2, 4, 3, rows, lanes)
    source = src_ref[...].reshape(shape)
    link_all = links_ref[...].astype(jnp.float32)
    links = [link_all[d].reshape(2, 3, 3, rows, lanes) for d in range(4)]
    if back_ref is not None:
        back_all = back_ref[...].astype(jnp.float32)
        back_links = [back_all[d].reshape(2, 3, 3, rows, lanes) for d in range(4)]
    else:
        back_links = []
        for direction in range(4):
            ghost = None
            if direction in ghost_scratch:
                halo = halo_refs[("behind", direction)]
                place(ghost_scratch[direction], halo[width:], "behind", direction)
                ghost = ghost_scratch[direction][...].reshape(2, 3, 3, rows, lanes)
            back_links.append(sh.behind(direction, links[direction], ghost, True))
    if back_out_ref is not None:
        for direction in range(4):
            back_out_ref[direction] = back_links[direction].reshape(18, rows, lanes).astype(back_out_ref.dtype)

    for key, scratch in scratch_refs.items():
        halo = halo_refs[key]
        value = halo[:width] if (key[0] == "behind" and key[1] in ghost_scratch) else halo[...]
        place(scratch, value, key[0], key[1])

    def load_halo(side, direction):
        ref = scratch_refs.get((side, direction), halo_refs.get((side, direction)))
        return None if ref is None else ref[...].reshape(shape)

    def wilson_global(spinor):
        ahead_list = [sh.ahead(d, spinor, load_halo("ahead", d), True) for d in range(4)]
        behind_list = [sh.behind(d, spinor, load_halo("behind", d), True) for d in range(4)]
        return hopping(spinor, links, back_links, ahead_list, behind_list)

    if first:
        residue = source
        current = None
    else:
        current = spinor_ref[...].reshape(shape)
        residue = source - wilson_global(current)
    if residual_only:
        out_ref[...] = residue.reshape(out_ref.shape).astype(out_ref.dtype)
        return

    label_index = labels_ref[...]
    labels = (label_index + 1).astype(jnp.float32)
    ahead_masks = [(sh.ahead(d, labels, None) == labels).astype(jnp.float32) for d in range(4)]
    behind_masks = [(sh.behind(d, labels, None) == labels).astype(jnp.float32) for d in range(4)]
    member_bool = label_index[None] == lax.broadcasted_iota(jnp.int32, (AGG, 1, 1), 0)
    member = member_bool.astype(jnp.float32)
    site_colour = jnp.zeros((rows, lanes), jnp.int32)
    for block in range(AGG):
        site_colour = jnp.where(label_index == block, colouring_ref[block], site_colour)
    colour_mask = (site_colour == colour_pass).astype(jnp.float32)

    def wilson_block(spinor):
        ahead_list = [sh.ahead(d, spinor, None) * ahead_masks[d] for d in range(4)]
        behind_list = [sh.behind(d, spinor, None) * behind_masks[d] for d in range(4)]
        return hopping(spinor, links, back_links, ahead_list, behind_list)

    def block_total(values):
        return jnp.sum(jnp.sum(member * values[None], axis=2, keepdims=True), axis=1, keepdims=True)

    update = None
    remainder = residue
    for repeat in range(MR_STEPS):
        image = wilson_block(remainder)
        image_flat = image.reshape(2, 12, rows, lanes)
        rest_flat = remainder.reshape(2, 12, rows, lanes)
        dot_real = jnp.sum(image_flat[0] * rest_flat[0] + image_flat[1] * rest_flat[1], axis=0)
        dot_imag = jnp.sum(image_flat[0] * rest_flat[1] - image_flat[1] * rest_flat[0], axis=0)
        norm = jnp.sum(image_flat[0] * image_flat[0] + image_flat[1] * image_flat[1], axis=0)
        denominator = block_total(norm) + 1e-06
        factor_real = jnp.sum(member * (block_total(dot_real) / denominator), axis=0)
        factor_imag = jnp.sum(member * (block_total(dot_imag) / denominator), axis=0)
        step = complex_scale(factor_real, factor_imag, remainder)
        update = step if update is None else update + step
        remainder = remainder - complex_scale(factor_real, factor_imag, image)
    update = update * colour_mask
    result = update if current is None else current + update
    out_ref[...] = result.reshape(out_ref.shape)
    if link_face_scratch is not None:
        link_face_scratch[...] = link_all[2]
    for name, face_ref in face_refs.items():
        if name == "y_low":
            face_ref[...] = out_ref[:, :, pl.ds(0, lanes // 2)]
        elif name == "y_high":
            face_ref[0:width] = pltpu.roll(out_ref[...], lanes // 2, 2)[:, :, : lanes // 2]
            if append_links:
                face_ref[width:] = pltpu.roll(link_all[1], lanes // 2, 2)[:, :, : lanes // 2]
        else:
            start, stride = face_rows(name)
            face_ref[0:width] = out_ref[:, pl.ds(start, 4, stride=stride), :]
            if append_links and name == "z_high":
                face_ref[width:] = link_face_scratch[:, pl.ds(start, 4, stride=stride), :]
            elif append_links and name == "t_high":
                face_ref[width:] = link_all[3][:, start:start + 4, :]


def run_pass(source, links, back, labels, colouring, colour_pass, spinor, halos, residual_only=False, faces=(),
             link_mode="given", append_links=False, emit_back=False):
    first = spinor is None
    present = {
        "ahead": [h is not None for h in halos["ahead"]] if not first else [False] * 4,
        "behind": [h is not None for h in halos["behind"]] if not first else [False] * 4,
    }
    operands = [source, links] + ([back] if link_mode == "given" else []) + [labels]
    spaces = [pltpu.VMEM] * len(operands)
    if not residual_only:
        operands.append(colouring)
        spaces.append(pltpu.SMEM)
    if not first:
        operands.append(spinor)
        for key in HALO_KEYS:
            if present[key[0]][key[1]]:
                operands.append(halos[key[0]][key[1]])
    spaces += [pltpu.VMEM] * (len(operands) - len(spaces))
    kernel = functools.partial(
        pass_kernel, first=first, residual_only=residual_only, present=present, faces=faces,
        link_mode=link_mode, append_links=append_links, emit_back=emit_back, colour_pass=colour_pass,
    )
    width = source.shape[0]

    def face_shape(name):
        rows = width + (18 if append_links and name.endswith("high") else 0)
        if name.startswith("y"):
            return (rows, source.shape[1], source.shape[2] // 2)
        return (rows, 4, source.shape[2])

    out_shape = [jax.ShapeDtypeStruct(source.shape, jnp.bfloat16 if residual_only else jnp.float32)]
    out_shape += [jax.ShapeDtypeStruct(face_shape(name), jnp.float32) for name in faces]
    if emit_back:
        out_shape.append(jax.ShapeDtypeStruct(links.shape, links.dtype))
    scratch = [pltpu.VMEM(source.shape, jnp.float32) for k in HALO_KEYS if present[k[0]][k[1]]]
    if link_mode == "combined":
        scratch += [pltpu.VMEM(links.shape[1:], jnp.float32) for d in (1, 2, 3) if present["behind"][d]]
    if append_links and "z_high" in faces:
        scratch.append(pltpu.VMEM(links.shape[1:], jnp.float32))
    in_specs = [pl.BlockSpec(memory_space=space) for space in spaces]
    results = pl.pallas_call(kernel, out_shape=out_shape, scratch_shapes=scratch, in_specs=in_specs)(*operands)
    face_values = dict(zip(faces, results[1:1 + len(faces)]))
    return results[0], face_values, (results[-1] if emit_back else None)


def coarse_kernel(*refs, present):
    refs = list(refs)
    out_ref = refs.pop()
    source_ref, inverse_ref = refs[0], refs[1]
    first = len(refs) == 2
    width = source_ref.shape[-1]
    chunks = width // 128
    lane = lax.broadcasted_iota(jnp.int32, (1, width), 1)
    position = lane % AGG
    selector = (
        lax.broadcasted_iota(jnp.int32, (8, 128), 1) // AGG == lax.broadcasted_iota(jnp.int32, (8, 128), 0)
    ).astype(jnp.float32)

    def reduce_flat(product):
        partial = product[:, 0:128]
        for q in range(1, chunks):
            partial = partial + product[:, q * 128:(q + 1) * 128]
        for shift in (64, 32, 16):
            partial = partial + pltpu.roll(partial, shift, 1)
        pieces = [
            jnp.sum(partial[8 * q:8 * q + 8] * selector, axis=0, keepdims=True) for q in range(chunks)
        ]
        return jnp.concatenate(pieces, axis=1)

    def roll_within(vector, shift):
        pieces = [pltpu.roll(vector[:, q * 128:(q + 1) * 128], shift % 128, 1) for q in range(chunks)]
        return jnp.concatenate(pieces, axis=1)

    def accumulate(acc, blocks_ref, index, vector):
        block_real = blocks_ref[index + (0,)].astype(jnp.float32)
        block_imag = blocks_ref[index + (1,)].astype(jnp.float32)
        real_part = block_real * vector[0] - block_imag * vector[1]
        imag_part = block_real * vector[1] + block_imag * vector[0]
        if acc is None:
            return [real_part, imag_part]
        return [acc[0] + real_part, acc[1] + imag_part]

    def precondition(vector):
        acc = accumulate(None, inverse_ref, (), vector)
        return [reduce_flat(acc[0]), reduce_flat(acc[1])]

    source = [source_ref[0], source_ref[1]]
    if first:
        result = precondition(source)
    else:
        operator_ref, current_ref = refs[2], refs[3]
        nearby_refs = refs[4:]
        current = [current_ref[0], current_ref[1]]
        ahead = [
            jnp.where(position == AGG - 1, roll_within(c, AGG - 1), roll_within(c, -1)) for c in current
        ]
        behind = [jnp.where(position == 0, roll_within(c, 1 - AGG), roll_within(c, 1)) for c in current]
        vectors = [current, ahead, behind]
        taken = 0
        for flag in present:
            if flag:
                vectors.append([nearby_refs[taken][0], nearby_refs[taken][1]])
                taken += 1
            else:
                vectors.append(None)
        acc = None
        for direction, vector in enumerate(vectors):
            if vector is not None:
                acc = accumulate(acc, operator_ref, (direction,), vector)
        residue = [source[0] - reduce_flat(acc[0]), source[1] - reduce_flat(acc[1])]
        step = precondition(residue)
        result = [current[0] + step[0], current[1] + step[1]]
    out_ref[0] = result[0]
    out_ref[1] = result[1]


def coarse_step_kernel(*refs, count):
    refs = list(refs)
    acc_ref = refs.pop()
    out_ref = refs.pop()
    source_ref, inverse_ref, operator_ref, current_ref = refs[:4]
    nearby_refs = refs[4:]
    step_index = pl.program_id(0)
    width = source_ref.shape[-1]
    chunks = width // 128
    lane = lax.broadcasted_iota(jnp.int32, (1, width), 1)
    position = lane % AGG
    selector = (
        lax.broadcasted_iota(jnp.int32, (8, 128), 1) // AGG == lax.broadcasted_iota(jnp.int32, (8, 128), 0)
    ).astype(jnp.float32)

    def reduce_flat(product):
        partial = product[:, 0:128]
        for q in range(1, chunks):
            partial = partial + product[:, q * 128:(q + 1) * 128]
        for shift in (64, 32, 16):
            partial = partial + pltpu.roll(partial, shift, 1)
        pieces = [
            jnp.sum(partial[8 * q:8 * q + 8] * selector, axis=0, keepdims=True) for q in range(chunks)
        ]
        return jnp.concatenate(pieces, axis=1)

    def roll_within(vector, shift):
        pieces = [pltpu.roll(vector[:, q * 128:(q + 1) * 128], shift % 128, 1) for q in range(chunks)]
        return jnp.concatenate(pieces, axis=1)

    def product(blocks_ref, index, vector):
        block_real = blocks_ref[index + (0,)].astype(jnp.float32)
        block_imag = blocks_ref[index + (1,)].astype(jnp.float32)
        return [
            block_real * vector[0] - block_imag * vector[1],
            block_real * vector[1] + block_imag * vector[0],
        ]

    def vector_of(direction):
        current = [current_ref[0], current_ref[1]]
        if direction == 0:
            return current
        if direction == 1:
            return [jnp.where(position == AGG - 1, roll_within(c, AGG - 1), roll_within(c, -1)) for c in current]
        if direction == 2:
            return [jnp.where(position == 0, roll_within(c, 1 - AGG), roll_within(c, 1)) for c in current]
        ref = nearby_refs[direction - 3]
        return [ref[0], ref[1]]

    for direction in range(count):
        @pl.when(step_index == direction)
        def _():
            part = product(operator_ref, (0,), vector_of(direction))
            if direction == 0:
                acc_ref[0] = part[0]
                acc_ref[1] = part[1]
            else:
                acc_ref[0] = acc_ref[0] + part[0]
                acc_ref[1] = acc_ref[1] + part[1]

    @pl.when(step_index == count - 1)
    def _():
        residue = [source_ref[0] - reduce_flat(acc_ref[0]), source_ref[1] - reduce_flat(acc_ref[1])]
        acc = product(inverse_ref, (), residue)
        out_ref[0] = current_ref[0] + reduce_flat(acc[0])
        out_ref[1] = current_ref[1] + reduce_flat(acc[1])


def run_coarse(source, inverse_blocks, operator_blocks, current, nearby):
    if current is None:
        kernel = functools.partial(coarse_kernel, present=())
        return pl.pallas_call(kernel, out_shape=jax.ShapeDtypeStruct(source.shape, jnp.float32))(
            source, inverse_blocks
        )
    present = [v is not None for v in nearby]
    count = 3 + sum(present)
    if present[:count - 3] != [True] * (count - 3):
        raise ValueError("not a prefix")
    arrays = [v for v in nearby if v is not None]

    def whole(array):
        return pl.BlockSpec(array.shape, lambda i, n=array.ndim: (0,) * n)

    in_specs = [whole(source), whole(inverse_blocks)]
    in_specs.append(pl.BlockSpec((1,) + operator_blocks.shape[1:], lambda i: (i, 0, 0, 0)))
    in_specs += [whole(current)] + [whole(v) for v in arrays]
    kernel = functools.partial(coarse_step_kernel, count=count)
    return pl.pallas_call(
        kernel,
        out_shape=jax.ShapeDtypeStruct(source.shape, jnp.float32),
        grid=(count,),
        in_specs=in_specs,
        out_specs=whole(source),
        scratch_shapes=[pltpu.VMEM((2,) + operator_blocks.shape[2:], jnp.float32)],
    )(source, inverse_blocks, operator_blocks, current, *arrays)


def body(
    fine_source, links, test_vectors, aggregate_map, colouring, coarse_operator, block_inverse
):
    time_extent = fine_source.shape[2]
    plane_extent = fine_source.shape[3]
    line_extent = fine_source.shape[4]
    rows = time_extent * plane_extent
    site_count = rows * line_extent
    domain_index = lax.axis_index("lat")
    domain_count = lax.axis_size("lat")
    plane_position = (domain_index + 2) % PZ
    upper_valid = plane_position < PZ - 1
    lower_valid = plane_position > 0
    later_valid = domain_index < domain_count - PZ
    earlier_valid = domain_index >= PZ

    source = fine_source.reshape(24, rows, line_extent)
    link_rows = links.reshape(4, 18, rows, line_extent)
    label_rows = aggregate_map.reshape(rows, line_extent)
    member = (label_rows[None] == jnp.arange(AGG, dtype=jnp.int32)[:, None, None]).astype(jnp.float32)
    colour_list = colouring.reshape(AGG)

    def z_up_ok(i):
        return (i + 2) % PZ != PZ - 1

    def z_down_ok(i):
        return (i + 2) % PZ != 0

    def t_up_ok(i):
        return i + PZ < domain_count

    def t_down_ok(i):
        return i - PZ >= 0

    half = line_extent // 2

    needed = ["y_low", "y_high"] + [
        name for name, ok in zip(FACES[2:], (z_up_ok, z_down_ok, t_up_ok, t_down_ok))
        if any(ok(i) for i in range(domain_count))
    ]

    def faces_of(spinor):
        result = {"y_low": spinor[..., :half], "y_high": spinor[..., half:]}
        for name in needed[2:]:
            start, stride = face_rows(name)
            result[name] = lax.slice_in_dim(spinor, start, start + 3 * stride + 1, stride, axis=1)
        return result

    def halos_of(spinor, faces):
        def face(name):
            return faces[name] if name in faces else None

        return {
            "ahead": [
                None,
                permute_from(faces["y_low"], "grp", 1, lambda i: True),
                permute_from(face("z_low"), "lat", 1, z_up_ok) if face("z_low") is not None else None,
                permute_from(face("t_low"), "lat", PZ, t_up_ok) if face("t_low") is not None else None,
            ],
            "behind": [
                None,
                permute_from(faces["y_high"], "grp", -1, lambda i: True),
                permute_from(face("z_high"), "lat", -1, z_down_ok) if face("z_high") is not None else None,
                permute_from(face("t_high"), "lat", -PZ, t_down_ok) if face("t_high") is not None else None,
            ],
        }

    smoothed_first, first_faces, _ = run_pass(
        source, link_rows, None, label_rows, colour_list, 0, None, None,
        faces=tuple(needed), link_mode="none", append_links=True,
    )
    vectors = test_vectors.reshape(NVEC, 2, 2, 6, site_count)
    vectors, smoothed_first = lax.optimization_barrier((vectors, smoothed_first))
    smoothed, smoothed_faces, back_rows = run_pass(
        source, link_rows, None, label_rows, colour_list, 1, smoothed_first,
        halos_of(smoothed_first, first_faces), faces=tuple(needed), link_mode="combined", emit_back=True,
    )

    def sweep(start, faces):
        current, current_faces, _ = run_pass(
            source, link_rows, back_rows, label_rows, colour_list, 0, start, halos_of(start, faces),
            faces=tuple(needed),
        )
        result, _, _ = run_pass(
            source, link_rows, back_rows, label_rows, colour_list, 1, current,
            halos_of(current, current_faces),
        )
        return result

    residue, _, _ = run_pass(
        source, link_rows, back_rows, label_rows, None, None, smoothed, halos_of(smoothed, smoothed_faces),
        residual_only=True,
    )
    residual = residue
    membership = member.reshape(AGG, site_count).T
    member_weights = membership.astype(jnp.bfloat16)
    weighted = residual.reshape(2, 2, 6, site_count)[..., None] * member_weights

    pairs = jnp.einsum("krxqn,sxqnj->rsxkj", vectors, weighted, preferred_element_type=jnp.float32)
    real_part = pairs[0, 0] + pairs[1, 1]
    imag_part = pairs[0, 1] - pairs[1, 0]
    coarse_source = jnp.stack([real_part, imag_part]).reshape(2, CDOF, AGG)
    flat_source = coarse_source.reshape(2, 1, CDOF * AGG)
    operator_blocks = coarse_operator.reshape(9, 2, CDOF, CDOF * AGG)
    inverse_blocks = block_inverse.reshape(2, CDOF, CDOF * AGG)
    correction = run_coarse(flat_source, inverse_blocks, operator_blocks, None, None)
    for repeat in range(2):
        nearby = [
            permute_from(correction, "grp", 1, lambda i: True),
            permute_from(correction, "grp", -1, lambda i: True),
            permute_from(correction, "lat", 1, z_up_ok),
            permute_from(correction, "lat", -1, z_down_ok),
            permute_from(correction, "lat", PZ, t_up_ok),
            permute_from(correction, "lat", -PZ, t_down_ok),
        ]
        correction = run_coarse(flat_source, inverse_blocks, operator_blocks, correction, nearby)
    correction = correction.reshape(2, CDOF, AGG)
    expanded = jnp.dot(
        correction.reshape(2 * CDOF, AGG), membership.T, precision=lax.Precision.HIGHEST
    ).reshape(2, 2, NVEC, site_count)
    spread_real = jnp.swapaxes(expanded[0], 0, 1)[:, :, None]
    spread_imag = jnp.swapaxes(expanded[1], 0, 1)[:, :, None]
    real_part = jnp.sum(vectors[:, 0] * spread_real - vectors[:, 1] * spread_imag, axis=0)
    imag_part = jnp.sum(vectors[:, 0] * spread_imag + vectors[:, 1] * spread_real, axis=0)
    corrected = smoothed + jnp.stack([real_part, imag_part]).reshape(24, rows, line_extent)
    solution = sweep(corrected, faces_of(corrected))
    return (
        solution.reshape(1, 24, time_extent, plane_extent, line_extent),
        correction.reshape(1, 1, 2, CDOF, AGG),
    )


def solution(mesh):
    return jax.shard_map(
        body,
        mesh=mesh,
        in_specs=(
            P("lat", None, None, None, "grp"),
            P("lat", None, None, None, None, "grp"),
            P("lat", None, None, None, None, "grp"),
            P("lat", None, None, "grp", None),
            P("lat", "grp", None),
            P("lat", "grp", None, None, None, None),
            P("lat", "grp", None, None, None),
        ),
        out_specs=(P("lat", None, None, None, "grp"), P("lat", "grp", None, None, None)),
        check_vma=False,
    )
```

```python
import functools

import jax
import jax.numpy as jnp
from jax import lax
from jax.experimental import pallas as pl
from jax.experimental.pallas import tpu as pltpu
from jax.sharding import PartitionSpec as P

CX = 64
PZ = 8
NVEC = 24
AGG = 16
MR_STEPS = 2
CDOF = 48


def passed_along(shard, axis, by):
    size = lax.axis_size(axis)
    return lax.ppermute(shard, axis, [(i, (i + by) % size) for i in range(size)])


def padded_2(shard, sides, width):
    for axis, dim in sides:
        size, length = (lax.axis_size(axis), shard.shape[dim])
        up = [(i, (i + 1) % size) for i in range(size)]
        down = [(j, i) for i, j in up]
        last = lax.slice_in_dim(shard, length - width, length, axis=dim)
        first = lax.slice_in_dim(shard, 0, width, axis=dim)
        before = lax.ppermute(last, axis, up)
        after = lax.ppermute(first, axis, down)
        shard = jnp.concatenate([before, shard, after], axis=dim)
    return shard


def times_minus_i(values):
    return jnp.stack([values[1], -values[0]])


def times_plus_i(values):
    return jnp.stack([-values[1], values[0]])


def spin_factor(direction, spin_pair):
    if direction == 0:
        return jnp.stack([times_minus_i(spin_pair[:, 1]), times_minus_i(spin_pair[:, 0])], axis=1)
    if direction == 1:
        return jnp.stack([-spin_pair[:, 1], spin_pair[:, 0]], axis=1)
    if direction == 2:
        return jnp.stack([times_minus_i(spin_pair[:, 0]), times_plus_i(spin_pair[:, 1])], axis=1)
    return spin_pair


def project_minus(direction, spinor):
    return spinor[:, :2] - spin_factor(direction, spinor[:, 2:])


def project_plus(direction, spinor):
    return spinor[:, :2] + spin_factor(direction, spinor[:, 2:])


def rebuild_minus(direction, half_spinor):
    lower_part = spin_factor(direction, half_spinor) if direction < 3 else -half_spinor
    return jnp.concatenate([half_spinor, lower_part], axis=1)


def rebuild_plus(direction, half_spinor):
    lower_part = -spin_factor(direction, half_spinor) if direction < 3 else half_spinor
    return jnp.concatenate([half_spinor, lower_part], axis=1)


def colour_product(gauge_link, half_spinor, adjoint):
    link_real = gauge_link[0]
    link_imag = gauge_link[1]
    if adjoint:
        link_real = jnp.swapaxes(link_real, 0, 1)
        link_imag = -jnp.swapaxes(link_imag, 0, 1)
    spin_real = half_spinor[0][:, None]
    spin_imag = half_spinor[1][:, None]
    real_part = jnp.sum(link_real[None] * spin_real - link_imag[None] * spin_imag, axis=2)
    imag_part = jnp.sum(link_real[None] * spin_imag + link_imag[None] * spin_real, axis=2)
    return jnp.stack([real_part, imag_part])


def complex_scale(factor_real, factor_imag, lattice):
    return jnp.stack(
        [
            factor_real * lattice[0] - factor_imag * lattice[1],
            factor_real * lattice[1] + factor_imag * lattice[0],
        ]
    )


def apply_blocks(blocks, nearby):
    matrices = blocks.reshape(blocks.shape[0], 2, CDOF, CDOF, AGG)
    vector_real = nearby[:, 0][:, None]
    vector_imag = nearby[:, 1][:, None]
    real_part = jnp.sum(matrices[:, 0] * vector_real - matrices[:, 1] * vector_imag, axis=(0, 2))
    imag_part = jnp.sum(matrices[:, 0] * vector_imag + matrices[:, 1] * vector_real, axis=(0, 2))
    return jnp.stack([real_part, imag_part])


def keep_if(allowed, values):
    return jnp.where(allowed, values, jnp.zeros_like(values))


def permute_from(value, axis, offset, allowed):
    size = lax.axis_size(axis)
    pairs = [((i + offset) % size, i) for i in range(size) if allowed(i)]
    if not pairs:
        return None
    return lax.ppermute(value, axis, pairs)


class Shifts:
    def __init__(self, rows, lanes):
        self.rows = rows
        self.lanes = lanes
        self.lane = lax.broadcasted_iota(jnp.int32, (rows, lanes), 1)
        self.row = lax.broadcasted_iota(jnp.int32, (rows, lanes), 0)
        self.xpos = self.lane % CX
        self.zpos = self.row % 4

    def roll(self, a, shift, axis):
        n = a.shape[axis]
        return pltpu.roll(a, shift % n, a.ndim + axis)

    def ahead(self, direction, a, nbr, placed=False):
        if direction == 0:
            return jnp.where(self.xpos == CX - 1, self.roll(a, CX - 1, -1), self.roll(a, -1, -1))
        if direction == 1:
            half = self.lanes // 2
            if placed and nbr is not None:
                return jnp.where(self.lane >= half, self.roll(nbr, half, -1), self.roll(a, half, -1))
            filled = jnp.where(self.lane < half, 0.0 if nbr is None else nbr, a)
            return self.roll(filled, half, -1)
        if direction == 2:
            inner = self.roll(a, -1, -2)
            outer = 0.0 if nbr is None else (nbr if placed else self.roll(nbr, 3, -2))
            return jnp.where(self.zpos == 3, outer, inner)
        filled = jnp.where(self.row < 4, 0.0 if nbr is None else nbr, a)
        return self.roll(filled, -4, -2)

    def behind(self, direction, a, nbr, placed=False):
        if direction == 0:
            return jnp.where(self.xpos == 0, self.roll(a, 1 - CX, -1), self.roll(a, 1, -1))
        if direction == 1:
            half = self.lanes // 2
            if placed and nbr is not None:
                return jnp.where(self.lane < half, nbr, self.roll(a, half, -1))
            filled = jnp.where(self.lane >= half, 0.0 if nbr is None else nbr, a)
            return self.roll(filled, half, -1)
        if direction == 2:
            inner = self.roll(a, 1, -2)
            outer = 0.0 if nbr is None else (nbr if placed else self.roll(nbr, -3, -2))
            return jnp.where(self.zpos == 0, outer, inner)
        filled = jnp.where(self.row >= self.rows - 4, 0.0 if nbr is None else nbr, a)
        return self.roll(filled, 4, -2)


def hopping(spinor, links, back_links, ahead_list, behind_list):
    hop_total = None
    for direction in range(4):
        ahead_half = colour_product(links[direction], project_minus(direction, ahead_list[direction]), False)
        behind_half = colour_product(back_links[direction], project_plus(direction, behind_list[direction]), True)
        term = rebuild_minus(direction, ahead_half) + rebuild_plus(direction, behind_half)
        hop_total = term if hop_total is None else hop_total + term
    return 4.5 * spinor - 0.5 * hop_total


FACES = ("y_low", "y_high", "z_low", "z_high", "t_low", "t_high")
HALO_KEYS = tuple((side, d) for d in (1, 2, 3) for side in ("ahead", "behind"))


def face_rows(name):
    return {"z_low": (0, 4), "z_high": (3, 4), "t_low": (0, 1), "t_high": (12, 1)}[name]


def place(scratch, value, side, direction):
    if direction == 1:
        scratch[..., pl.ds(0, value.shape[-1])] = value
        return
    start, stride = {("ahead", 2): (3, 4), ("behind", 2): (0, 4), ("ahead", 3): (0, 1), ("behind", 3): (12, 1)}[
        (side, direction)
    ]
    scratch[:, pl.ds(start, 4, stride=stride), :] = value


def pass_kernel(*refs, first, residual_only, present, faces, link_mode, append_links, emit_back, colour_pass):
    refs = list(refs)
    width = 24
    ghost_dirs = [d for d in (1, 2, 3) if link_mode == "combined" and present["behind"][d]]
    link_face_scratch = refs.pop() if append_links and "z_high" in faces else None
    ghost_scratch = {}
    for direction in reversed(ghost_dirs):
        ghost_scratch[direction] = refs.pop()
    scratch_refs = {}
    for key in reversed([k for k in HALO_KEYS if present[k[0]][k[1]]]):
        scratch_refs[key] = refs.pop()
    back_out_ref = refs.pop() if emit_back else None
    face_refs = {}
    for name in reversed(faces):
        face_refs[name] = refs.pop()
    out_ref = refs.pop()

    def take():
        return refs.pop(0)

    src_ref = take()
    links_ref = take()
    back_ref = take() if link_mode == "given" else None
    labels_ref = take()
    colouring_ref = None if residual_only else take()
    spinor_ref = None
    halo_refs = {}
    if not first:
        spinor_ref = take()
        for key in HALO_KEYS:
            if present[key[0]][key[1]]:
                halo_refs[key] = take()

    rows, lanes = src_ref.shape[-2], src_ref.shape[-1]
    sh = Shifts(rows, lanes)
    shape = (2, 4, 3, rows, lanes)
    source = src_ref[...].reshape(shape)
    link_all = links_ref[...].astype(jnp.float32)
    links = [link_all[d].reshape(2, 3, 3, rows, lanes) for d in range(4)]
    if back_ref is not None:
        back_all = back_ref[...].astype(jnp.float32)
        back_links = [back_all[d].reshape(2, 3, 3, rows, lanes) for d in range(4)]
    else:
        back_links = []
        for direction in range(4):
            ghost = None
            if direction in ghost_scratch:
                halo = halo_refs[("behind", direction)]
                place(ghost_scratch[direction], halo[width:], "behind", direction)
                ghost = ghost_scratch[direction][...].reshape(2, 3, 3, rows, lanes)
            back_links.append(sh.behind(direction, links[direction], ghost, True))
    if back_out_ref is not None:
        for direction in range(4):
            back_out_ref[direction] = back_links[direction].reshape(18, rows, lanes).astype(back_out_ref.dtype)

    for key, scratch in scratch_refs.items():
        halo = halo_refs[key]
        value = halo[:width] if (key[0] == "behind" and key[1] in ghost_scratch) else halo[...]
        place(scratch, value, key[0], key[1])

    def load_halo(side, direction):
        ref = scratch_refs.get((side, direction), halo_refs.get((side, direction)))
        return None if ref is None else ref[...].reshape(shape)

    def wilson_global(spinor):
        ahead_list = [sh.ahead(d, spinor, load_halo("ahead", d), True) for d in range(4)]
        behind_list = [sh.behind(d, spinor, load_halo("behind", d), True) for d in range(4)]
        return hopping(spinor, links, back_links, ahead_list, behind_list)

    if first:
        residue = source
        current = None
    else:
        current = spinor_ref[...].reshape(shape)
        residue = source - wilson_global(current)
    if residual_only:
        out_ref[...] = residue.reshape(out_ref.shape).astype(out_ref.dtype)
        return

    label_index = labels_ref[...]
    labels = (label_index + 1).astype(jnp.float32)
    ahead_masks = [(sh.ahead(d, labels, None) == labels).astype(jnp.float32) for d in range(4)]
    behind_masks = [(sh.behind(d, labels, None) == labels).astype(jnp.float32) for d in range(4)]
    member_bool = label_index[None] == lax.broadcasted_iota(jnp.int32, (AGG, 1, 1), 0)
    member = member_bool.astype(jnp.float32)
    site_colour = jnp.zeros((rows, lanes), jnp.int32)
    for block in range(AGG):
        site_colour = jnp.where(label_index == block, colouring_ref[block], site_colour)
    colour_mask = (site_colour == colour_pass).astype(jnp.float32)

    def wilson_block(spinor):
        ahead_list = [sh.ahead(d, spinor, None) * ahead_masks[d] for d in range(4)]
        behind_list = [sh.behind(d, spinor, None) * behind_masks[d] for d in range(4)]
        return hopping(spinor, links, back_links, ahead_list, behind_list)

    def block_total(values):
        return jnp.sum(jnp.sum(member * values[None], axis=2, keepdims=True), axis=1, keepdims=True)

    update = None
    remainder = residue
    for repeat in range(MR_STEPS):
        image = wilson_block(remainder)
        image_flat = image.reshape(2, 12, rows, lanes)
        rest_flat = remainder.reshape(2, 12, rows, lanes)
        dot_real = jnp.sum(image_flat[0] * rest_flat[0] + image_flat[1] * rest_flat[1], axis=0)
        dot_imag = jnp.sum(image_flat[0] * rest_flat[1] - image_flat[1] * rest_flat[0], axis=0)
        norm = jnp.sum(image_flat[0] * image_flat[0] + image_flat[1] * image_flat[1], axis=0)
        denominator = block_total(norm) + 1e-06
        factor_real = jnp.sum(member * (block_total(dot_real) / denominator), axis=0)
        factor_imag = jnp.sum(member * (block_total(dot_imag) / denominator), axis=0)
        step = complex_scale(factor_real, factor_imag, remainder)
        update = step if update is None else update + step
        remainder = remainder - complex_scale(factor_real, factor_imag, image)
    update = update * colour_mask
    result = update if current is None else current + update
    out_ref[...] = result.reshape(out_ref.shape)
    if link_face_scratch is not None:
        link_face_scratch[...] = link_all[2]
    for name, face_ref in face_refs.items():
        if name == "y_low":
            face_ref[...] = out_ref[:, :, pl.ds(0, lanes // 2)]
        elif name == "y_high":
            face_ref[0:width] = pltpu.roll(out_ref[...], lanes // 2, 2)[:, :, : lanes // 2]
            if append_links:
                face_ref[width:] = pltpu.roll(link_all[1], lanes // 2, 2)[:, :, : lanes // 2]
        else:
            start, stride = face_rows(name)
            face_ref[0:width] = out_ref[:, pl.ds(start, 4, stride=stride), :]
            if append_links and name == "z_high":
                face_ref[width:] = link_face_scratch[:, pl.ds(start, 4, stride=stride), :]
            elif append_links and name == "t_high":
                face_ref[width:] = link_all[3][:, start:start + 4, :]


def run_pass(source, links, back, labels, colouring, colour_pass, spinor, halos, residual_only=False, faces=(),
             link_mode="given", append_links=False, emit_back=False):
    first = spinor is None
    present = {
        "ahead": [h is not None for h in halos["ahead"]] if not first else [False] * 4,
        "behind": [h is not None for h in halos["behind"]] if not first else [False] * 4,
    }
    operands = [source, links] + ([back] if link_mode == "given" else []) + [labels]
    spaces = [pltpu.VMEM] * len(operands)
    if not residual_only:
        operands.append(colouring)
        spaces.append(pltpu.SMEM)
    if not first:
        operands.append(spinor)
        for key in HALO_KEYS:
            if present[key[0]][key[1]]:
                operands.append(halos[key[0]][key[1]])
    spaces += [pltpu.VMEM] * (len(operands) - len(spaces))
    kernel = functools.partial(
        pass_kernel, first=first, residual_only=residual_only, present=present, faces=faces,
        link_mode=link_mode, append_links=append_links, emit_back=emit_back, colour_pass=colour_pass,
    )
    width = source.shape[0]

    def face_shape(name):
        rows = width + (18 if append_links and name.endswith("high") else 0)
        if name.startswith("y"):
            return (rows, source.shape[1], source.shape[2] // 2)
        return (rows, 4, source.shape[2])

    out_shape = [jax.ShapeDtypeStruct(source.shape, jnp.bfloat16 if residual_only else jnp.float32)]
    out_shape += [jax.ShapeDtypeStruct(face_shape(name), jnp.float32) for name in faces]
    if emit_back:
        out_shape.append(jax.ShapeDtypeStruct(links.shape, links.dtype))
    scratch = [pltpu.VMEM(source.shape, jnp.float32) for k in HALO_KEYS if present[k[0]][k[1]]]
    if link_mode == "combined":
        scratch += [pltpu.VMEM(links.shape[1:], jnp.float32) for d in (1, 2, 3) if present["behind"][d]]
    if append_links and "z_high" in faces:
        scratch.append(pltpu.VMEM(links.shape[1:], jnp.float32))
    in_specs = [pl.BlockSpec(memory_space=space) for space in spaces]
    results = pl.pallas_call(kernel, out_shape=out_shape, scratch_shapes=scratch, in_specs=in_specs)(*operands)
    face_values = dict(zip(faces, results[1:1 + len(faces)]))
    return results[0], face_values, (results[-1] if emit_back else None)


def coarse_kernel(*refs, present):
    refs = list(refs)
    out_ref = refs.pop()
    source_ref, inverse_ref = refs[0], refs[1]
    first = len(refs) == 2
    width = source_ref.shape[-1]
    chunks = width // 128
    lane = lax.broadcasted_iota(jnp.int32, (1, width), 1)
    position = lane % AGG
    selector = (
        lax.broadcasted_iota(jnp.int32, (8, 128), 1) // AGG == lax.broadcasted_iota(jnp.int32, (8, 128), 0)
    ).astype(jnp.float32)

    def reduce_flat(product):
        partial = product[:, 0:128]
        for q in range(1, chunks):
            partial = partial + product[:, q * 128:(q + 1) * 128]
        for shift in (64, 32, 16):
            partial = partial + pltpu.roll(partial, shift, 1)
        pieces = [
            jnp.sum(partial[8 * q:8 * q + 8] * selector, axis=0, keepdims=True) for q in range(chunks)
        ]
        return jnp.concatenate(pieces, axis=1)

    def roll_within(vector, shift):
        pieces = [pltpu.roll(vector[:, q * 128:(q + 1) * 128], shift % 128, 1) for q in range(chunks)]
        return jnp.concatenate(pieces, axis=1)

    def accumulate(acc, blocks_ref, index, vector):
        block_real = blocks_ref[index + (0,)].astype(jnp.float32)
        block_imag = blocks_ref[index + (1,)].astype(jnp.float32)
        real_part = block_real * vector[0] - block_imag * vector[1]
        imag_part = block_real * vector[1] + block_imag * vector[0]
        if acc is None:
            return [real_part, imag_part]
        return [acc[0] + real_part, acc[1] + imag_part]

    def precondition(vector):
        acc = accumulate(None, inverse_ref, (), vector)
        return [reduce_flat(acc[0]), reduce_flat(acc[1])]

    source = [source_ref[0], source_ref[1]]
    if first:
        result = precondition(source)
    else:
        operator_ref, current_ref = refs[2], refs[3]
        nearby_refs = refs[4:]
        current = [current_ref[0], current_ref[1]]
        ahead = [
            jnp.where(position == AGG - 1, roll_within(c, AGG - 1), roll_within(c, -1)) for c in current
        ]
        behind = [jnp.where(position == 0, roll_within(c, 1 - AGG), roll_within(c, 1)) for c in current]
        vectors = [current, ahead, behind]
        taken = 0
        for flag in present:
            if flag:
                vectors.append([nearby_refs[taken][0], nearby_refs[taken][1]])
                taken += 1
            else:
                vectors.append(None)
        acc = None
        for direction, vector in enumerate(vectors):
            if vector is not None:
                acc = accumulate(acc, operator_ref, (direction,), vector)
        residue = [source[0] - reduce_flat(acc[0]), source[1] - reduce_flat(acc[1])]
        step = precondition(residue)
        result = [current[0] + step[0], current[1] + step[1]]
    out_ref[0] = result[0]
    out_ref[1] = result[1]


def run_coarse(source, inverse_blocks, operator_blocks, current, nearby):
    operands = [source, inverse_blocks]
    present = ()
    if current is not None:
        present = tuple(v is not None for v in nearby)
        operands += [operator_blocks, current] + [v for v in nearby if v is not None]
    kernel = functools.partial(coarse_kernel, present=present)
    return pl.pallas_call(kernel, out_shape=jax.ShapeDtypeStruct(source.shape, jnp.float32))(*operands)


def body(
    fine_source, links, test_vectors, aggregate_map, colouring, coarse_operator, block_inverse
):
    time_extent = fine_source.shape[2]
    plane_extent = fine_source.shape[3]
    line_extent = fine_source.shape[4]
    rows = time_extent * plane_extent
    site_count = rows * line_extent
    domain_index = lax.axis_index("lat")
    domain_count = lax.axis_size("lat")
    plane_position = (domain_index + 2) % PZ
    upper_valid = plane_position < PZ - 1
    lower_valid = plane_position > 0
    later_valid = domain_index < domain_count - PZ
    earlier_valid = domain_index >= PZ

    source = fine_source.reshape(24, rows, line_extent)
    link_rows = links.reshape(4, 18, rows, line_extent)
    label_rows = aggregate_map.reshape(rows, line_extent)
    member = (label_rows[None] == jnp.arange(AGG, dtype=jnp.int32)[:, None, None]).astype(jnp.float32)
    colour_list = colouring.reshape(AGG)

    def z_up_ok(i):
        return (i + 2) % PZ != PZ - 1

    def z_down_ok(i):
        return (i + 2) % PZ != 0

    def t_up_ok(i):
        return i + PZ < domain_count

    def t_down_ok(i):
        return i - PZ >= 0

    half = line_extent // 2

    needed = ["y_low", "y_high"] + [
        name for name, ok in zip(FACES[2:], (z_up_ok, z_down_ok, t_up_ok, t_down_ok))
        if any(ok(i) for i in range(domain_count))
    ]

    def faces_of(spinor):
        result = {"y_low": spinor[..., :half], "y_high": spinor[..., half:]}
        for name in needed[2:]:
            start, stride = face_rows(name)
            result[name] = lax.slice_in_dim(spinor, start, start + 3 * stride + 1, stride, axis=1)
        return result

    def halos_of(spinor, faces):
        def face(name):
            return faces[name] if name in faces else None

        return {
            "ahead": [
                None,
                permute_from(faces["y_low"], "grp", 1, lambda i: True),
                permute_from(face("z_low"), "lat", 1, z_up_ok) if face("z_low") is not None else None,
                permute_from(face("t_low"), "lat", PZ, t_up_ok) if face("t_low") is not None else None,
            ],
            "behind": [
                None,
                permute_from(faces["y_high"], "grp", -1, lambda i: True),
                permute_from(face("z_high"), "lat", -1, z_down_ok) if face("z_high") is not None else None,
                permute_from(face("t_high"), "lat", -PZ, t_down_ok) if face("t_high") is not None else None,
            ],
        }

    smoothed_first, first_faces, _ = run_pass(
        source, link_rows, None, label_rows, colour_list, 0, None, None,
        faces=tuple(needed), link_mode="none", append_links=True,
    )
    vectors = test_vectors.reshape(NVEC, 2, 2, 6, site_count)
    vectors, smoothed_first = lax.optimization_barrier((vectors, smoothed_first))
    smoothed, smoothed_faces, back_rows = run_pass(
        source, link_rows, None, label_rows, colour_list, 1, smoothed_first,
        halos_of(smoothed_first, first_faces), faces=tuple(needed), link_mode="combined", emit_back=True,
    )

    def sweep(start, faces):
        current, current_faces, _ = run_pass(
            source, link_rows, back_rows, label_rows, colour_list, 0, start, halos_of(start, faces),
            faces=tuple(needed),
        )
        result, _, _ = run_pass(
            source, link_rows, back_rows, label_rows, colour_list, 1, current,
            halos_of(current, current_faces),
        )
        return result

    residue, _, _ = run_pass(
        source, link_rows, back_rows, label_rows, None, None, smoothed, halos_of(smoothed, smoothed_faces),
        residual_only=True,
    )
    residual = residue
    membership = member.reshape(AGG, site_count).T
    member_weights = membership.astype(jnp.bfloat16)
    weighted = residual.reshape(2, 2, 6, site_count)[..., None] * member_weights

    pairs = jnp.einsum("krxqn,sxqnj->rsxkj", vectors, weighted, preferred_element_type=jnp.float32)
    real_part = pairs[0, 0] + pairs[1, 1]
    imag_part = pairs[0, 1] - pairs[1, 0]
    coarse_source = jnp.stack([real_part, imag_part]).reshape(2, CDOF, AGG)
    flat_source = coarse_source.reshape(2, 1, CDOF * AGG)
    operator_blocks = coarse_operator.reshape(9, 2, CDOF, CDOF * AGG)
    inverse_blocks = block_inverse.reshape(2, CDOF, CDOF * AGG)
    correction = run_coarse(flat_source, inverse_blocks, operator_blocks, None, None)
    for repeat in range(2):
        nearby = [
            permute_from(correction, "grp", 1, lambda i: True),
            permute_from(correction, "grp", -1, lambda i: True),
            permute_from(correction, "lat", 1, z_up_ok),
            permute_from(correction, "lat", -1, z_down_ok),
            permute_from(correction, "lat", PZ, t_up_ok),
            permute_from(correction, "lat", -PZ, t_down_ok),
        ]
        correction = run_coarse(flat_source, inverse_blocks, operator_blocks, correction, nearby)
    correction = correction.reshape(2, CDOF, AGG)
    expanded = jnp.dot(
        correction.reshape(2 * CDOF, AGG), membership.T, precision=lax.Precision.HIGH
    ).reshape(2, 2, NVEC, site_count)
    spread_real = jnp.swapaxes(expanded[0], 0, 1)[:, :, None]
    spread_imag = jnp.swapaxes(expanded[1], 0, 1)[:, :, None]
    real_part = jnp.sum(vectors[:, 0] * spread_real - vectors[:, 1] * spread_imag, axis=0)
    imag_part = jnp.sum(vectors[:, 0] * spread_imag + vectors[:, 1] * spread_real, axis=0)
    corrected = smoothed + jnp.stack([real_part, imag_part]).reshape(24, rows, line_extent)
    solution = sweep(corrected, faces_of(corrected))
    return (
        solution.reshape(1, 24, time_extent, plane_extent, line_extent),
        correction.reshape(1, 1, 2, CDOF, AGG),
    )


def solution(mesh):
    return jax.shard_map(
        body,
        mesh=mesh,
        in_specs=(
            P("lat", None, None, None, "grp"),
            P("lat", None, None, None, None, "grp"),
            P("lat", None, None, None, None, "grp"),
            P("lat", None, None, "grp", None),
            P("lat", "grp", None),
            P("lat", "grp", None, None, None, None),
            P("lat", "grp", None, None, None),
        ),
        out_specs=(P("lat", None, None, None, "grp"), P("lat", "grp", None, None, None)),
        check_vma=False,
    )
```

```python
import functools

import jax
import jax.numpy as jnp
from jax import lax
from jax.experimental import pallas as pl
from jax.experimental.pallas import tpu as pltpu
from jax.sharding import PartitionSpec as P

CX = 64
PZ = 8
NVEC = 24
AGG = 16
MR_STEPS = 2
CDOF = 48


def passed_along(shard, axis, by):
    size = lax.axis_size(axis)
    return lax.ppermute(shard, axis, [(i, (i + by) % size) for i in range(size)])


def padded_2(shard, sides, width):
    for axis, dim in sides:
        size, length = (lax.axis_size(axis), shard.shape[dim])
        up = [(i, (i + 1) % size) for i in range(size)]
        down = [(j, i) for i, j in up]
        last = lax.slice_in_dim(shard, length - width, length, axis=dim)
        first = lax.slice_in_dim(shard, 0, width, axis=dim)
        before = lax.ppermute(last, axis, up)
        after = lax.ppermute(first, axis, down)
        shard = jnp.concatenate([before, shard, after], axis=dim)
    return shard


def times_minus_i(values):
    return jnp.stack([values[1], -values[0]])


def times_plus_i(values):
    return jnp.stack([-values[1], values[0]])


def spin_factor(direction, spin_pair):
    if direction == 0:
        return jnp.stack([times_minus_i(spin_pair[:, 1]), times_minus_i(spin_pair[:, 0])], axis=1)
    if direction == 1:
        return jnp.stack([-spin_pair[:, 1], spin_pair[:, 0]], axis=1)
    if direction == 2:
        return jnp.stack([times_minus_i(spin_pair[:, 0]), times_plus_i(spin_pair[:, 1])], axis=1)
    return spin_pair


def project_minus(direction, spinor):
    return spinor[:, :2] - spin_factor(direction, spinor[:, 2:])


def project_plus(direction, spinor):
    return spinor[:, :2] + spin_factor(direction, spinor[:, 2:])


def rebuild_minus(direction, half_spinor):
    lower_part = spin_factor(direction, half_spinor) if direction < 3 else -half_spinor
    return jnp.concatenate([half_spinor, lower_part], axis=1)


def rebuild_plus(direction, half_spinor):
    lower_part = -spin_factor(direction, half_spinor) if direction < 3 else half_spinor
    return jnp.concatenate([half_spinor, lower_part], axis=1)


def colour_product(gauge_link, half_spinor, adjoint):
    link_real = gauge_link[0]
    link_imag = gauge_link[1]
    if adjoint:
        link_real = jnp.swapaxes(link_real, 0, 1)
        link_imag = -jnp.swapaxes(link_imag, 0, 1)
    spin_real = half_spinor[0][:, None]
    spin_imag = half_spinor[1][:, None]
    real_part = jnp.sum(link_real[None] * spin_real - link_imag[None] * spin_imag, axis=2)
    imag_part = jnp.sum(link_real[None] * spin_imag + link_imag[None] * spin_real, axis=2)
    return jnp.stack([real_part, imag_part])


def complex_scale(factor_real, factor_imag, lattice):
    return jnp.stack(
        [
            factor_real * lattice[0] - factor_imag * lattice[1],
            factor_real * lattice[1] + factor_imag * lattice[0],
        ]
    )


def apply_blocks(blocks, nearby):
    matrices = blocks.reshape(blocks.shape[0], 2, CDOF, CDOF, AGG)
    vector_real = nearby[:, 0][:, None]
    vector_imag = nearby[:, 1][:, None]
    real_part = jnp.sum(matrices[:, 0] * vector_real - matrices[:, 1] * vector_imag, axis=(0, 2))
    imag_part = jnp.sum(matrices[:, 0] * vector_imag + matrices[:, 1] * vector_real, axis=(0, 2))
    return jnp.stack([real_part, imag_part])


def keep_if(allowed, values):
    return jnp.where(allowed, values, jnp.zeros_like(values))


def permute_from(value, axis, offset, allowed):
    size = lax.axis_size(axis)
    pairs = [((i + offset) % size, i) for i in range(size) if allowed(i)]
    if not pairs:
        return None
    return lax.ppermute(value, axis, pairs)


class Shifts:
    def __init__(self, rows, lanes):
        self.rows = rows
        self.lanes = lanes
        self.lane = lax.broadcasted_iota(jnp.int32, (rows, lanes), 1)
        self.row = lax.broadcasted_iota(jnp.int32, (rows, lanes), 0)
        self.xpos = self.lane % CX
        self.zpos = self.row % 4

    def roll(self, a, shift, axis):
        n = a.shape[axis]
        return pltpu.roll(a, shift % n, a.ndim + axis)

    def ahead(self, direction, a, nbr, placed=False):
        if direction == 0:
            return jnp.where(self.xpos == CX - 1, self.roll(a, CX - 1, -1), self.roll(a, -1, -1))
        if direction == 1:
            half = self.lanes // 2
            if placed and nbr is not None:
                return jnp.where(self.lane >= half, self.roll(nbr, half, -1), self.roll(a, half, -1))
            filled = jnp.where(self.lane < half, 0.0 if nbr is None else nbr, a)
            return self.roll(filled, half, -1)
        if direction == 2:
            inner = self.roll(a, -1, -2)
            outer = 0.0 if nbr is None else (nbr if placed else self.roll(nbr, 3, -2))
            return jnp.where(self.zpos == 3, outer, inner)
        filled = jnp.where(self.row < 4, 0.0 if nbr is None else nbr, a)
        return self.roll(filled, -4, -2)

    def behind(self, direction, a, nbr, placed=False):
        if direction == 0:
            return jnp.where(self.xpos == 0, self.roll(a, 1 - CX, -1), self.roll(a, 1, -1))
        if direction == 1:
            half = self.lanes // 2
            if placed and nbr is not None:
                return jnp.where(self.lane < half, nbr, self.roll(a, half, -1))
            filled = jnp.where(self.lane >= half, 0.0 if nbr is None else nbr, a)
            return self.roll(filled, half, -1)
        if direction == 2:
            inner = self.roll(a, 1, -2)
            outer = 0.0 if nbr is None else (nbr if placed else self.roll(nbr, -3, -2))
            return jnp.where(self.zpos == 0, outer, inner)
        filled = jnp.where(self.row >= self.rows - 4, 0.0 if nbr is None else nbr, a)
        return self.roll(filled, 4, -2)


def hopping(spinor, links, back_links, ahead_list, behind_list):
    hop_total = None
    for direction in range(4):
        ahead_half = colour_product(links[direction], project_minus(direction, ahead_list[direction]), False)
        behind_half = colour_product(back_links[direction], project_plus(direction, behind_list[direction]), True)
        term = rebuild_minus(direction, ahead_half) + rebuild_plus(direction, behind_half)
        hop_total = term if hop_total is None else hop_total + term
    return 4.5 * spinor - 0.5 * hop_total


FACES = ("y_low", "y_high", "z_low", "z_high", "t_low", "t_high")
HALO_KEYS = tuple((side, d) for d in (1, 2, 3) for side in ("ahead", "behind"))


def face_rows(name):
    return {"z_low": (0, 4), "z_high": (3, 4), "t_low": (0, 1), "t_high": (12, 1)}[name]


def place(scratch, value, side, direction):
    if direction == 1:
        scratch[..., pl.ds(0, value.shape[-1])] = value
        return
    start, stride = {("ahead", 2): (3, 4), ("behind", 2): (0, 4), ("ahead", 3): (0, 1), ("behind", 3): (12, 1)}[
        (side, direction)
    ]
    scratch[:, pl.ds(start, 4, stride=stride), :] = value


def pass_kernel(*refs, first, residual_only, present, faces, link_mode, append_links, emit_back, colour_pass):
    refs = list(refs)
    width = 24
    ghost_dirs = [d for d in (1, 2, 3) if link_mode == "combined" and present["behind"][d]]
    link_face_scratch = refs.pop() if append_links and "z_high" in faces else None
    ghost_scratch = {}
    for direction in reversed(ghost_dirs):
        ghost_scratch[direction] = refs.pop()
    scratch_refs = {}
    for key in reversed([k for k in HALO_KEYS if present[k[0]][k[1]]]):
        scratch_refs[key] = refs.pop()
    back_out_ref = refs.pop() if emit_back else None
    face_refs = {}
    for name in reversed(faces):
        face_refs[name] = refs.pop()
    out_ref = refs.pop()

    def take():
        return refs.pop(0)

    src_ref = take()
    links_ref = take()
    back_ref = take() if link_mode == "given" else None
    labels_ref = take()
    colouring_ref = None if residual_only else take()
    spinor_ref = None
    halo_refs = {}
    if not first:
        spinor_ref = take()
        for key in HALO_KEYS:
            if present[key[0]][key[1]]:
                halo_refs[key] = take()

    rows, lanes = src_ref.shape[-2], src_ref.shape[-1]
    sh = Shifts(rows, lanes)
    shape = (2, 4, 3, rows, lanes)
    source = src_ref[...].reshape(shape)
    link_all = links_ref[...].astype(jnp.float32)
    links = [link_all[d].reshape(2, 3, 3, rows, lanes) for d in range(4)]
    if back_ref is not None:
        back_all = back_ref[...].astype(jnp.float32)
        back_links = [back_all[d].reshape(2, 3, 3, rows, lanes) for d in range(4)]
    else:
        back_links = []
        for direction in range(4):
            ghost = None
            if direction in ghost_scratch:
                halo = halo_refs[("behind", direction)]
                place(ghost_scratch[direction], halo[width:], "behind", direction)
                ghost = ghost_scratch[direction][...].reshape(2, 3, 3, rows, lanes)
            back_links.append(sh.behind(direction, links[direction], ghost, True))
    if back_out_ref is not None:
        for direction in range(4):
            back_out_ref[direction] = back_links[direction].reshape(18, rows, lanes).astype(back_out_ref.dtype)

    for key, scratch in scratch_refs.items():
        halo = halo_refs[key]
        value = halo[:width] if (key[0] == "behind" and key[1] in ghost_scratch) else halo[...]
        place(scratch, value, key[0], key[1])

    def load_halo(side, direction):
        ref = scratch_refs.get((side, direction), halo_refs.get((side, direction)))
        return None if ref is None else ref[...].reshape(shape)

    def wilson_global(spinor):
        ahead_list = [sh.ahead(d, spinor, load_halo("ahead", d), True) for d in range(4)]
        behind_list = [sh.behind(d, spinor, load_halo("behind", d), True) for d in range(4)]
        return hopping(spinor, links, back_links, ahead_list, behind_list)

    if first:
        residue = source
        current = None
    else:
        current = spinor_ref[...].reshape(shape)
        residue = source - wilson_global(current)
    if residual_only:
        out_ref[...] = residue.reshape(out_ref.shape).astype(out_ref.dtype)
        return

    label_index = labels_ref[...]
    labels = (label_index + 1).astype(jnp.float32)
    ahead_masks = [(sh.ahead(d, labels, None) == labels).astype(jnp.float32) for d in range(4)]
    behind_masks = [(sh.behind(d, labels, None) == labels).astype(jnp.float32) for d in range(4)]
    member_bool = label_index[None] == lax.broadcasted_iota(jnp.int32, (AGG, 1, 1), 0)
    member = member_bool.astype(jnp.float32)
    site_colour = jnp.zeros((rows, lanes), jnp.int32)
    for block in range(AGG):
        site_colour = jnp.where(label_index == block, colouring_ref[block], site_colour)
    colour_mask = (site_colour == colour_pass).astype(jnp.float32)

    def wilson_block(spinor):
        ahead_list = [sh.ahead(d, spinor, None) * ahead_masks[d] for d in range(4)]
        behind_list = [sh.behind(d, spinor, None) * behind_masks[d] for d in range(4)]
        return hopping(spinor, links, back_links, ahead_list, behind_list)

    def block_total(values):
        return jnp.sum(member * values[None], axis=(1, 2), keepdims=True)

    update = None
    remainder = residue
    for repeat in range(MR_STEPS):
        image = wilson_block(remainder)
        image_flat = image.reshape(2, 12, rows, lanes)
        rest_flat = remainder.reshape(2, 12, rows, lanes)
        dot_real = jnp.sum(image_flat[0] * rest_flat[0] + image_flat[1] * rest_flat[1], axis=0)
        dot_imag = jnp.sum(image_flat[0] * rest_flat[1] - image_flat[1] * rest_flat[0], axis=0)
        norm = jnp.sum(image_flat[0] * image_flat[0] + image_flat[1] * image_flat[1], axis=0)
        denominator = block_total(norm) + 1e-06
        factor_real = jnp.sum(member * (block_total(dot_real) / denominator), axis=0)
        factor_imag = jnp.sum(member * (block_total(dot_imag) / denominator), axis=0)
        step = complex_scale(factor_real, factor_imag, remainder)
        update = step if update is None else update + step
        remainder = remainder - complex_scale(factor_real, factor_imag, image)
    update = update * colour_mask
    result = update if current is None else current + update
    out_ref[...] = result.reshape(out_ref.shape)
    if link_face_scratch is not None:
        link_face_scratch[...] = link_all[2]
    for name, face_ref in face_refs.items():
        if name == "y_low":
            face_ref[...] = out_ref[:, :, pl.ds(0, lanes // 2)]
        elif name == "y_high":
            face_ref[0:width] = pltpu.roll(out_ref[...], lanes // 2, 2)[:, :, : lanes // 2]
            if append_links:
                face_ref[width:] = pltpu.roll(link_all[1], lanes // 2, 2)[:, :, : lanes // 2]
        else:
            start, stride = face_rows(name)
            face_ref[0:width] = out_ref[:, pl.ds(start, 4, stride=stride), :]
            if append_links and name == "z_high":
                face_ref[width:] = link_face_scratch[:, pl.ds(start, 4, stride=stride), :]
            elif append_links and name == "t_high":
                face_ref[width:] = link_all[3][:, start:start + 4, :]


def run_pass(source, links, back, labels, colouring, colour_pass, spinor, halos, residual_only=False, faces=(),
             link_mode="given", append_links=False, emit_back=False):
    first = spinor is None
    present = {
        "ahead": [h is not None for h in halos["ahead"]] if not first else [False] * 4,
        "behind": [h is not None for h in halos["behind"]] if not first else [False] * 4,
    }
    operands = [source, links] + ([back] if link_mode == "given" else []) + [labels]
    spaces = [pltpu.VMEM] * len(operands)
    if not residual_only:
        operands.append(colouring)
        spaces.append(pltpu.SMEM)
    if not first:
        operands.append(spinor)
        for key in HALO_KEYS:
            if present[key[0]][key[1]]:
                operands.append(halos[key[0]][key[1]])
    spaces += [pltpu.VMEM] * (len(operands) - len(spaces))
    kernel = functools.partial(
        pass_kernel, first=first, residual_only=residual_only, present=present, faces=faces,
        link_mode=link_mode, append_links=append_links, emit_back=emit_back, colour_pass=colour_pass,
    )
    width = source.shape[0]

    def face_shape(name):
        rows = width + (18 if append_links and name.endswith("high") else 0)
        if name.startswith("y"):
            return (rows, source.shape[1], source.shape[2] // 2)
        return (rows, 4, source.shape[2])

    out_shape = [jax.ShapeDtypeStruct(source.shape, jnp.bfloat16 if residual_only else jnp.float32)]
    out_shape += [jax.ShapeDtypeStruct(face_shape(name), jnp.float32) for name in faces]
    if emit_back:
        out_shape.append(jax.ShapeDtypeStruct(links.shape, links.dtype))
    scratch = [pltpu.VMEM(source.shape, jnp.float32) for k in HALO_KEYS if present[k[0]][k[1]]]
    if link_mode == "combined":
        scratch += [pltpu.VMEM(links.shape[1:], jnp.float32) for d in (1, 2, 3) if present["behind"][d]]
    if append_links and "z_high" in faces:
        scratch.append(pltpu.VMEM(links.shape[1:], jnp.float32))
    in_specs = [pl.BlockSpec(memory_space=space) for space in spaces]
    results = pl.pallas_call(kernel, out_shape=out_shape, scratch_shapes=scratch, in_specs=in_specs)(*operands)
    face_values = dict(zip(faces, results[1:1 + len(faces)]))
    return results[0], face_values, (results[-1] if emit_back else None)


def coarse_kernel(*refs, present):
    refs = list(refs)
    out_ref = refs.pop()
    source_ref, inverse_ref = refs[0], refs[1]
    first = len(refs) == 2
    width = source_ref.shape[-1]
    chunks = width // 128
    lane = lax.broadcasted_iota(jnp.int32, (1, width), 1)
    position = lane % AGG
    selector = (
        lax.broadcasted_iota(jnp.int32, (8, 128), 1) // AGG == lax.broadcasted_iota(jnp.int32, (8, 128), 0)
    ).astype(jnp.float32)

    def reduce_flat(product):
        partial = product[:, 0:128]
        for q in range(1, chunks):
            partial = partial + product[:, q * 128:(q + 1) * 128]
        for shift in (64, 32, 16):
            partial = partial + pltpu.roll(partial, shift, 1)
        pieces = [
            jnp.sum(partial[8 * q:8 * q + 8] * selector, axis=0, keepdims=True) for q in range(chunks)
        ]
        return jnp.concatenate(pieces, axis=1)

    def roll_within(vector, shift):
        pieces = [pltpu.roll(vector[:, q * 128:(q + 1) * 128], shift % 128, 1) for q in range(chunks)]
        return jnp.concatenate(pieces, axis=1)

    def accumulate(acc, blocks_ref, index, vector):
        block_real = blocks_ref[index + (0,)].astype(jnp.float32)
        block_imag = blocks_ref[index + (1,)].astype(jnp.float32)
        real_part = block_real * vector[0] - block_imag * vector[1]
        imag_part = block_real * vector[1] + block_imag * vector[0]
        if acc is None:
            return [real_part, imag_part]
        return [acc[0] + real_part, acc[1] + imag_part]

    def precondition(vector):
        acc = accumulate(None, inverse_ref, (), vector)
        return [reduce_flat(acc[0]), reduce_flat(acc[1])]

    source = [source_ref[0], source_ref[1]]
    if first:
        result = precondition(source)
    else:
        operator_ref, current_ref = refs[2], refs[3]
        nearby_refs = refs[4:]
        current = [current_ref[0], current_ref[1]]
        ahead = [
            jnp.where(position == AGG - 1, roll_within(c, AGG - 1), roll_within(c, -1)) for c in current
        ]
        behind = [jnp.where(position == 0, roll_within(c, 1 - AGG), roll_within(c, 1)) for c in current]
        vectors = [current, ahead, behind]
        taken = 0
        for flag in present:
            if flag:
                vectors.append([nearby_refs[taken][0], nearby_refs[taken][1]])
                taken += 1
            else:
                vectors.append(None)
        acc = None
        for direction, vector in enumerate(vectors):
            if vector is not None:
                acc = accumulate(acc, operator_ref, (direction,), vector)
        residue = [source[0] - reduce_flat(acc[0]), source[1] - reduce_flat(acc[1])]
        step = precondition(residue)
        result = [current[0] + step[0], current[1] + step[1]]
    out_ref[0] = result[0]
    out_ref[1] = result[1]


def run_coarse(source, inverse_blocks, operator_blocks, current, nearby):
    operands = [source, inverse_blocks]
    present = ()
    if current is not None:
        present = tuple(v is not None for v in nearby)
        operands += [operator_blocks, current] + [v for v in nearby if v is not None]
    kernel = functools.partial(coarse_kernel, present=present)
    return pl.pallas_call(kernel, out_shape=jax.ShapeDtypeStruct(source.shape, jnp.float32))(*operands)


def body(
    fine_source, links, test_vectors, aggregate_map, colouring, coarse_operator, block_inverse
):
    time_extent = fine_source.shape[2]
    plane_extent = fine_source.shape[3]
    line_extent = fine_source.shape[4]
    rows = time_extent * plane_extent
    site_count = rows * line_extent
    domain_index = lax.axis_index("lat")
    domain_count = lax.axis_size("lat")
    plane_position = (domain_index + 2) % PZ
    upper_valid = plane_position < PZ - 1
    lower_valid = plane_position > 0
    later_valid = domain_index < domain_count - PZ
    earlier_valid = domain_index >= PZ

    source = fine_source.reshape(24, rows, line_extent)
    link_rows = links.reshape(4, 18, rows, line_extent)
    label_rows = aggregate_map.reshape(rows, line_extent)
    member = (label_rows[None] == jnp.arange(AGG, dtype=jnp.int32)[:, None, None]).astype(jnp.float32)
    colour_list = colouring.reshape(AGG)

    def z_up_ok(i):
        return (i + 2) % PZ != PZ - 1

    def z_down_ok(i):
        return (i + 2) % PZ != 0

    def t_up_ok(i):
        return i + PZ < domain_count

    def t_down_ok(i):
        return i - PZ >= 0

    half = line_extent // 2

    needed = ["y_low", "y_high"] + [
        name for name, ok in zip(FACES[2:], (z_up_ok, z_down_ok, t_up_ok, t_down_ok))
        if any(ok(i) for i in range(domain_count))
    ]

    def faces_of(spinor):
        result = {"y_low": spinor[..., :half], "y_high": spinor[..., half:]}
        for name in needed[2:]:
            start, stride = face_rows(name)
            result[name] = lax.slice_in_dim(spinor, start, start + 3 * stride + 1, stride, axis=1)
        return result

    def halos_of(spinor, faces):
        def face(name):
            return faces[name] if name in faces else None

        return {
            "ahead": [
                None,
                permute_from(faces["y_low"], "grp", 1, lambda i: True),
                permute_from(face("z_low"), "lat", 1, z_up_ok) if face("z_low") is not None else None,
                permute_from(face("t_low"), "lat", PZ, t_up_ok) if face("t_low") is not None else None,
            ],
            "behind": [
                None,
                permute_from(faces["y_high"], "grp", -1, lambda i: True),
                permute_from(face("z_high"), "lat", -1, z_down_ok) if face("z_high") is not None else None,
                permute_from(face("t_high"), "lat", -PZ, t_down_ok) if face("t_high") is not None else None,
            ],
        }

    smoothed_first, first_faces, _ = run_pass(
        source, link_rows, None, label_rows, colour_list, 0, None, None,
        faces=tuple(needed), link_mode="none", append_links=True,
    )
    vectors = test_vectors.reshape(NVEC, 2, 2, 6, site_count)
    vectors, smoothed_first = lax.optimization_barrier((vectors, smoothed_first))
    smoothed, smoothed_faces, back_rows = run_pass(
        source, link_rows, None, label_rows, colour_list, 1, smoothed_first,
        halos_of(smoothed_first, first_faces), faces=tuple(needed), link_mode="combined", emit_back=True,
    )

    def sweep(start, faces):
        current, current_faces, _ = run_pass(
            source, link_rows, back_rows, label_rows, colour_list, 0, start, halos_of(start, faces),
            faces=tuple(needed),
        )
        result, _, _ = run_pass(
            source, link_rows, back_rows, label_rows, colour_list, 1, current,
            halos_of(current, current_faces),
        )
        return result

    residue, _, _ = run_pass(
        source, link_rows, back_rows, label_rows, None, None, smoothed, halos_of(smoothed, smoothed_faces),
        residual_only=True,
    )
    residual = residue
    membership = member.reshape(AGG, site_count).T
    member_weights = membership.astype(jnp.bfloat16)
    weighted = residual.reshape(2, 2, 6, site_count)[..., None] * member_weights

    pairs = jnp.einsum("krxqn,sxqnj->rsxkj", vectors, weighted, preferred_element_type=jnp.float32)
    real_part = pairs[0, 0] + pairs[1, 1]
    imag_part = pairs[0, 1] - pairs[1, 0]
    coarse_source = jnp.stack([real_part, imag_part]).reshape(2, CDOF, AGG)
    flat_source = coarse_source.reshape(2, 1, CDOF * AGG)
    operator_blocks = coarse_operator.reshape(9, 2, CDOF, CDOF * AGG)
    inverse_blocks = block_inverse.reshape(2, CDOF, CDOF * AGG)
    correction = run_coarse(flat_source, inverse_blocks, operator_blocks, None, None)
    for repeat in range(2):
        nearby = [
            permute_from(correction, "grp", 1, lambda i: True),
            permute_from(correction, "grp", -1, lambda i: True),
            permute_from(correction, "lat", 1, z_up_ok),
            permute_from(correction, "lat", -1, z_down_ok),
            permute_from(correction, "lat", PZ, t_up_ok),
            permute_from(correction, "lat", -PZ, t_down_ok),
        ]
        correction = run_coarse(flat_source, inverse_blocks, operator_blocks, correction, nearby)
    correction = correction.reshape(2, CDOF, AGG)
    expanded = jnp.dot(
        correction.reshape(2 * CDOF, AGG), membership.T, precision=lax.Precision.HIGHEST
    ).reshape(2, 2, NVEC, site_count)
    spread_real = jnp.swapaxes(expanded[0], 0, 1)[:, :, None]
    spread_imag = jnp.swapaxes(expanded[1], 0, 1)[:, :, None]
    real_part = jnp.sum(vectors[:, 0] * spread_real - vectors[:, 1] * spread_imag, axis=0)
    imag_part = jnp.sum(vectors[:, 0] * spread_imag + vectors[:, 1] * spread_real, axis=0)
    corrected = smoothed + jnp.stack([real_part, imag_part]).reshape(24, rows, line_extent)
    solution = sweep(corrected, faces_of(corrected))
    return (
        solution.reshape(1, 24, time_extent, plane_extent, line_extent),
        correction.reshape(1, 1, 2, CDOF, AGG),
    )


def solution(mesh):
    return jax.shard_map(
        body,
        mesh=mesh,
        in_specs=(
            P("lat", None, None, None, "grp"),
            P("lat", None, None, None, None, "grp"),
            P("lat", None, None, None, None, "grp"),
            P("lat", None, None, "grp", None),
            P("lat", "grp", None),
            P("lat", "grp", None, None, None, None),
            P("lat", "grp", None, None, None),
        ),
        out_specs=(P("lat", None, None, None, "grp"), P("lat", "grp", None, None, None)),
        check_vma=False,
    )
```
